32 devices in a mesh: fsdp: 8 (over y, x, core), rep: 4 (over z).
Axes of the slice: x: 2, y: 2, z: 4, core: 2. Of those that a mesh axis runs over, the one named last changes fastest.
Arguments:
- tokens: bfloat16 [12288, 2048], P(('fsdp', 'rep')), may hold values from -6 to 6
- lengths: int32 [32], replicated, may hold values from 96 to 384, as said below
- placement: int32 [32], replicated, may hold values from 0 to 31, each once
- attention_gain: bfloat16 [2048], P('fsdp'), may hold values from 0.5 to 1.5
- query_weight: bfloat16 [2048, 2048], P('fsdp'), may hold values from -0.125 to 0.125
- key_weight: bfloat16 [2048, 1024], P('fsdp'), may hold values from -0.125 to 0.125
- value_weight: bfloat16 [2048, 1024], P('fsdp'), may hold values from -0.125 to 0.125
- query_gain: bfloat16 [128], replicated, may hold values from 0.5 to 1.5
- key_gain: bfloat16 [128], replicated, may hold values from 0.5 to 1.5
- output_weight: bfloat16 [2048, 2048], P('fsdp'), may hold values from -1 to 1
- feed_gain: bfloat16 [2048], P('fsdp'), may hold values from 0.5 to 1.5
- gate_weight: bfloat16 [2048, 6144], P('fsdp'), may hold values from -0.125 to 0.125
- up_weight: bfloat16 [2048, 6144], P('fsdp'), may hold values from -0.125 to 0.125
- down_weight: bfloat16 [6144, 2048], P('fsdp'), may hold values from -0.078125 to 0.078125
- cotangent: bfloat16 [12288, 2048], P(('fsdp', 'rep')), may hold values from -6 to 6
Outputs:
- layer_out: bfloat16 [12288, 2048], P(('fsdp', 'rep'))
- input_grad: float32 [12288, 2048], P(('fsdp', 'rep'))
- attention_gain_grad: float32 [2048], P('fsdp')
- query_weight_grad: float32 [2048, 2048], P('fsdp')
- key_weight_grad: float32 [2048, 1024], P('fsdp')
- value_weight_grad: float32 [2048, 1024], P('fsdp')
- query_gain_grad: float32 [128], replicated
- key_gain_grad: float32 [128], replicated
- output_weight_grad: float32 [2048, 2048], P('fsdp')
- feed_gain_grad: float32 [2048], P('fsdp')
- gate_weight_grad: float32 [2048, 6144], P('fsdp')
- up_weight_grad: float32 [2048, 6144], P('fsdp')
- down_weight_grad: float32 [6144, 2048], P('fsdp')
The draws below stay inside these ranges and needn't reach their ends.
Inputs may be any that keep to these rules, and one draw needn't show every extreme that they name: lengths[s] is the number of valid leading positions of sequence s; some sequence has exactly 384 and some exactly 96. `placement`: each sequence stands in exactly one slot.
All inputs are finite; a program needn't handle non-finite values.
Results may differ from the reference program's by a relative error of at most 0.018.
Values may be sent and summed in bfloat16 or wider, within the bound.
No kernel may reach another device: no remote copies, remote signals or barrier semaphores. Data moves between devices by JAX's collectives and lax.ppermute only.
A program may use at most 448 MiB of HBM per device.

```python
import jax
import jax.numpy as jnp
from jax import lax

D = 2048
H = 16
KVH = 8
HD = 128
FF = 6144
TOK_DEV = 384
SEQS = 32
TOKENS = 12288


def draw_lengths(key, part):
    base = jax.random.randint(key, (SEQS,), TOK_DEV // 4, TOK_DEV + 1)
    first = jax.random.randint(jax.random.fold_in(key, 1), (), 0, SEQS)
    offset = jax.random.randint(jax.random.fold_in(key, 2), (), 1, SEQS)
    second = (first + offset) % SEQS
    return base.at[first].set(TOK_DEV).at[second].set(TOK_DEV // 4).astype(jnp.int32)


def shard_levels(rng, shape, pieces, low, high):
    loudness, own = 1.0, jax.random.fold_in(rng, 6)
    for dim, blocks in pieces:
        heights = jnp.exp(jax.random.uniform(jax.random.fold_in(own, dim), (blocks,), jnp.float32, low / len(pieces), high / len(pieces)))
        loudness = loudness * jnp.repeat(heights, shape[dim] // blocks).reshape([-1 if axis == dim else 1 for axis in range(len(shape))])
    return loudness


def normal_values(key, dims, scale, reach, cuts=(), dtype=jnp.bfloat16):
    values = scale * jax.random.normal(key, dims, jnp.float32)
    if cuts:
        values = values * shard_levels(key, dims, cuts, -0.22, 0.18)
    return jnp.clip(values, -reach, reach).astype(dtype)


def setup_inputs(seed: int = 0) -> dict:
    arg_keys = jax.random.split(jax.random.key(seed), 16)
    tokens = normal_values(arg_keys[0], (TOKENS, D), 1.0, 6.0, ((0, 32),))
    lengths = draw_lengths(jax.random.fold_in(arg_keys[15], 71), 0)
    placement = jax.random.permutation(arg_keys[2], SEQS).astype(jnp.int32)
    attention_gain = jnp.clip(1.0 + 0.1 * jax.random.normal(arg_keys[3], (D,), jnp.float32), 0.5, 1.5).astype(jnp.bfloat16)
    query_weight = normal_values(arg_keys[4], (D, H * HD), D ** -0.5, 0.125, ((0, 8),))
    key_weight = normal_values(arg_keys[5], (D, KVH * HD), D ** -0.5, 0.125, ((0, 8),))
    value_weight = normal_values(arg_keys[6], (D, KVH * HD), D ** -0.5, 0.125, ((0, 8),))
    query_gain = jnp.clip(1.0 + 0.1 * jax.random.normal(arg_keys[7], (HD,), jnp.float32), 0.5, 1.5).astype(jnp.bfloat16)
    key_gain = jnp.clip(1.0 + 0.1 * jax.random.normal(arg_keys[8], (HD,), jnp.float32), 0.5, 1.5).astype(jnp.bfloat16)
    output_weight = normal_values(arg_keys[9], (H * HD, D), (D // 64) ** -0.5, 1.0, ((0, 8),))
    feed_gain = jnp.clip(1.0 + 0.1 * jax.random.normal(arg_keys[10], (D,), jnp.float32), 0.5, 1.5).astype(jnp.bfloat16)
    gate_weight = normal_values(arg_keys[11], (D, FF), D ** -0.5, 0.125, ((0, 8),))
    up_weight = normal_values(arg_keys[12], (D, FF), D ** -0.5, 0.125, ((0, 8),))
    down_weight = normal_values(arg_keys[13], (FF, D), FF ** -0.5, 0.078125, ((0, 8),))
    cotangent = normal_values(arg_keys[14], (TOKENS, D), 1.0, 6.0, ((0, 32),))
    return dict(tokens=tokens, lengths=lengths, placement=placement, attention_gain=attention_gain, query_weight=query_weight, key_weight=key_weight, value_weight=value_weight, query_gain=query_gain, key_gain=key_gain, output_weight=output_weight, feed_gain=feed_gain, gate_weight=gate_weight, up_weight=up_weight, down_weight=down_weight, cotangent=cotangent)


EPSILON = 1e-06
ROPE_BASE = 1000000.0
HIGHEST = lax.Precision.HIGHEST

@jax.custom_vjp
def low(v):
    return lax.optimization_barrier(v.astype(jnp.bfloat16)).astype(jnp.float32)

@jax.custom_vjp
def low_back(v):
    return v

def low_keep(v):
    return (low(v), None)

def low_pass(kept, grad):
    return (grad,)

def back_keep(v):
    return (v, None)

def back_low(kept, grad):
    return (low(grad),)
low.defvjp(low_keep, low_pass)
low_back.defvjp(back_keep, back_low)

def rms_norm(values, norm_gain):
    return values * lax.rsqrt(lax.optimization_barrier(jnp.mean(values * values, axis=-1, keepdims=True)) + EPSILON) * norm_gain

def turn_half(values):
    half_width = values.shape[-1] // 2
    return jnp.concatenate([-values[..., half_width:], values[..., :half_width]], axis=-1)

def rotate(values, cosine, sine):
    return values * cosine + turn_half(values) * sine

def angle_tables(length, width):
    exponent = jnp.arange(width // 2).astype(jnp.float32) * (2.0 / width)
    frequency = ROPE_BASE ** (-exponent)
    position = jnp.arange(length).astype(jnp.float32)
    phase = position[:, None] * frequency[None, :]
    phase = jnp.concatenate([phase, phase], axis=-1)
    return (jnp.cos(phase), jnp.sin(phase))

def attend(query_low, key_low, value_low):
    length = query_low.shape[0]
    grouped = query_low.reshape(length, KVH, H // KVH, HD)
    scores = jnp.einsum('qkgd,skd->kgqs', grouped, key_low, precision=HIGHEST)
    causal = jnp.arange(length)[:, None] >= jnp.arange(length)[None, :]
    scores = low_back(jnp.where(causal, scores, -1000000000.0))
    row_top = lax.optimization_barrier(jnp.max(scores, axis=-1, keepdims=True))
    exp_scores = jnp.exp(scores - row_top)
    probs_low = low(exp_scores / lax.optimization_barrier(jnp.sum(exp_scores, axis=-1, keepdims=True)))
    mixed = jnp.einsum('kgqs,skd->qkgd', probs_low, value_low, precision=HIGHEST)
    return mixed.reshape(length, H * HD)

def attend_item(items):
    return attend(items[0], items[1], items[2])

def layer(tokens, attention_gain, query_weight, key_weight, value_weight, query_gain, key_gain, output_weight, feed_gain, gate_weight, up_weight, down_weight, valid, cosine, sine):
    token_count = tokens.shape[0]
    normed_one = low(rms_norm(tokens, attention_gain))
    query_raw = low_back(jnp.dot(normed_one, query_weight, precision=HIGHEST)).reshape(token_count, H, HD)
    key_raw = low_back(jnp.dot(normed_one, key_weight, precision=HIGHEST)).reshape(token_count, KVH, HD)
    value_low = low(low_back(jnp.dot(normed_one, value_weight, precision=HIGHEST))).reshape(token_count, KVH, HD)
    query_low = low(rotate(rms_norm(query_raw, query_gain), cosine[:, None, :], sine[:, None, :]) * HD ** (-0.5))
    key_low = low(rotate(rms_norm(key_raw, key_gain), cosine[:, None, :], sine[:, None, :]))
    mixed = lax.map(jax.checkpoint(attend_item), (query_low.reshape(SEQS, TOK_DEV, H, HD), key_low.reshape(SEQS, TOK_DEV, KVH, HD), value_low.reshape(SEQS, TOK_DEV, KVH, HD)))
    mixed_low = low(low_back(mixed.reshape(token_count, H * HD)))
    branch = low_back(jnp.dot(mixed_low, output_weight, precision=HIGHEST))
    middle = tokens + branch
    normed_two = low(rms_norm(middle, feed_gain))
    gate_value = low_back(jnp.dot(normed_two, gate_weight, precision=HIGHEST))
    up_value = low_back(jnp.dot(normed_two, up_weight, precision=HIGHEST))
    hidden = low(jax.nn.silu(gate_value) * up_value)
    down_value = low_back(jnp.dot(hidden, down_weight, precision=HIGHEST))
    return (middle + down_value) * valid

def reference(tokens, lengths, placement, attention_gain, query_weight, key_weight, value_weight, query_gain, key_gain, output_weight, feed_gain, gate_weight, up_weight, down_weight, cotangent):
    slot_length = lengths[placement]
    position = jnp.arange(TOK_DEV).astype(jnp.int32)
    valid = (position[None, :] < slot_length[:, None]).astype(jnp.float32).reshape(SEQS * TOK_DEV, 1)
    cosine, sine = angle_tables(TOK_DEV, HD)
    cosine = jnp.tile(cosine, (SEQS, 1))
    sine = jnp.tile(sine, (SEQS, 1))
    params = (tokens.astype(jnp.float32), attention_gain.astype(jnp.float32), query_weight.astype(jnp.float32), key_weight.astype(jnp.float32), value_weight.astype(jnp.float32), query_gain.astype(jnp.float32), key_gain.astype(jnp.float32), output_weight.astype(jnp.float32), feed_gain.astype(jnp.float32), gate_weight.astype(jnp.float32), up_weight.astype(jnp.float32), down_weight.astype(jnp.float32))

    def forward(*inputs):
        return layer(*inputs, valid, cosine, sine)
    result, pullback = jax.vjp(forward, *params)
    grads = pullback(cotangent.astype(jnp.float32))
    return (result.astype(jnp.bfloat16), grads[0], grads[1], grads[2], grads[3], grads[4], grads[5], grads[6], grads[7], grads[8], grads[9], grads[10], grads[11])
```

```python
import jax
import jax.numpy as jnp
from jax import lax
from jax.sharding import PartitionSpec as P

EPSILON = 1e-06
ROPE_BASE = 1000000.0


def angle_tables(length, width):
    exponent = jnp.arange(width // 2).astype(jnp.float32) * (2.0 / width)
    frequency = ROPE_BASE ** (-exponent)
    position = jnp.arange(length).astype(jnp.float32)
    phase = position[:, None] * frequency[None, :]
    phase = jnp.concatenate([phase, phase], axis=-1)
    return (jnp.cos(phase), jnp.sin(phase))


def turn_half(values):
    half_width = values.shape[-1] // 2
    return jnp.concatenate([-values[..., half_width:], values[..., :half_width]], axis=-1)


def rotate(values, cosine, sine):
    return values * cosine + turn_half(values) * sine


def unrotate(grads_out, cosine, sine):
    return grads_out * cosine - turn_half(grads_out * sine)


def rms_forward(values, norm_gain):
    inverse = lax.rsqrt(jnp.mean(values * values, axis=-1, keepdims=True) + EPSILON)
    normal = values * inverse
    return (normal * norm_gain, normal, inverse)


def rms_backward(grads_out, normal, inverse, norm_gain):
    scaled = grads_out * norm_gain
    grads_in = inverse * (scaled - normal * jnp.mean(scaled * normal, axis=-1, keepdims=True))
    return (grads_in, grads_out * normal)


def inner_rows(left, right):
    return lax.dot_general(
        left, right, (((0,), (0,)), ((), ())), preferred_element_type=jnp.float32
    )


def times_transposed(left, right):
    return lax.dot_general(
        left, right, (((1,), (1,)), ((), ())), preferred_element_type=jnp.float32
    )


def masked_scores(query_low, key_low):
    scores = jnp.einsum("qkgd,skd->kgqs", query_low, key_low, preferred_element_type=jnp.float32)
    length = query_low.shape[0]
    causal = jnp.arange(length)[:, None] >= jnp.arange(length)[None, :]
    return jnp.where(causal, scores, -1000000000.0)


def per_device(
    tokens,
    lengths,
    placement,
    attention_gain,
    query_weight,
    key_weight,
    value_weight,
    query_gain,
    key_gain,
    output_weight,
    feed_gain,
    gate_weight,
    up_weight,
    down_weight,
    cotangent,
):
    row_count = tokens.shape[0]
    head_width = query_gain.shape[0]
    value_heads = key_weight.shape[1] // head_width
    query_heads = query_weight.shape[1] // head_width
    group_size = query_heads // value_heads
    slot_index = lax.axis_index("fsdp") * lax.axis_size("rep") + lax.axis_index("rep")
    slot_length = lengths[placement[slot_index]]
    valid_rows = (jnp.arange(row_count) < slot_length).astype(jnp.float32)[:, None]
    cosine, sine = angle_tables(row_count, head_width)
    cosine = cosine[:, None, :]
    sine = sine[:, None, :]
    scale = head_width ** (-0.5)
    gain_query = query_gain.astype(jnp.float32)
    gain_key = key_gain.astype(jnp.float32)
    attention_set = (
        lax.all_gather(attention_gain, "fsdp", axis=0, tiled=True),
        lax.all_gather(query_weight, "fsdp", axis=0, tiled=True),
        lax.all_gather(key_weight, "fsdp", axis=0, tiled=True),
        lax.all_gather(value_weight, "fsdp", axis=0, tiled=True),
        lax.all_gather(output_weight, "fsdp", axis=0, tiled=True),
    )
    gate_block = lax.all_to_all(gate_weight, "fsdp", 1, 0, tiled=True)
    up_block = lax.all_to_all(up_weight, "fsdp", 1, 0, tiled=True)
    inputs_wide = tokens.astype(jnp.float32)
    gain_one = attention_set[0].astype(jnp.float32)
    normed_one, normal_one, inverse_one = rms_forward(inputs_wide, gain_one)
    normed_one_low = normed_one.astype(jnp.bfloat16)
    query_raw = jnp.dot(
        normed_one_low, attention_set[1], preferred_element_type=jnp.float32
    ).reshape(row_count, query_heads, head_width)
    key_raw = jnp.dot(normed_one_low, attention_set[2], preferred_element_type=jnp.float32).reshape(
        row_count, value_heads, head_width
    )
    value_low = (
        jnp.dot(normed_one_low, attention_set[3], preferred_element_type=jnp.float32)
        .astype(jnp.bfloat16)
        .reshape(row_count, value_heads, head_width)
    )
    query_normed, query_normal, query_inverse = rms_forward(query_raw, gain_query)
    key_normed, key_normal, key_inverse = rms_forward(key_raw, gain_key)
    query_low = (
        (rotate(query_normed, cosine, sine) * scale)
        .astype(jnp.bfloat16)
        .reshape(row_count, value_heads, group_size, head_width)
    )
    key_low = rotate(key_normed, cosine, sine).astype(jnp.bfloat16)
    scores = masked_scores(query_low, key_low)
    row_top = jnp.max(scores, axis=-1, keepdims=True)
    exp_scores = jnp.exp(scores - row_top)
    row_total = jnp.sum(exp_scores, axis=-1, keepdims=True)
    probs_low = (exp_scores / row_total).astype(jnp.bfloat16)
    log_total = row_top + jnp.log(row_total)
    mixed = jnp.einsum("kgqs,skd->qkgd", probs_low, value_low, preferred_element_type=jnp.float32)
    mixed_low = mixed.reshape(row_count, query_heads * head_width).astype(jnp.bfloat16)
    branch = jnp.dot(mixed_low, attention_set[4], preferred_element_type=jnp.float32)
    middle = inputs_wide + branch
    gain_two = lax.all_gather(feed_gain, "fsdp", axis=0, tiled=True).astype(jnp.float32)
    normed_two, normal_two, inverse_two = rms_forward(middle, gain_two)
    normed_two_low = normed_two.astype(jnp.bfloat16)
    normed_two_group = lax.all_gather(normed_two_low, "fsdp", axis=0, tiled=True)
    gate_value = jnp.dot(normed_two_group, gate_block, preferred_element_type=jnp.float32)
    up_value = jnp.dot(normed_two_group, up_block, preferred_element_type=jnp.float32)
    hidden_low = (jax.nn.silu(gate_value) * up_value).astype(jnp.bfloat16)
    down_part = jnp.dot(hidden_low, down_weight, preferred_element_type=jnp.float32)
    down_value = lax.psum_scatter(down_part, "fsdp", scatter_dimension=0, tiled=True)
    layer_out = ((middle + down_value) * valid_rows).astype(jnp.bfloat16)
    grad_top = cotangent.astype(jnp.float32) * valid_rows
    grad_down_low = grad_top.astype(jnp.bfloat16)
    grad_down_group = lax.all_gather(grad_down_low, "fsdp", axis=0, tiled=True)
    down_grad = inner_rows(hidden_low, grad_down_group)
    grad_hidden = times_transposed(grad_down_group, down_weight)
    sigmoid_gate = jax.nn.sigmoid(gate_value)
    grad_gate_low = (
        grad_hidden * up_value * sigmoid_gate * (1.0 + gate_value * (1.0 - sigmoid_gate))
    ).astype(jnp.bfloat16)
    grad_up_low = (grad_hidden * (gate_value * sigmoid_gate)).astype(jnp.bfloat16)
    gate_grad_block = inner_rows(normed_two_group, grad_gate_low)
    up_grad_block = inner_rows(normed_two_group, grad_up_low)
    grad_normed_part = times_transposed(grad_gate_low, gate_block) + times_transposed(
        grad_up_low, up_block
    )
    grad_normed_two = lax.psum_scatter(grad_normed_part, "fsdp", scatter_dimension=0, tiled=True)
    grad_from_two, gain_two_terms = rms_backward(grad_normed_two, normal_two, inverse_two, gain_two)
    feed_gain_grad = jnp.sum(gain_two_terms, axis=0)
    grad_middle = grad_top + grad_from_two
    feed_parts = (
        lax.psum_scatter(
            feed_gain_grad.astype(jnp.bfloat16), "fsdp", scatter_dimension=0, tiled=True
        ).astype(jnp.float32),
        lax.all_to_all(gate_grad_block.astype(jnp.bfloat16), "fsdp", 0, 1, tiled=True).astype(
            jnp.float32
        ),
        lax.all_to_all(up_grad_block.astype(jnp.bfloat16), "fsdp", 0, 1, tiled=True).astype(
            jnp.float32
        ),
        down_grad,
    )
    grad_branch_low = grad_middle.astype(jnp.bfloat16)
    output_grad = inner_rows(mixed_low, grad_branch_low)
    grad_mixed_low = (
        times_transposed(grad_branch_low, attention_set[4])
        .astype(jnp.bfloat16)
        .reshape(row_count, value_heads, group_size, head_width)
    )
    scores_again = masked_scores(query_low, key_low)
    probs_again = jnp.exp(scores_again - log_total)
    probs_again_low = probs_again.astype(jnp.bfloat16)
    grad_probs = jnp.einsum(
        "qkgd,skd->kgqs", grad_mixed_low, value_low, preferred_element_type=jnp.float32
    )
    row_term = jnp.sum(probs_again * grad_probs, axis=-1, keepdims=True)
    grad_scores_low = (probs_again * (grad_probs - row_term)).astype(jnp.bfloat16)
    grad_query_rot = (
        jnp.einsum(
            "kgqs,skd->qkgd", grad_scores_low, key_low, preferred_element_type=jnp.float32
        ).reshape(row_count, query_heads, head_width)
        * scale
    )
    grad_key_rot = jnp.einsum(
        "kgqs,qkgd->skd", grad_scores_low, query_low, preferred_element_type=jnp.float32
    )
    grad_value_low = (
        jnp.einsum(
            "kgqs,qkgd->skd", probs_again_low, grad_mixed_low, preferred_element_type=jnp.float32
        )
        .astype(jnp.bfloat16)
        .reshape(row_count, value_heads * head_width)
    )
    grad_query_raw, query_gain_terms = rms_backward(
        unrotate(grad_query_rot, cosine, sine), query_normal, query_inverse, gain_query
    )
    grad_key_raw, key_gain_terms = rms_backward(
        unrotate(grad_key_rot, cosine, sine), key_normal, key_inverse, gain_key
    )
    query_gain_grad = jnp.sum(query_gain_terms, axis=(0, 1))
    key_gain_grad = jnp.sum(key_gain_terms, axis=(0, 1))
    grad_query_low = grad_query_raw.astype(jnp.bfloat16).reshape(
        row_count, query_heads * head_width
    )
    grad_key_low = grad_key_raw.astype(jnp.bfloat16).reshape(row_count, value_heads * head_width)
    query_grad = inner_rows(normed_one_low, grad_query_low)
    key_grad = inner_rows(normed_one_low, grad_key_low)
    value_grad = inner_rows(normed_one_low, grad_value_low)
    grad_normed_one = (
        times_transposed(grad_query_low, attention_set[1])
        + times_transposed(grad_key_low, attention_set[2])
        + times_transposed(grad_value_low, attention_set[3])
    )
    grad_from_one, gain_one_terms = rms_backward(grad_normed_one, normal_one, inverse_one, gain_one)
    attention_gain_grad = jnp.sum(gain_one_terms, axis=0)
    input_grad = grad_middle + grad_from_one
    head_terms = jnp.concatenate([query_gain_grad, key_gain_grad])
    head_tiles = jnp.broadcast_to(head_terms[None, :], (lax.axis_size("fsdp"), head_terms.shape[0]))
    low_sum = lambda v: lax.psum_scatter(
        v.astype(jnp.bfloat16), "fsdp", scatter_dimension=0, tiled=True
    )
    attention_parts = (
        lax.psum_scatter(attention_gain_grad, "fsdp", scatter_dimension=0, tiled=True),
        low_sum(query_grad),
        low_sum(key_grad),
        low_sum(value_grad),
        low_sum(output_grad),
        lax.psum_scatter(head_tiles, "fsdp", scatter_dimension=0, tiled=True),
    )
    finals = (
        lax.psum(feed_parts[0].astype(jnp.bfloat16), "rep").astype(jnp.float32),
        lax.psum(feed_parts[1].astype(jnp.bfloat16), "rep").astype(jnp.float32),
        lax.psum(feed_parts[2].astype(jnp.bfloat16), "rep").astype(jnp.float32),
        lax.psum(feed_parts[3].astype(jnp.bfloat16), "rep").astype(jnp.float32),
        lax.psum(attention_parts[0].astype(jnp.bfloat16), "rep").astype(jnp.float32),
        lax.psum(attention_parts[1].astype(jnp.bfloat16), "rep").astype(jnp.float32),
        lax.psum(attention_parts[2].astype(jnp.bfloat16), "rep").astype(jnp.float32),
        lax.psum(attention_parts[3].astype(jnp.bfloat16), "rep").astype(jnp.float32),
        lax.psum(attention_parts[4].astype(jnp.bfloat16), "rep").astype(jnp.float32),
        lax.psum(attention_parts[5].astype(jnp.bfloat16), "rep").astype(jnp.float32),
    )
    head_sum = finals[9]
    return (
        layer_out,
        input_grad,
        finals[4],
        finals[5],
        finals[6],
        finals[7],
        head_sum[0, :head_width],
        head_sum[0, head_width:],
        finals[8],
        finals[0],
        finals[1],
        finals[2],
        finals[3],
    )


def solution(mesh):
    return jax.shard_map(
        per_device,
        mesh=mesh,
        in_specs=(
            P(("fsdp", "rep"), None),
            P(),
            P(),
            P("fsdp"),
            P("fsdp", None),
            P("fsdp", None),
            P("fsdp", None),
            P(),
            P(),
            P("fsdp", None),
            P("fsdp"),
            P("fsdp", None),
            P("fsdp", None),
            P("fsdp", None),
            P(("fsdp", "rep"), None),
        ),
        out_specs=(
            P(("fsdp", "rep"), None),
            P(("fsdp", "rep"), None),
            P("fsdp"),
            P("fsdp", None),
            P("fsdp", None),
            P("fsdp", None),
            P(),
            P(),
            P("fsdp", None),
            P("fsdp"),
            P("fsdp", None),
            P("fsdp", None),
            P("fsdp", None),
        ),
        check_vma=False,
    )
```

```python
import jax
import jax.numpy as jnp
from jax import lax
from jax.sharding import PartitionSpec as P

EPSILON = 1e-06
ROPE_BASE = 1000000.0


def angle_tables(length, width):
    exponent = jnp.arange(width // 2).astype(jnp.float32) * (2.0 / width)
    frequency = ROPE_BASE ** (-exponent)
    position = jnp.arange(length).astype(jnp.float32)
    phase = position[:, None] * frequency[None, :]
    phase = jnp.concatenate([phase, phase], axis=-1)
    return (jnp.cos(phase), jnp.sin(phase))


def turn_half(values):
    half_width = values.shape[-1] // 2
    return jnp.concatenate([-values[..., half_width:], values[..., :half_width]], axis=-1)


def rotate(values, cosine, sine):
    return values * cosine + turn_half(values) * sine


def unrotate(grads_out, cosine, sine):
    return grads_out * cosine - turn_half(grads_out * sine)


def rms_forward(values, norm_gain):
    inverse = lax.rsqrt(jnp.mean(values * values, axis=-1, keepdims=True) + EPSILON)
    normal = values * inverse
    return (normal * norm_gain, normal, inverse)


def rms_backward(grads_out, normal, inverse, norm_gain):
    scaled = grads_out * norm_gain
    grads_in = inverse * (scaled - normal * jnp.mean(scaled * normal, axis=-1, keepdims=True))
    return (grads_in, grads_out * normal)


def inner_rows(left, right):
    return lax.dot_general(
        left, right, (((0,), (0,)), ((), ())), preferred_element_type=jnp.float32
    )


def times_transposed(left, right):
    return lax.dot_general(
        left, right, (((1,), (1,)), ((), ())), preferred_element_type=jnp.float32
    )


def masked_scores(query_low, key_low):
    scores = jnp.einsum("qkgd,skd->kgqs", query_low, key_low, preferred_element_type=jnp.float32)
    length = query_low.shape[0]
    causal = jnp.arange(length)[:, None] >= jnp.arange(length)[None, :]
    return jnp.where(causal, scores, -1000000000.0)


def ring_sum(parts, axis):
    n = lax.axis_size(axis)
    me = lax.axis_index(axis)
    forward = [(i, (i + 1) % n) for i in range(n)]
    backward = [(i, (i - 1) % n) for i in range(n)]
    pieces = [p.reshape((2, n, p.shape[0] // (2 * n)) + p.shape[1:]) for p in parts]
    ahead = [q[0] for q in pieces]
    behind = [q[1] for q in pieces]
    take = lambda q, i: lax.dynamic_index_in_dim(q, i % n, axis=0, keepdims=False)
    run_a = [take(q, me) for q in ahead]
    run_b = [take(q, me) for q in behind]
    for step in range(n - 1):
        got_a = lax.ppermute([r.astype(jnp.bfloat16) for r in run_a], axis, forward)
        got_b = lax.ppermute([r.astype(jnp.bfloat16) for r in run_b], axis, backward)
        run_a = [g.astype(jnp.float32) + take(q, me - 1 - step) for g, q in zip(got_a, ahead)]
        run_b = [g.astype(jnp.float32) + take(q, me + 1 + step) for g, q in zip(got_b, behind)]
    own_a = [r.astype(jnp.bfloat16) for r in run_a]
    own_b = [r.astype(jnp.bfloat16) for r in run_b]
    out_a = [
        lax.dynamic_update_index_in_dim(jnp.zeros(q.shape, jnp.bfloat16), o, (me + 1) % n, 0)
        for q, o in zip(ahead, own_a)
    ]
    out_b = [
        lax.dynamic_update_index_in_dim(jnp.zeros(q.shape, jnp.bfloat16), o, (me - 1) % n, 0)
        for q, o in zip(behind, own_b)
    ]
    for step in range(n - 1):
        own_a = lax.ppermute(own_a, axis, forward)
        own_b = lax.ppermute(own_b, axis, backward)
        out_a = [
            lax.dynamic_update_index_in_dim(t, o, (me - step) % n, 0)
            for t, o in zip(out_a, own_a)
        ]
        out_b = [
            lax.dynamic_update_index_in_dim(t, o, (me + step) % n, 0)
            for t, o in zip(out_b, own_b)
        ]
    return [
        jnp.stack([a, b]).reshape(p.shape).astype(jnp.float32)
        for a, b, p in zip(out_a, out_b, parts)
    ]


def per_device(
    tokens,
    lengths,
    placement,
    attention_gain,
    query_weight,
    key_weight,
    value_weight,
    query_gain,
    key_gain,
    output_weight,
    feed_gain,
    gate_weight,
    up_weight,
    down_weight,
    cotangent,
):
    row_count = tokens.shape[0]
    head_width = query_gain.shape[0]
    value_heads = key_weight.shape[1] // head_width
    query_heads = query_weight.shape[1] // head_width
    group_size = query_heads // value_heads
    slot_index = lax.axis_index("fsdp") * lax.axis_size("rep") + lax.axis_index("rep")
    slot_length = lengths[placement[slot_index]]
    valid_rows = (jnp.arange(row_count) < slot_length).astype(jnp.float32)[:, None]
    cosine, sine = angle_tables(row_count, head_width)
    cosine = cosine[:, None, :]
    sine = sine[:, None, :]
    scale = head_width ** (-0.5)
    gain_query = query_gain.astype(jnp.float32)
    gain_key = key_gain.astype(jnp.float32)
    attention_set = (
        lax.all_gather(attention_gain, "fsdp", axis=0, tiled=True),
        lax.all_gather(query_weight, "fsdp", axis=0, tiled=True),
        lax.all_gather(key_weight, "fsdp", axis=0, tiled=True),
        lax.all_gather(value_weight, "fsdp", axis=0, tiled=True),
        lax.all_gather(output_weight, "fsdp", axis=0, tiled=True),
    )
    gate_block = lax.all_to_all(gate_weight, "fsdp", 1, 0, tiled=True)
    up_block = lax.all_to_all(up_weight, "fsdp", 1, 0, tiled=True)
    inputs_wide = tokens.astype(jnp.float32)
    gain_one = attention_set[0].astype(jnp.float32)
    normed_one, normal_one, inverse_one = rms_forward(inputs_wide, gain_one)
    normed_one_low = normed_one.astype(jnp.bfloat16)
    query_raw = jnp.dot(
        normed_one_low, attention_set[1], preferred_element_type=jnp.float32
    ).reshape(row_count, query_heads, head_width)
    key_raw = jnp.dot(normed_one_low, attention_set[2], preferred_element_type=jnp.float32).reshape(
        row_count, value_heads, head_width
    )
    value_low = (
        jnp.dot(normed_one_low, attention_set[3], preferred_element_type=jnp.float32)
        .astype(jnp.bfloat16)
        .reshape(row_count, value_heads, head_width)
    )
    query_normed, query_normal, query_inverse = rms_forward(query_raw, gain_query)
    key_normed, key_normal, key_inverse = rms_forward(key_raw, gain_key)
    query_low = (
        (rotate(query_normed, cosine, sine) * scale)
        .astype(jnp.bfloat16)
        .reshape(row_count, value_heads, group_size, head_width)
    )
    key_low = rotate(key_normed, cosine, sine).astype(jnp.bfloat16)
    scores = masked_scores(query_low, key_low)
    row_top = jnp.max(scores, axis=-1, keepdims=True)
    exp_scores = jnp.exp(scores - row_top)
    row_total = jnp.sum(exp_scores, axis=-1, keepdims=True)
    probs_low = (exp_scores / row_total).astype(jnp.bfloat16)
    log_total = row_top + jnp.log(row_total)
    mixed = jnp.einsum("kgqs,skd->qkgd", probs_low, value_low, preferred_element_type=jnp.float32)
    mixed_low = mixed.reshape(row_count, query_heads * head_width).astype(jnp.bfloat16)
    branch = jnp.dot(mixed_low, attention_set[4], preferred_element_type=jnp.float32)
    middle = inputs_wide + branch
    gain_two = lax.all_gather(feed_gain, "fsdp", axis=0, tiled=True).astype(jnp.float32)
    normed_two, normal_two, inverse_two = rms_forward(middle, gain_two)
    normed_two_low = normed_two.astype(jnp.bfloat16)
    normed_two_group = lax.all_gather(normed_two_low, "fsdp", axis=0, tiled=True)
    gate_value = jnp.dot(normed_two_group, gate_block, preferred_element_type=jnp.float32)
    up_value = jnp.dot(normed_two_group, up_block, preferred_element_type=jnp.float32)
    hidden_low = (jax.nn.silu(gate_value) * up_value).astype(jnp.bfloat16)
    down_part = jnp.dot(hidden_low, down_weight, preferred_element_type=jnp.float32)
    grad_top = cotangent.astype(jnp.float32) * valid_rows
    grad_down_low = grad_top.astype(jnp.bfloat16)
    grad_down_group = lax.all_gather(grad_down_low, "fsdp", axis=0, tiled=True)
    down_grad = inner_rows(hidden_low, grad_down_group)
    grad_hidden = times_transposed(grad_down_group, down_weight)
    sigmoid_gate = jax.nn.sigmoid(gate_value)
    grad_gate_low = (
        grad_hidden * up_value * sigmoid_gate * (1.0 + gate_value * (1.0 - sigmoid_gate))
    ).astype(jnp.bfloat16)
    grad_up_low = (grad_hidden * (gate_value * sigmoid_gate)).astype(jnp.bfloat16)
    gate_grad_block = inner_rows(normed_two_group, grad_gate_low)
    up_grad_block = inner_rows(normed_two_group, grad_up_low)
    grad_normed_part = times_transposed(grad_gate_low, gate_block) + times_transposed(
        grad_up_low, up_block
    )
    grad_normed_two = lax.psum_scatter(grad_normed_part, "fsdp", scatter_dimension=0, tiled=True)
    grad_normed_two, down_part = lax.optimization_barrier((grad_normed_two, down_part))
    down_value = lax.psum_scatter(down_part, "fsdp", scatter_dimension=0, tiled=True)
    layer_out = ((middle + down_value) * valid_rows).astype(jnp.bfloat16)
    grad_from_two, gain_two_terms = rms_backward(grad_normed_two, normal_two, inverse_two, gain_two)
    feed_gain_grad = jnp.sum(gain_two_terms, axis=0)
    grad_middle = grad_top + grad_from_two
    feed_parts = (
        lax.psum_scatter(
            feed_gain_grad.astype(jnp.bfloat16), "fsdp", scatter_dimension=0, tiled=True
        ).astype(jnp.float32),
        lax.all_to_all(gate_grad_block.astype(jnp.bfloat16), "fsdp", 0, 1, tiled=True).astype(
            jnp.float32
        ),
        lax.all_to_all(up_grad_block.astype(jnp.bfloat16), "fsdp", 0, 1, tiled=True).astype(
            jnp.float32
        ),
        down_grad,
    )
    feed_rep = ring_sum(list(feed_parts[1:]), "rep")
    grad_branch_low = grad_middle.astype(jnp.bfloat16)
    output_grad = inner_rows(mixed_low, grad_branch_low)
    grad_mixed_low = (
        times_transposed(grad_branch_low, attention_set[4])
        .astype(jnp.bfloat16)
        .reshape(row_count, value_heads, group_size, head_width)
    )
    scores_again = masked_scores(query_low, key_low)
    probs_again = jnp.exp(scores_again - log_total)
    probs_again_low = probs_again.astype(jnp.bfloat16)
    grad_probs = jnp.einsum(
        "qkgd,skd->kgqs", grad_mixed_low, value_low, preferred_element_type=jnp.float32
    )
    row_term = jnp.sum(probs_again * grad_probs, axis=-1, keepdims=True)
    grad_scores_low = (probs_again * (grad_probs - row_term)).astype(jnp.bfloat16)
    grad_query_rot = (
        jnp.einsum(
            "kgqs,skd->qkgd", grad_scores_low, key_low, preferred_element_type=jnp.float32
        ).reshape(row_count, query_heads, head_width)
        * scale
    )
    grad_key_rot = jnp.einsum(
        "kgqs,qkgd->skd", grad_scores_low, query_low, preferred_element_type=jnp.float32
    )
    grad_value_low = (
        jnp.einsum(
            "kgqs,qkgd->skd", probs_again_low, grad_mixed_low, preferred_element_type=jnp.float32
        )
        .astype(jnp.bfloat16)
        .reshape(row_count, value_heads * head_width)
    )
    grad_query_raw, query_gain_terms = rms_backward(
        unrotate(grad_query_rot, cosine, sine), query_normal, query_inverse, gain_query
    )
    grad_key_raw, key_gain_terms = rms_backward(
        unrotate(grad_key_rot, cosine, sine), key_normal, key_inverse, gain_key
    )
    query_gain_grad = jnp.sum(query_gain_terms, axis=(0, 1))
    key_gain_grad = jnp.sum(key_gain_terms, axis=(0, 1))
    grad_query_low = grad_query_raw.astype(jnp.bfloat16).reshape(
        row_count, query_heads * head_width
    )
    grad_key_low = grad_key_raw.astype(jnp.bfloat16).reshape(row_count, value_heads * head_width)
    query_grad = inner_rows(normed_one_low, grad_query_low)
    key_grad = inner_rows(normed_one_low, grad_key_low)
    value_grad = inner_rows(normed_one_low, grad_value_low)
    grad_normed_one = (
        times_transposed(grad_query_low, attention_set[1])
        + times_transposed(grad_key_low, attention_set[2])
        + times_transposed(grad_value_low, attention_set[3])
    )
    grad_from_one, gain_one_terms = rms_backward(grad_normed_one, normal_one, inverse_one, gain_one)
    attention_gain_grad = jnp.sum(gain_one_terms, axis=0)
    input_grad = grad_middle + grad_from_one
    head_terms = jnp.concatenate([query_gain_grad, key_gain_grad])
    head_tiles = jnp.broadcast_to(head_terms[None, :], (lax.axis_size("fsdp"), head_terms.shape[0]))
    low_sum = lambda v: lax.psum_scatter(
        v.astype(jnp.bfloat16), "fsdp", scatter_dimension=0, tiled=True
    )
    attention_parts = (
        lax.psum_scatter(attention_gain_grad, "fsdp", scatter_dimension=0, tiled=True),
        low_sum(query_grad),
        low_sum(key_grad),
        low_sum(value_grad),
        low_sum(output_grad),
        lax.psum_scatter(head_tiles, "fsdp", scatter_dimension=0, tiled=True),
    )
    finals = (
        lax.psum(feed_parts[0].astype(jnp.bfloat16), "rep").astype(jnp.float32),
        feed_rep[0],
        feed_rep[1],
        feed_rep[2],
        lax.psum(attention_parts[0].astype(jnp.bfloat16), "rep").astype(jnp.float32),
        lax.psum(attention_parts[1].astype(jnp.bfloat16), "rep").astype(jnp.float32),
        lax.psum(attention_parts[2].astype(jnp.bfloat16), "rep").astype(jnp.float32),
        lax.psum(attention_parts[3].astype(jnp.bfloat16), "rep").astype(jnp.float32),
        lax.psum(attention_parts[4].astype(jnp.bfloat16), "rep").astype(jnp.float32),
        lax.psum(attention_parts[5].astype(jnp.bfloat16), "rep").astype(jnp.float32),
    )
    head_sum = finals[9]
    return (
        layer_out,
        input_grad,
        finals[4],
        finals[5],
        finals[6],
        finals[7],
        head_sum[0, :head_width],
        head_sum[0, head_width:],
        finals[8],
        finals[0],
        finals[1],
        finals[2],
        finals[3],
    )


def solution(mesh):
    return jax.shard_map(
        per_device,
        mesh=mesh,
        in_specs=(
            P(("fsdp", "rep"), None),
            P(),
            P(),
            P("fsdp"),
            P("fsdp", None),
            P("fsdp", None),
            P("fsdp", None),
            P(),
            P(),
            P("fsdp", None),
            P("fsdp"),
            P("fsdp", None),
            P("fsdp", None),
            P("fsdp", None),
            P(("fsdp", "rep"), None),
        ),
        out_specs=(
            P(("fsdp", "rep"), None),
            P(("fsdp", "rep"), None),
            P("fsdp"),
            P("fsdp", None),
            P("fsdp", None),
            P("fsdp", None),
            P(),
            P(),
            P("fsdp", None),
            P("fsdp"),
            P("fsdp", None),
            P("fsdp", None),
            P("fsdp", None),
        ),
        check_vma=False,
    )
```

```python
import jax
import jax.numpy as jnp
from jax import lax
from jax.sharding import PartitionSpec as P

EPSILON = 1e-06
ROPE_BASE = 1000000.0


def angle_tables(length, width):
    exponent = jnp.arange(width // 2).astype(jnp.float32) * (2.0 / width)
    frequency = ROPE_BASE ** (-exponent)
    position = jnp.arange(length).astype(jnp.float32)
    phase = position[:, None] * frequency[None, :]
    phase = jnp.concatenate([phase, phase], axis=-1)
    return (jnp.cos(phase), jnp.sin(phase))


def turn_half(values):
    half_width = values.shape[-1] // 2
    return jnp.concatenate([-values[..., half_width:], values[..., :half_width]], axis=-1)


def rotate(values, cosine, sine):
    return values * cosine + turn_half(values) * sine


def unrotate(grads_out, cosine, sine):
    return grads_out * cosine - turn_half(grads_out * sine)


def rms_forward(values, norm_gain):
    inverse = lax.rsqrt(jnp.mean(values * values, axis=-1, keepdims=True) + EPSILON)
    normal = values * inverse
    return (normal * norm_gain, normal, inverse)


def rms_backward(grads_out, normal, inverse, norm_gain):
    scaled = grads_out * norm_gain
    grads_in = inverse * (scaled - normal * jnp.mean(scaled * normal, axis=-1, keepdims=True))
    return (grads_in, grads_out * normal)


def inner_rows(left, right):
    return lax.dot_general(
        left, right, (((0,), (0,)), ((), ())), preferred_element_type=jnp.float32
    )


def times_transposed(left, right):
    return lax.dot_general(
        left, right, (((1,), (1,)), ((), ())), preferred_element_type=jnp.float32
    )


def masked_scores(query_low, key_low):
    scores = jnp.einsum("qkgd,skd->kgqs", query_low, key_low, preferred_element_type=jnp.float32)
    length = query_low.shape[0]
    causal = jnp.arange(length)[:, None] >= jnp.arange(length)[None, :]
    return jnp.where(causal, scores, -1000000000.0)


def ring_sum(parts, axis):
    n = lax.axis_size(axis)
    me = lax.axis_index(axis)
    forward = [(i, (i + 1) % n) for i in range(n)]
    backward = [(i, (i - 1) % n) for i in range(n)]
    pieces = [p.reshape((2, n, p.shape[0] // (2 * n)) + p.shape[1:]) for p in parts]
    ahead = [q[0] for q in pieces]
    behind = [q[1] for q in pieces]
    take = lambda q, i: lax.dynamic_index_in_dim(q, i % n, axis=0, keepdims=False).astype(
        jnp.float32
    )
    run_a = [take(q, me) for q in ahead]
    run_b = [take(q, me) for q in behind]
    for step in range(n - 1):
        got_a = lax.ppermute([r.astype(jnp.bfloat16) for r in run_a], axis, forward)
        got_b = lax.ppermute([r.astype(jnp.bfloat16) for r in run_b], axis, backward)
        run_a = [g.astype(jnp.float32) + take(q, me - 1 - step) for g, q in zip(got_a, ahead)]
        run_b = [g.astype(jnp.float32) + take(q, me + 1 + step) for g, q in zip(got_b, behind)]
    own_a = [r.astype(jnp.bfloat16) for r in run_a]
    own_b = [r.astype(jnp.bfloat16) for r in run_b]
    out_a = [
        lax.dynamic_update_index_in_dim(jnp.zeros(q.shape, jnp.bfloat16), o, (me + 1) % n, 0)
        for q, o in zip(ahead, own_a)
    ]
    out_b = [
        lax.dynamic_update_index_in_dim(jnp.zeros(q.shape, jnp.bfloat16), o, (me - 1) % n, 0)
        for q, o in zip(behind, own_b)
    ]
    for step in range(n - 1):
        own_a = lax.ppermute(own_a, axis, forward)
        own_b = lax.ppermute(own_b, axis, backward)
        out_a = [
            lax.dynamic_update_index_in_dim(t, o, (me - step) % n, 0)
            for t, o in zip(out_a, own_a)
        ]
        out_b = [
            lax.dynamic_update_index_in_dim(t, o, (me + step) % n, 0)
            for t, o in zip(out_b, own_b)
        ]
    return [
        jnp.stack([a, b]).reshape(p.shape).astype(jnp.float32)
        for a, b, p in zip(out_a, out_b, parts)
    ]


def per_device(
    tokens,
    lengths,
    placement,
    attention_gain,
    query_weight,
    key_weight,
    value_weight,
    query_gain,
    key_gain,
    output_weight,
    feed_gain,
    gate_weight,
    up_weight,
    down_weight,
    cotangent,
):
    row_count = tokens.shape[0]
    head_width = query_gain.shape[0]
    value_heads = key_weight.shape[1] // head_width
    query_heads = query_weight.shape[1] // head_width
    group_size = query_heads // value_heads
    slot_index = lax.axis_index("fsdp") * lax.axis_size("rep") + lax.axis_index("rep")
    slot_length = lengths[placement[slot_index]]
    valid_rows = (jnp.arange(row_count) < slot_length).astype(jnp.float32)[:, None]
    cosine, sine = angle_tables(row_count, head_width)
    cosine = cosine[:, None, :]
    sine = sine[:, None, :]
    scale = head_width ** (-0.5)
    gain_query = query_gain.astype(jnp.float32)
    gain_key = key_gain.astype(jnp.float32)
    attention_set = (
        lax.all_gather(attention_gain, "fsdp", axis=0, tiled=True),
        lax.all_gather(query_weight, "fsdp", axis=0, tiled=True),
        lax.all_gather(key_weight, "fsdp", axis=0, tiled=True),
        lax.all_gather(value_weight, "fsdp", axis=0, tiled=True),
        lax.all_gather(output_weight, "fsdp", axis=0, tiled=True),
    )
    gate_block = lax.all_to_all(gate_weight, "fsdp", 1, 0, tiled=True)
    up_block = lax.all_to_all(up_weight, "fsdp", 1, 0, tiled=True)
    tokens, gate_block, up_block = lax.optimization_barrier((tokens, gate_block, up_block))
    inputs_wide = tokens.astype(jnp.float32)
    gain_one = attention_set[0].astype(jnp.float32)
    normed_one, normal_one, inverse_one = rms_forward(inputs_wide, gain_one)
    normed_one_low = normed_one.astype(jnp.bfloat16)
    query_raw = jnp.dot(
        normed_one_low, attention_set[1], preferred_element_type=jnp.float32
    ).reshape(row_count, query_heads, head_width)
    key_raw = jnp.dot(normed_one_low, attention_set[2], preferred_element_type=jnp.float32).reshape(
        row_count, value_heads, head_width
    )
    value_low = (
        jnp.dot(normed_one_low, attention_set[3], preferred_element_type=jnp.float32)
        .astype(jnp.bfloat16)
        .reshape(row_count, value_heads, head_width)
    )
    query_normed, query_normal, query_inverse = rms_forward(query_raw, gain_query)
    key_normed, key_normal, key_inverse = rms_forward(key_raw, gain_key)
    query_low = (
        (rotate(query_normed, cosine, sine) * scale)
        .astype(jnp.bfloat16)
        .reshape(row_count, value_heads, group_size, head_width)
    )
    key_low = rotate(key_normed, cosine, sine).astype(jnp.bfloat16)
    scores = masked_scores(query_low, key_low)
    row_top = jnp.max(scores, axis=-1, keepdims=True)
    exp_scores = jnp.exp(scores - row_top)
    row_total = jnp.sum(exp_scores, axis=-1, keepdims=True)
    probs_low = (exp_scores / row_total).astype(jnp.bfloat16)
    log_total = row_top + jnp.log(row_total)
    mixed = jnp.einsum("kgqs,skd->qkgd", probs_low, value_low, preferred_element_type=jnp.float32)
    mixed_low = mixed.reshape(row_count, query_heads * head_width).astype(jnp.bfloat16)
    branch = jnp.dot(mixed_low, attention_set[4], preferred_element_type=jnp.float32)
    middle = inputs_wide + branch
    gain_two = lax.all_gather(feed_gain, "fsdp", axis=0, tiled=True).astype(jnp.float32)
    normed_two, normal_two, inverse_two = rms_forward(middle, gain_two)
    normed_two_low = normed_two.astype(jnp.bfloat16)
    normed_two_group = lax.all_gather(normed_two_low, "fsdp", axis=0, tiled=True)
    gate_value = jnp.dot(normed_two_group, gate_block, preferred_element_type=jnp.float32)
    up_value = jnp.dot(normed_two_group, up_block, preferred_element_type=jnp.float32)
    hidden_low = (jax.nn.silu(gate_value) * up_value).astype(jnp.bfloat16)
    down_part = jnp.dot(hidden_low, down_weight, preferred_element_type=jnp.float32)
    grad_top = cotangent.astype(jnp.float32) * valid_rows
    grad_down_low = grad_top.astype(jnp.bfloat16)
    grad_down_group = lax.all_gather(grad_down_low, "fsdp", axis=0, tiled=True)
    down_grad = inner_rows(hidden_low, grad_down_group)
    grad_hidden = times_transposed(grad_down_group, down_weight)
    sigmoid_gate = jax.nn.sigmoid(gate_value)
    grad_gate_low = (
        grad_hidden * up_value * sigmoid_gate * (1.0 + gate_value * (1.0 - sigmoid_gate))
    ).astype(jnp.bfloat16)
    grad_up_low = (grad_hidden * (gate_value * sigmoid_gate)).astype(jnp.bfloat16)
    gate_grad_block = inner_rows(normed_two_group, grad_gate_low)
    up_grad_block = inner_rows(normed_two_group, grad_up_low)
    grad_normed_part = times_transposed(grad_gate_low, gate_block) + times_transposed(
        grad_up_low, up_block
    )
    grad_normed_two = lax.psum_scatter(
        grad_normed_part.astype(jnp.bfloat16), "fsdp", scatter_dimension=0, tiled=True
    ).astype(jnp.float32)
    grad_normed_two, down_part = lax.optimization_barrier((grad_normed_two, down_part))
    down_value = lax.psum_scatter(
        down_part.astype(jnp.bfloat16), "fsdp", scatter_dimension=0, tiled=True
    ).astype(jnp.float32)
    layer_out = ((middle + down_value) * valid_rows).astype(jnp.bfloat16)
    grad_from_two, gain_two_terms = rms_backward(grad_normed_two, normal_two, inverse_two, gain_two)
    feed_gain_grad = jnp.sum(gain_two_terms, axis=0)
    grad_middle = grad_top + grad_from_two
    feed_parts = (
        lax.psum_scatter(
            feed_gain_grad.astype(jnp.bfloat16), "fsdp", scatter_dimension=0, tiled=True
        ).astype(jnp.float32),
        lax.all_to_all(gate_grad_block.astype(jnp.bfloat16), "fsdp", 0, 1, tiled=True),
        lax.all_to_all(up_grad_block.astype(jnp.bfloat16), "fsdp", 0, 1, tiled=True),
        down_grad.astype(jnp.bfloat16),
    )
    feed_width = feed_parts[1].shape[1]
    feed_rows = [feed_parts[1].shape[0], feed_parts[2].shape[0]]
    feed_stack = jnp.concatenate(
        [feed_parts[1], feed_parts[2], feed_parts[3].reshape(-1, feed_width)], axis=0
    )
    (feed_sum,) = ring_sum([feed_stack], "rep")
    feed_rep = (
        feed_sum[: feed_rows[0]],
        feed_sum[feed_rows[0] : feed_rows[0] + feed_rows[1]],
        feed_sum[feed_rows[0] + feed_rows[1] :].reshape(feed_parts[3].shape),
    )
    grad_branch_low = grad_middle.astype(jnp.bfloat16)
    output_grad = inner_rows(mixed_low, grad_branch_low)
    grad_mixed_low = (
        times_transposed(grad_branch_low, attention_set[4])
        .astype(jnp.bfloat16)
        .reshape(row_count, value_heads, group_size, head_width)
    )
    scores_again = masked_scores(query_low, key_low)
    probs_again = jnp.exp(scores_again - log_total)
    probs_again_low = probs_again.astype(jnp.bfloat16)
    grad_probs = jnp.einsum(
        "qkgd,skd->kgqs", grad_mixed_low, value_low, preferred_element_type=jnp.float32
    )
    row_term = jnp.sum(probs_again * grad_probs, axis=-1, keepdims=True)
    grad_scores_low = (probs_again * (grad_probs - row_term)).astype(jnp.bfloat16)
    grad_query_rot = (
        jnp.einsum(
            "kgqs,skd->qkgd", grad_scores_low, key_low, preferred_element_type=jnp.float32
        ).reshape(row_count, query_heads, head_width)
        * scale
    )
    grad_key_rot = jnp.einsum(
        "kgqs,qkgd->skd", grad_scores_low, query_low, preferred_element_type=jnp.float32
    )
    grad_value_low = (
        jnp.einsum(
            "kgqs,qkgd->skd", probs_again_low, grad_mixed_low, preferred_element_type=jnp.float32
        )
        .astype(jnp.bfloat16)
        .reshape(row_count, value_heads * head_width)
    )
    grad_query_raw, query_gain_terms = rms_backward(
        unrotate(grad_query_rot, cosine, sine), query_normal, query_inverse, gain_query
    )
    grad_key_raw, key_gain_terms = rms_backward(
        unrotate(grad_key_rot, cosine, sine), key_normal, key_inverse, gain_key
    )
    query_gain_grad = jnp.sum(query_gain_terms, axis=(0, 1))
    key_gain_grad = jnp.sum(key_gain_terms, axis=(0, 1))
    grad_query_low = grad_query_raw.astype(jnp.bfloat16).reshape(
        row_count, query_heads * head_width
    )
    grad_key_low = grad_key_raw.astype(jnp.bfloat16).reshape(row_count, value_heads * head_width)
    query_grad = inner_rows(normed_one_low, grad_query_low)
    key_grad = inner_rows(normed_one_low, grad_key_low)
    value_grad = inner_rows(normed_one_low, grad_value_low)
    grad_normed_one = (
        times_transposed(grad_query_low, attention_set[1])
        + times_transposed(grad_key_low, attention_set[2])
        + times_transposed(grad_value_low, attention_set[3])
    )
    grad_from_one, gain_one_terms = rms_backward(grad_normed_one, normal_one, inverse_one, gain_one)
    attention_gain_grad = jnp.sum(gain_one_terms, axis=0)
    input_grad = grad_middle + grad_from_one
    head_terms = jnp.concatenate([query_gain_grad, key_gain_grad])
    head_tiles = jnp.broadcast_to(head_terms[None, :], (lax.axis_size("fsdp"), head_terms.shape[0]))
    low_sum = lambda v: lax.psum_scatter(
        v.astype(jnp.bfloat16), "fsdp", scatter_dimension=0, tiled=True
    )
    attention_parts = (
        lax.psum_scatter(attention_gain_grad, "fsdp", scatter_dimension=0, tiled=True),
        low_sum(query_grad),
        low_sum(key_grad),
        low_sum(value_grad),
        low_sum(output_grad),
        lax.psum_scatter(head_tiles, "fsdp", scatter_dimension=0, tiled=True),
    )
    finals = (
        lax.psum(feed_parts[0].astype(jnp.bfloat16), "rep").astype(jnp.float32),
        feed_rep[0],
        feed_rep[1],
        feed_rep[2],
        lax.psum(attention_parts[0].astype(jnp.bfloat16), "rep").astype(jnp.float32),
        lax.psum(attention_parts[1].astype(jnp.bfloat16), "rep").astype(jnp.float32),
        lax.psum(attention_parts[2].astype(jnp.bfloat16), "rep").astype(jnp.float32),
        lax.psum(attention_parts[3].astype(jnp.bfloat16), "rep").astype(jnp.float32),
        lax.psum(attention_parts[4].astype(jnp.bfloat16), "rep").astype(jnp.float32),
        lax.psum(attention_parts[5].astype(jnp.bfloat16), "rep").astype(jnp.float32),
    )
    head_sum = finals[9]
    return (
        layer_out,
        input_grad,
        finals[4],
        finals[5],
        finals[6],
        finals[7],
        head_sum[0, :head_width],
        head_sum[0, head_width:],
        finals[8],
        finals[0],
        finals[1],
        finals[2],
        finals[3],
    )


def solution(mesh):
    return jax.shard_map(
        per_device,
        mesh=mesh,
        in_specs=(
            P(("fsdp", "rep"), None),
            P(),
            P(),
            P("fsdp"),
            P("fsdp", None),
            P("fsdp", None),
            P("fsdp", None),
            P(),
            P(),
            P("fsdp", None),
            P("fsdp"),
            P("fsdp", None),
            P("fsdp", None),
            P("fsdp", None),
            P(("fsdp", "rep"), None),
        ),
        out_specs=(
            P(("fsdp", "rep"), None),
            P(("fsdp", "rep"), None),
            P("fsdp"),
            P("fsdp", None),
            P("fsdp", None),
            P("fsdp", None),
            P(),
            P(),
            P("fsdp", None),
            P("fsdp"),
            P("fsdp", None),
            P("fsdp", None),
            P("fsdp", None),
        ),
        check_vma=False,
    )
```

```python
import jax
import jax.numpy as jnp
from jax import lax
from jax.sharding import PartitionSpec as P


EPSILON = 1e-06
ROPE_BASE = 1000000.0


def angle_tables(length, width):
    exponent = jnp.arange(width // 2).astype(jnp.float32) * (2.0 / width)
    frequency = ROPE_BASE ** (-exponent)
    position = jnp.arange(length).astype(jnp.float32)
    phase = position[:, None] * frequency[None, :]
    phase = jnp.concatenate([phase, phase], axis=-1)
    return (jnp.cos(phase), jnp.sin(phase))


def turn_half(values):
    half_width = values.shape[-1] // 2
    return jnp.concatenate([-values[..., half_width:], values[..., :half_width]], axis=-1)


def rotate(values, cosine, sine):
    return values * cosine + turn_half(values) * sine


def unrotate(grads_out, cosine, sine):
    return grads_out * cosine - turn_half(grads_out * sine)


def rms_forward(values, norm_gain):
    inverse = lax.rsqrt(jnp.mean(values * values, axis=-1, keepdims=True) + EPSILON)
    normal = values * inverse
    return (normal * norm_gain, normal, inverse)


def rms_backward(grads_out, normal, inverse, norm_gain):
    scaled = grads_out * norm_gain
    grads_in = inverse * (scaled - normal * jnp.mean(scaled * normal, axis=-1, keepdims=True))
    return (grads_in, grads_out * normal)


def inner_rows(left, right):
    return lax.dot_general(
        left, right, (((0,), (0,)), ((), ())), preferred_element_type=jnp.float32
    )


def times_transposed(left, right):
    return lax.dot_general(
        left, right, (((1,), (1,)), ((), ())), preferred_element_type=jnp.float32
    )


def masked_scores(query_low, key_low):
    scores = jnp.einsum("qkgd,skd->kgqs", query_low, key_low, preferred_element_type=jnp.float32)
    length = query_low.shape[0]
    causal = jnp.arange(length)[:, None] >= jnp.arange(length)[None, :]
    return jnp.where(causal, scores, -1000000000.0)


class RepRing:
    def __init__(self, part, axis):
        n = lax.axis_size(axis)
        self.n, self.axis, self.shape = n, axis, part.shape
        self.me = lax.axis_index(axis)
        self.forward = [(i, (i + 1) % n) for i in range(n)]
        self.backward = [(i, (i - 1) % n) for i in range(n)]
        pieces = part.reshape((2, n, part.shape[0] // (2 * n)) + part.shape[1:])
        self.ahead, self.behind = pieces[0], pieces[1]
        self.run_a = self.take(self.ahead, self.me)
        self.run_b = self.take(self.behind, self.me)
        self.step = 0
        self.steps = 2 * (n - 1)

    def take(self, q, i):
        return lax.dynamic_index_in_dim(q, i % self.n, axis=0, keepdims=False).astype(
            jnp.float32
        )

    def issue(self):
        if self.step >= self.steps:
            return
        if self.step < self.n - 1:
            sends = (self.run_a.astype(jnp.bfloat16), self.run_b.astype(jnp.bfloat16))
        else:
            sends = (self.own_a, self.own_b)
        self.pending = (
            lax.ppermute(sends[0], self.axis, self.forward),
            lax.ppermute(sends[1], self.axis, self.backward),
        )

    def land(self, carry):
        if self.step >= self.steps:
            return carry
        (got_a, got_b), carry = lax.optimization_barrier((self.pending, carry))
        n, me, s = self.n, self.me, self.step
        if s < n - 1:
            self.run_a = got_a.astype(jnp.float32) + self.take(self.ahead, me - 1 - s)
            self.run_b = got_b.astype(jnp.float32) + self.take(self.behind, me + 1 + s)
            if s == n - 2:
                self.own_a = self.run_a.astype(jnp.bfloat16)
                self.own_b = self.run_b.astype(jnp.bfloat16)
                zeros = jnp.zeros(self.ahead.shape, jnp.bfloat16)
                self.out_a = lax.dynamic_update_index_in_dim(zeros, self.own_a, (me + 1) % n, 0)
                self.out_b = lax.dynamic_update_index_in_dim(zeros, self.own_b, (me - 1) % n, 0)
        else:
            t = s - (n - 1)
            self.own_a, self.own_b = got_a, got_b
            self.out_a = lax.dynamic_update_index_in_dim(self.out_a, got_a, (me - t) % n, 0)
            self.out_b = lax.dynamic_update_index_in_dim(self.out_b, got_b, (me + t) % n, 0)
        self.step += 1
        return carry

    def result(self):
        while self.step < self.steps:
            self.issue()
            self.land(())
        return jnp.stack([self.out_a, self.out_b]).reshape(self.shape).astype(jnp.float32)


def per_device(
    tokens,
    lengths,
    placement,
    attention_gain,
    query_weight,
    key_weight,
    value_weight,
    query_gain,
    key_gain,
    output_weight,
    feed_gain,
    gate_weight,
    up_weight,
    down_weight,
    cotangent,
):
    row_count = tokens.shape[0]
    head_width = query_gain.shape[0]
    value_heads = key_weight.shape[1] // head_width
    query_heads = query_weight.shape[1] // head_width
    group_size = query_heads // value_heads
    slot_index = lax.axis_index("fsdp") * lax.axis_size("rep") + lax.axis_index("rep")
    slot_length = lengths[placement[slot_index]]
    valid_rows = (jnp.arange(row_count) < slot_length).astype(jnp.float32)[:, None]
    cosine, sine = angle_tables(row_count, head_width)
    cosine = cosine[:, None, :]
    sine = sine[:, None, :]
    scale = head_width ** (-0.5)
    gain_query = query_gain.astype(jnp.float32)
    gain_key = key_gain.astype(jnp.float32)
    attention_set = (
        lax.all_gather(attention_gain, "fsdp", axis=0, tiled=True),
        lax.all_gather(query_weight, "fsdp", axis=0, tiled=True),
        lax.all_gather(key_weight, "fsdp", axis=0, tiled=True),
        lax.all_gather(value_weight, "fsdp", axis=0, tiled=True),
        lax.all_gather(output_weight, "fsdp", axis=0, tiled=True),
    )
    gate_block = lax.all_to_all(gate_weight, "fsdp", 1, 0, tiled=True)
    up_block = lax.all_to_all(up_weight, "fsdp", 1, 0, tiled=True)
    tokens, gate_block, up_block = lax.optimization_barrier((tokens, gate_block, up_block))
    inputs_wide = tokens.astype(jnp.float32)
    gain_one = attention_set[0].astype(jnp.float32)
    normed_one, normal_one, inverse_one = rms_forward(inputs_wide, gain_one)
    normed_one_low = normed_one.astype(jnp.bfloat16)
    query_raw = jnp.dot(
        normed_one_low, attention_set[1], preferred_element_type=jnp.float32
    ).reshape(row_count, query_heads, head_width)
    key_raw = jnp.dot(normed_one_low, attention_set[2], preferred_element_type=jnp.float32).reshape(
        row_count, value_heads, head_width
    )
    value_low = (
        jnp.dot(normed_one_low, attention_set[3], preferred_element_type=jnp.float32)
        .astype(jnp.bfloat16)
        .reshape(row_count, value_heads, head_width)
    )
    query_normed, query_normal, query_inverse = rms_forward(query_raw, gain_query)
    key_normed, key_normal, key_inverse = rms_forward(key_raw, gain_key)
    query_low = (
        (rotate(query_normed, cosine, sine) * scale)
        .astype(jnp.bfloat16)
        .reshape(row_count, value_heads, group_size, head_width)
    )
    key_low = rotate(key_normed, cosine, sine).astype(jnp.bfloat16)
    scores = masked_scores(query_low, key_low)
    row_top = jnp.max(scores, axis=-1, keepdims=True)
    exp_scores = jnp.exp(scores - row_top)
    row_total = jnp.sum(exp_scores, axis=-1, keepdims=True)
    probs_low = (exp_scores / row_total).astype(jnp.bfloat16)
    log_total = row_top + jnp.log(row_total)
    mixed = jnp.einsum("kgqs,skd->qkgd", probs_low, value_low, preferred_element_type=jnp.float32)
    mixed_low = mixed.reshape(row_count, query_heads * head_width).astype(jnp.bfloat16)
    branch = jnp.dot(mixed_low, attention_set[4], preferred_element_type=jnp.float32)
    middle = inputs_wide + branch
    gain_two = lax.all_gather(feed_gain, "fsdp", axis=0, tiled=True).astype(jnp.float32)
    normed_two, normal_two, inverse_two = rms_forward(middle, gain_two)
    normed_two_low = normed_two.astype(jnp.bfloat16)
    normed_two_group = lax.all_gather(normed_two_low, "fsdp", axis=0, tiled=True)
    gate_value = jnp.dot(normed_two_group, gate_block, preferred_element_type=jnp.float32)
    up_value = jnp.dot(normed_two_group, up_block, preferred_element_type=jnp.float32)
    hidden_low = (jax.nn.silu(gate_value) * up_value).astype(jnp.bfloat16)
    down_part = jnp.dot(hidden_low, down_weight, preferred_element_type=jnp.float32)
    grad_top = cotangent.astype(jnp.float32) * valid_rows
    grad_down_low = grad_top.astype(jnp.bfloat16)
    grad_down_group = lax.all_gather(grad_down_low, "fsdp", axis=0, tiled=True)
    down_grad = inner_rows(hidden_low, grad_down_group)
    grad_hidden = times_transposed(grad_down_group, down_weight)
    sigmoid_gate = jax.nn.sigmoid(gate_value)
    grad_gate_low = (
        grad_hidden * up_value * sigmoid_gate * (1.0 + gate_value * (1.0 - sigmoid_gate))
    ).astype(jnp.bfloat16)
    grad_up_low = (grad_hidden * (gate_value * sigmoid_gate)).astype(jnp.bfloat16)
    gate_grad_block = inner_rows(normed_two_group, grad_gate_low)
    up_grad_block = inner_rows(normed_two_group, grad_up_low)
    grad_normed_part = times_transposed(grad_gate_low, gate_block) + times_transposed(
        grad_up_low, up_block
    )
    grad_normed_two = lax.psum_scatter(
        grad_normed_part.astype(jnp.bfloat16), "fsdp", scatter_dimension=0, tiled=True
    ).astype(jnp.float32)
    grad_normed_two, down_part = lax.optimization_barrier((grad_normed_two, down_part))
    down_value = lax.psum_scatter(
        down_part.astype(jnp.bfloat16), "fsdp", scatter_dimension=0, tiled=True
    ).astype(jnp.float32)
    grad_from_two, gain_two_terms = rms_backward(grad_normed_two, normal_two, inverse_two, gain_two)
    feed_gain_grad = jnp.sum(gain_two_terms, axis=0)
    grad_middle = grad_top + grad_from_two
    feed_parts = (
        lax.psum_scatter(
            feed_gain_grad.astype(jnp.bfloat16), "fsdp", scatter_dimension=0, tiled=True
        ).astype(jnp.float32),
        lax.all_to_all(gate_grad_block.astype(jnp.bfloat16), "fsdp", 0, 1, tiled=True),
        lax.all_to_all(up_grad_block.astype(jnp.bfloat16), "fsdp", 0, 1, tiled=True),
        down_grad.astype(jnp.bfloat16),
    )
    feed_width = feed_parts[1].shape[1]
    feed_rows = [feed_parts[1].shape[0], feed_parts[2].shape[0]]
    feed_stack = jnp.concatenate(
        [feed_parts[1], feed_parts[2], feed_parts[3].reshape(-1, feed_width)], axis=0
    )
    ring = RepRing(feed_stack, "rep")
    ring.issue()
    grad_branch_low = grad_middle.astype(jnp.bfloat16)
    output_grad = inner_rows(mixed_low, grad_branch_low)
    grad_mixed_low = (
        times_transposed(grad_branch_low, attention_set[4])
        .astype(jnp.bfloat16)
        .reshape(row_count, value_heads, group_size, head_width)
    )
    grad_mixed_low, output_grad = ring.land((grad_mixed_low, output_grad))
    ring.issue()
    scores_again = masked_scores(query_low, key_low)
    probs_again = jnp.exp(scores_again - log_total)
    probs_again_low = probs_again.astype(jnp.bfloat16)
    grad_probs = jnp.einsum(
        "qkgd,skd->kgqs", grad_mixed_low, value_low, preferred_element_type=jnp.float32
    )
    row_term = jnp.sum(probs_again * grad_probs, axis=-1, keepdims=True)
    grad_scores_low = (probs_again * (grad_probs - row_term)).astype(jnp.bfloat16)
    grad_scores_low, probs_again_low = ring.land((grad_scores_low, probs_again_low))
    ring.issue()
    grad_query_rot = (
        jnp.einsum(
            "kgqs,skd->qkgd", grad_scores_low, key_low, preferred_element_type=jnp.float32
        ).reshape(row_count, query_heads, head_width)
        * scale
    )
    grad_key_rot = jnp.einsum(
        "kgqs,qkgd->skd", grad_scores_low, query_low, preferred_element_type=jnp.float32
    )
    grad_value_low = (
        jnp.einsum(
            "kgqs,qkgd->skd", probs_again_low, grad_mixed_low, preferred_element_type=jnp.float32
        )
        .astype(jnp.bfloat16)
        .reshape(row_count, value_heads * head_width)
    )
    grad_query_rot, grad_key_rot, grad_value_low = ring.land(
        (grad_query_rot, grad_key_rot, grad_value_low)
    )
    ring.issue()
    grad_query_raw, query_gain_terms = rms_backward(
        unrotate(grad_query_rot, cosine, sine), query_normal, query_inverse, gain_query
    )
    grad_key_raw, key_gain_terms = rms_backward(
        unrotate(grad_key_rot, cosine, sine), key_normal, key_inverse, gain_key
    )
    query_gain_grad = jnp.sum(query_gain_terms, axis=(0, 1))
    key_gain_grad = jnp.sum(key_gain_terms, axis=(0, 1))
    grad_query_low = grad_query_raw.astype(jnp.bfloat16).reshape(
        row_count, query_heads * head_width
    )
    grad_key_low = grad_key_raw.astype(jnp.bfloat16).reshape(row_count, value_heads * head_width)
    value_grad = inner_rows(normed_one_low, grad_value_low)
    grad_query_low, grad_key_low = ring.land((grad_query_low, grad_key_low))
    ring.issue()
    query_grad = inner_rows(normed_one_low, grad_query_low)
    key_grad = inner_rows(normed_one_low, grad_key_low)
    grad_normed_one = times_transposed(grad_query_low, attention_set[1])
    grad_normed_one, down_value = ring.land((grad_normed_one, down_value))
    ring.issue()
    layer_out = ((middle + down_value) * valid_rows).astype(jnp.bfloat16)
    grad_normed_one = (
        grad_normed_one
        + times_transposed(grad_key_low, attention_set[2])
        + times_transposed(grad_value_low, attention_set[3])
    )
    grad_from_one, gain_one_terms = rms_backward(grad_normed_one, normal_one, inverse_one, gain_one)
    attention_gain_grad = jnp.sum(gain_one_terms, axis=0)
    input_grad = grad_middle + grad_from_one
    input_grad = ring.land(input_grad)
    feed_sum = ring.result()
    feed_rep = (
        feed_sum[: feed_rows[0]],
        feed_sum[feed_rows[0] : feed_rows[0] + feed_rows[1]],
        feed_sum[feed_rows[0] + feed_rows[1] :].reshape(feed_parts[3].shape),
    )
    head_terms = jnp.concatenate([query_gain_grad, key_gain_grad])
    head_tiles = jnp.broadcast_to(head_terms[None, :], (lax.axis_size("fsdp"), head_terms.shape[0]))
    low_sum = lambda v: lax.psum_scatter(
        v.astype(jnp.bfloat16), "fsdp", scatter_dimension=0, tiled=True
    )
    attention_parts = (
        lax.psum_scatter(attention_gain_grad, "fsdp", scatter_dimension=0, tiled=True),
        low_sum(query_grad),
        low_sum(key_grad),
        low_sum(value_grad),
        low_sum(output_grad),
        lax.psum_scatter(head_tiles, "fsdp", scatter_dimension=0, tiled=True),
    )
    finals = (
        lax.psum(feed_parts[0].astype(jnp.bfloat16), "rep").astype(jnp.float32),
        feed_rep[0],
        feed_rep[1],
        feed_rep[2],
        lax.psum(attention_parts[0].astype(jnp.bfloat16), "rep").astype(jnp.float32),
        lax.psum(attention_parts[1].astype(jnp.bfloat16), "rep").astype(jnp.float32),
        lax.psum(attention_parts[2].astype(jnp.bfloat16), "rep").astype(jnp.float32),
        lax.psum(attention_parts[3].astype(jnp.bfloat16), "rep").astype(jnp.float32),
        lax.psum(attention_parts[4].astype(jnp.bfloat16), "rep").astype(jnp.float32),
        lax.psum(attention_parts[5].astype(jnp.bfloat16), "rep").astype(jnp.float32),
    )
    head_sum = finals[9]
    return (
        layer_out,
        input_grad,
        finals[4],
        finals[5],
        finals[6],
        finals[7],
        head_sum[0, :head_width],
        head_sum[0, head_width:],
        finals[8],
        finals[0],
        finals[1],
        finals[2],
        finals[3],
    )


def solution(mesh):
    return jax.shard_map(
        per_device,
        mesh=mesh,
        in_specs=(
            P(("fsdp", "rep"), None),
            P(),
            P(),
            P("fsdp"),
            P("fsdp", None),
            P("fsdp", None),
            P("fsdp", None),
            P(),
            P(),
            P("fsdp", None),
            P("fsdp"),
            P("fsdp", None),
            P("fsdp", None),
            P("fsdp", None),
            P(("fsdp", "rep"), None),
        ),
        out_specs=(
            P(("fsdp", "rep"), None),
            P(("fsdp", "rep"), None),
            P("fsdp"),
            P("fsdp", None),
            P("fsdp", None),
            P("fsdp", None),
            P(),
            P(),
            P("fsdp", None),
            P("fsdp"),
            P("fsdp", None),
            P("fsdp", None),
            P("fsdp", None),
        ),
        check_vma=False,
    )
```

```python
import jax
import jax.numpy as jnp
from jax import lax
from jax.sharding import PartitionSpec as P


EPSILON = 1e-06
ROPE_BASE = 1000000.0


def angle_tables(length, width):
    exponent = jnp.arange(width // 2).astype(jnp.float32) * (2.0 / width)
    frequency = ROPE_BASE ** (-exponent)
    position = jnp.arange(length).astype(jnp.float32)
    phase = position[:, None] * frequency[None, :]
    phase = jnp.concatenate([phase, phase], axis=-1)
    return (jnp.cos(phase), jnp.sin(phase))


def turn_half(values):
    half_width = values.shape[-1] // 2
    return jnp.concatenate([-values[..., half_width:], values[..., :half_width]], axis=-1)


def rotate(values, cosine, sine):
    return values * cosine + turn_half(values) * sine


def unrotate(grads_out, cosine, sine):
    return grads_out * cosine - turn_half(grads_out * sine)


def rms_forward(values, norm_gain):
    inverse = lax.rsqrt(jnp.mean(values * values, axis=-1, keepdims=True) + EPSILON)
    normal = values * inverse
    return (normal * norm_gain, normal, inverse)


def rms_backward(grads_out, normal, inverse, norm_gain):
    scaled = grads_out * norm_gain
    grads_in = inverse * (scaled - normal * jnp.mean(scaled * normal, axis=-1, keepdims=True))
    return (grads_in, grads_out * normal)


def inner_rows(left, right):
    return lax.dot_general(
        left, right, (((0,), (0,)), ((), ())), preferred_element_type=jnp.float32
    )


def times_transposed(left, right):
    return lax.dot_general(
        left, right, (((1,), (1,)), ((), ())), preferred_element_type=jnp.float32
    )


def masked_scores(query_low, key_low):
    scores = jnp.einsum("qkgd,skd->kgqs", query_low, key_low, preferred_element_type=jnp.float32)
    length = query_low.shape[0]
    causal = jnp.arange(length)[:, None] >= jnp.arange(length)[None, :]
    return jnp.where(causal, scores, -1000000000.0)


class RepRing:
    def __init__(self, part, axis):
        n = lax.axis_size(axis)
        self.n, self.axis, self.shape = n, axis, part.shape
        self.me = lax.axis_index(axis)
        self.forward = [(i, (i + 1) % n) for i in range(n)]
        self.backward = [(i, (i - 1) % n) for i in range(n)]
        pieces = part.reshape((2, n, part.shape[0] // (2 * n)) + part.shape[1:])
        self.ahead, self.behind = pieces[0], pieces[1]
        self.run_a = self.take(self.ahead, self.me)
        self.run_b = self.take(self.behind, self.me)
        self.step = 0
        self.steps = 2 * (n - 1)

    def take(self, q, i):
        return lax.dynamic_index_in_dim(q, i % self.n, axis=0, keepdims=False).astype(
            jnp.float32
        )

    def issue(self):
        if self.step >= self.steps:
            return
        if self.step < self.n - 1:
            sends = (self.run_a.astype(jnp.bfloat16), self.run_b.astype(jnp.bfloat16))
        else:
            sends = (self.own_a, self.own_b)
        self.pending = (
            lax.ppermute(sends[0], self.axis, self.forward),
            lax.ppermute(sends[1], self.axis, self.backward),
        )

    def land(self, carry):
        if self.step >= self.steps:
            return carry
        (got_a, got_b), carry = lax.optimization_barrier((self.pending, carry))
        n, me, s = self.n, self.me, self.step
        if s < n - 1:
            self.run_a = got_a.astype(jnp.float32) + self.take(self.ahead, me - 1 - s)
            self.run_b = got_b.astype(jnp.float32) + self.take(self.behind, me + 1 + s)
            if s == n - 2:
                self.own_a = self.run_a.astype(jnp.bfloat16)
                self.own_b = self.run_b.astype(jnp.bfloat16)
                zeros = jnp.zeros(self.ahead.shape, jnp.bfloat16)
                self.out_a = lax.dynamic_update_index_in_dim(zeros, self.own_a, (me + 1) % n, 0)
                self.out_b = lax.dynamic_update_index_in_dim(zeros, self.own_b, (me - 1) % n, 0)
        else:
            t = s - (n - 1)
            self.own_a, self.own_b = got_a, got_b
            self.out_a = lax.dynamic_update_index_in_dim(self.out_a, got_a, (me - t) % n, 0)
            self.out_b = lax.dynamic_update_index_in_dim(self.out_b, got_b, (me + t) % n, 0)
        self.step += 1
        return carry

    def result(self):
        while self.step < self.steps:
            self.issue()
            self.land(())
        return jnp.stack([self.out_a, self.out_b]).reshape(self.shape).astype(jnp.float32)


def per_device(
    tokens,
    lengths,
    placement,
    attention_gain,
    query_weight,
    key_weight,
    value_weight,
    query_gain,
    key_gain,
    output_weight,
    feed_gain,
    gate_weight,
    up_weight,
    down_weight,
    cotangent,
):
    row_count = tokens.shape[0]
    head_width = query_gain.shape[0]
    value_heads = key_weight.shape[1] // head_width
    query_heads = query_weight.shape[1] // head_width
    group_size = query_heads // value_heads
    slot_index = lax.axis_index("fsdp") * lax.axis_size("rep") + lax.axis_index("rep")
    slot_length = lengths[placement[slot_index]]
    valid_rows = (jnp.arange(row_count) < slot_length).astype(jnp.float32)[:, None]
    cosine, sine = angle_tables(row_count, head_width)
    cosine = cosine[:, None, :]
    sine = sine[:, None, :]
    scale = head_width ** (-0.5)
    gain_query = query_gain.astype(jnp.float32)
    gain_key = key_gain.astype(jnp.float32)
    attention_set = (
        lax.all_gather(attention_gain, "fsdp", axis=0, tiled=True),
        lax.all_gather(query_weight, "fsdp", axis=0, tiled=True),
        lax.all_gather(key_weight, "fsdp", axis=0, tiled=True),
        lax.all_gather(value_weight, "fsdp", axis=0, tiled=True),
        lax.all_gather(output_weight, "fsdp", axis=0, tiled=True),
    )
    gate_block = lax.all_to_all(gate_weight, "fsdp", 1, 0, tiled=True)
    up_block = lax.all_to_all(up_weight, "fsdp", 1, 0, tiled=True)
    tokens, gate_block, up_block = lax.optimization_barrier((tokens, gate_block, up_block))
    inputs_wide = tokens.astype(jnp.float32)
    gain_one = attention_set[0].astype(jnp.float32)
    normed_one, normal_one, inverse_one = rms_forward(inputs_wide, gain_one)
    normed_one_low = normed_one.astype(jnp.bfloat16)
    query_raw = jnp.dot(
        normed_one_low, attention_set[1], preferred_element_type=jnp.float32
    ).reshape(row_count, query_heads, head_width)
    key_raw = jnp.dot(normed_one_low, attention_set[2], preferred_element_type=jnp.float32).reshape(
        row_count, value_heads, head_width
    )
    value_low = (
        jnp.dot(normed_one_low, attention_set[3], preferred_element_type=jnp.float32)
        .astype(jnp.bfloat16)
        .reshape(row_count, value_heads, head_width)
    )
    query_normed, query_normal, query_inverse = rms_forward(query_raw, gain_query)
    key_normed, key_normal, key_inverse = rms_forward(key_raw, gain_key)
    query_low = (
        (rotate(query_normed, cosine, sine) * scale)
        .astype(jnp.bfloat16)
        .reshape(row_count, value_heads, group_size, head_width)
    )
    key_low = rotate(key_normed, cosine, sine).astype(jnp.bfloat16)
    scores = masked_scores(query_low, key_low)
    row_top = jnp.max(scores, axis=-1, keepdims=True)
    exp_scores = jnp.exp(scores - row_top)
    row_total = jnp.sum(exp_scores, axis=-1, keepdims=True)
    probs_low = (exp_scores / row_total).astype(jnp.bfloat16)
    log_total = row_top + jnp.log(row_total)
    mixed = jnp.einsum("kgqs,skd->qkgd", probs_low, value_low, preferred_element_type=jnp.float32)
    mixed_low = mixed.reshape(row_count, query_heads * head_width).astype(jnp.bfloat16)
    branch = jnp.dot(mixed_low, attention_set[4], preferred_element_type=jnp.float32)
    middle = inputs_wide + branch
    gain_two = lax.all_gather(feed_gain, "fsdp", axis=0, tiled=True).astype(jnp.float32)
    normed_two, normal_two, inverse_two = rms_forward(middle, gain_two)
    normed_two_low = normed_two.astype(jnp.bfloat16)
    normed_two_group = lax.all_gather(normed_two_low, "fsdp", axis=0, tiled=True)
    gate_value = jnp.dot(normed_two_group, gate_block, preferred_element_type=jnp.float32)
    up_value = jnp.dot(normed_two_group, up_block, preferred_element_type=jnp.float32)
    hidden_low = (jax.nn.silu(gate_value) * up_value).astype(jnp.bfloat16)
    down_part = jnp.dot(hidden_low, down_weight, preferred_element_type=jnp.float32)
    grad_top = cotangent.astype(jnp.float32) * valid_rows
    grad_down_low = grad_top.astype(jnp.bfloat16)
    grad_down_group = lax.all_gather(grad_down_low, "fsdp", axis=0, tiled=True)
    down_grad = inner_rows(hidden_low, grad_down_group)
    grad_hidden = times_transposed(grad_down_group, down_weight)
    sigmoid_gate = jax.nn.sigmoid(gate_value)
    grad_gate_low = (
        grad_hidden * up_value * sigmoid_gate * (1.0 + gate_value * (1.0 - sigmoid_gate))
    ).astype(jnp.bfloat16)
    grad_up_low = (grad_hidden * (gate_value * sigmoid_gate)).astype(jnp.bfloat16)
    gate_grad_block = inner_rows(normed_two_group, grad_gate_low)
    up_grad_block = inner_rows(normed_two_group, grad_up_low)
    grad_normed_part = times_transposed(grad_gate_low, gate_block) + times_transposed(
        grad_up_low, up_block
    )
    grad_normed_two = lax.psum_scatter(
        grad_normed_part.astype(jnp.bfloat16), "fsdp", scatter_dimension=0, tiled=True
    ).astype(jnp.float32)
    grad_normed_two, down_part = lax.optimization_barrier((grad_normed_two, down_part))
    down_value = lax.psum_scatter(
        down_part.astype(jnp.bfloat16), "fsdp", scatter_dimension=0, tiled=True
    ).astype(jnp.float32)
    grad_from_two, gain_two_terms = rms_backward(grad_normed_two, normal_two, inverse_two, gain_two)
    feed_gain_grad = jnp.sum(gain_two_terms, axis=0)
    grad_middle = grad_top + grad_from_two
    feed_parts = (
        lax.psum_scatter(
            feed_gain_grad.astype(jnp.bfloat16), "fsdp", scatter_dimension=0, tiled=True
        ).astype(jnp.float32),
        lax.all_to_all(gate_grad_block.astype(jnp.bfloat16), "fsdp", 0, 1, tiled=True),
        lax.all_to_all(up_grad_block.astype(jnp.bfloat16), "fsdp", 0, 1, tiled=True),
        down_grad.astype(jnp.bfloat16),
    )
    feed_width = feed_parts[1].shape[1]
    feed_rows = [feed_parts[1].shape[0], feed_parts[2].shape[0]]
    feed_stack = jnp.concatenate(
        [feed_parts[1], feed_parts[2], feed_parts[3].reshape(-1, feed_width)], axis=0
    )
    ring = RepRing(feed_stack, "rep")
    ring.issue()
    grad_branch_low = grad_middle.astype(jnp.bfloat16)
    output_grad = inner_rows(mixed_low, grad_branch_low)
    grad_mixed_low = (
        times_transposed(grad_branch_low, attention_set[4])
        .astype(jnp.bfloat16)
        .reshape(row_count, value_heads, group_size, head_width)
    )
    grad_mixed_low, output_grad = ring.land((grad_mixed_low, output_grad))
    ring.issue()
    scores_again = masked_scores(query_low, key_low)
    probs_again = jnp.exp(scores_again - log_total)
    probs_again_low = probs_again.astype(jnp.bfloat16)
    grad_probs = jnp.einsum(
        "qkgd,skd->kgqs", grad_mixed_low, value_low, preferred_element_type=jnp.float32
    )
    row_term = jnp.sum(probs_again * grad_probs, axis=-1, keepdims=True)
    grad_scores_low = (probs_again * (grad_probs - row_term)).astype(jnp.bfloat16)
    grad_scores_low, probs_again_low = ring.land((grad_scores_low, probs_again_low))
    ring.issue()
    grad_query_rot = (
        jnp.einsum(
            "kgqs,skd->qkgd", grad_scores_low, key_low, preferred_element_type=jnp.float32
        ).reshape(row_count, query_heads, head_width)
        * scale
    )
    grad_key_rot = jnp.einsum(
        "kgqs,qkgd->skd", grad_scores_low, query_low, preferred_element_type=jnp.float32
    )
    grad_value_low = (
        jnp.einsum(
            "kgqs,qkgd->skd", probs_again_low, grad_mixed_low, preferred_element_type=jnp.float32
        )
        .astype(jnp.bfloat16)
        .reshape(row_count, value_heads * head_width)
    )
    grad_query_rot, grad_key_rot, grad_value_low = ring.land(
        (grad_query_rot, grad_key_rot, grad_value_low)
    )
    ring.issue()
    grad_query_raw, query_gain_terms = rms_backward(
        unrotate(grad_query_rot, cosine, sine), query_normal, query_inverse, gain_query
    )
    grad_key_raw, key_gain_terms = rms_backward(
        unrotate(grad_key_rot, cosine, sine), key_normal, key_inverse, gain_key
    )
    query_gain_grad = jnp.sum(query_gain_terms, axis=(0, 1))
    key_gain_grad = jnp.sum(key_gain_terms, axis=(0, 1))
    grad_query_low = grad_query_raw.astype(jnp.bfloat16).reshape(
        row_count, query_heads * head_width
    )
    grad_key_low = grad_key_raw.astype(jnp.bfloat16).reshape(row_count, value_heads * head_width)
    value_grad = inner_rows(normed_one_low, grad_value_low)
    grad_query_low, grad_key_low = ring.land((grad_query_low, grad_key_low))
    ring.issue()
    query_grad = inner_rows(normed_one_low, grad_query_low)
    key_grad = inner_rows(normed_one_low, grad_key_low)
    grad_normed_one = times_transposed(grad_query_low, attention_set[1])
    grad_normed_one, down_value = ring.land((grad_normed_one, down_value))
    ring.issue()
    layer_out = ((middle + down_value) * valid_rows).astype(jnp.bfloat16)
    grad_normed_one = (
        grad_normed_one
        + times_transposed(grad_key_low, attention_set[2])
        + times_transposed(grad_value_low, attention_set[3])
    )
    grad_from_one, gain_one_terms = rms_backward(grad_normed_one, normal_one, inverse_one, gain_one)
    attention_gain_grad = jnp.sum(gain_one_terms, axis=0)
    input_grad = grad_middle + grad_from_one
    input_grad = ring.land(input_grad)
    feed_sum = ring.result()
    feed_rep = (
        feed_sum[: feed_rows[0]],
        feed_sum[feed_rows[0] : feed_rows[0] + feed_rows[1]],
        feed_sum[feed_rows[0] + feed_rows[1] :].reshape(feed_parts[3].shape),
    )
    head_terms = jnp.concatenate([query_gain_grad, key_gain_grad])
    head_tiles = jnp.broadcast_to(head_terms[None, :], (lax.axis_size("fsdp"), head_terms.shape[0]))

    def low_sum(v):
        return lax.psum_scatter(v.astype(jnp.bfloat16), "fsdp", scatter_dimension=0, tiled=True)

    attention_parts = (
        lax.psum_scatter(attention_gain_grad, "fsdp", scatter_dimension=0, tiled=True),
        low_sum(query_grad),
        low_sum(key_grad),
        low_sum(value_grad),
        low_sum(output_grad),
        lax.psum_scatter(head_tiles, "fsdp", scatter_dimension=0, tiled=True),
    )
    finals = (
        lax.psum(feed_parts[0].astype(jnp.bfloat16), "rep").astype(jnp.float32),
        feed_rep[0],
        feed_rep[1],
        feed_rep[2],
        lax.psum(attention_parts[0].astype(jnp.bfloat16), "rep").astype(jnp.float32),
        lax.psum(attention_parts[1].astype(jnp.bfloat16), "rep").astype(jnp.float32),
        lax.psum(attention_parts[2].astype(jnp.bfloat16), "rep").astype(jnp.float32),
        lax.psum(attention_parts[3].astype(jnp.bfloat16), "rep").astype(jnp.float32),
        lax.psum(attention_parts[4].astype(jnp.bfloat16), "rep").astype(jnp.float32),
        lax.psum(attention_parts[5].astype(jnp.bfloat16), "rep").astype(jnp.float32),
    )
    head_sum = finals[9]
    return (
        layer_out,
        input_grad,
        finals[4],
        finals[5],
        finals[6],
        finals[7],
        head_sum[0, :head_width],
        head_sum[0, head_width:],
        finals[8],
        finals[0],
        finals[1],
        finals[2],
        finals[3],
    )


def solution(mesh):
    return jax.shard_map(
        per_device,
        mesh=mesh,
        in_specs=(
            P(("fsdp", "rep"), None),
            P(),
            P(),
            P("fsdp"),
            P("fsdp", None),
            P("fsdp", None),
            P("fsdp", None),
            P(),
            P(),
            P("fsdp", None),
            P("fsdp"),
            P("fsdp", None),
            P("fsdp", None),
            P("fsdp", None),
            P(("fsdp", "rep"), None),
        ),
        out_specs=(
            P(("fsdp", "rep"), None),
            P(("fsdp", "rep"), None),
            P("fsdp"),
            P("fsdp", None),
            P("fsdp", None),
            P("fsdp", None),
            P(),
            P(),
            P("fsdp", None),
            P("fsdp"),
            P("fsdp", None),
            P("fsdp", None),
            P("fsdp", None),
        ),
        check_vma=False,
    )
```

```python
import jax
import jax.numpy as jnp
from jax import lax
from jax.sharding import PartitionSpec as P


EPSILON = 1e-06
ROPE_BASE = 1000000.0


def angle_tables(length, width):
    exponent = jnp.arange(width // 2).astype(jnp.float32) * (2.0 / width)
    frequency = ROPE_BASE ** (-exponent)
    position = jnp.arange(length).astype(jnp.float32)
    phase = position[:, None] * frequency[None, :]
    phase = jnp.concatenate([phase, phase], axis=-1)
    return (jnp.cos(phase), jnp.sin(phase))


def turn_half(values):
    half_width = values.shape[-1] // 2
    return jnp.concatenate([-values[..., half_width:], values[..., :half_width]], axis=-1)


def rotate(values, cosine, sine):
    return values * cosine + turn_half(values) * sine


def unrotate(grads_out, cosine, sine):
    return grads_out * cosine - turn_half(grads_out * sine)


def rms_forward(values, norm_gain):
    inverse = lax.rsqrt(jnp.mean(values * values, axis=-1, keepdims=True) + EPSILON)
    normal = values * inverse
    return (normal * norm_gain, normal, inverse)


def rms_backward(grads_out, normal, inverse, norm_gain):
    scaled = grads_out * norm_gain
    grads_in = inverse * (scaled - normal * jnp.mean(scaled * normal, axis=-1, keepdims=True))
    return (grads_in, grads_out * normal)


def inner_rows(left, right):
    return lax.dot_general(
        left, right, (((0,), (0,)), ((), ())), preferred_element_type=jnp.float32
    )


def times_transposed(left, right):
    return lax.dot_general(
        left, right, (((1,), (1,)), ((), ())), preferred_element_type=jnp.float32
    )


def masked_scores(query_low, key_low):
    scores = jnp.einsum("qkgd,skd->kgqs", query_low, key_low, preferred_element_type=jnp.float32)
    length = query_low.shape[0]
    causal = jnp.arange(length)[:, None] >= jnp.arange(length)[None, :]
    return jnp.where(causal, scores, -1000000000.0)


class RepRing:
    def __init__(self, part, axis):
        n = lax.axis_size(axis)
        self.n, self.axis, self.shape = n, axis, part.shape
        self.me = lax.axis_index(axis)
        self.forward = [(i, (i + 1) % n) for i in range(n)]
        self.backward = [(i, (i - 1) % n) for i in range(n)]
        pieces = part.reshape((2, n, part.shape[0] // (2 * n)) + part.shape[1:])
        self.ahead, self.behind = pieces[0], pieces[1]
        self.run_a = self.take(self.ahead, self.me)
        self.run_b = self.take(self.behind, self.me)
        self.step = 0
        self.steps = 2 * (n - 1)

    def take(self, q, i):
        return lax.dynamic_index_in_dim(q, i % self.n, axis=0, keepdims=False).astype(
            jnp.float32
        )

    def issue(self):
        if self.step >= self.steps:
            return
        if self.step < self.n - 1:
            sends = (self.run_a.astype(jnp.bfloat16), self.run_b.astype(jnp.bfloat16))
        else:
            sends = (self.own_a, self.own_b)
        self.pending = (
            lax.ppermute(sends[0], self.axis, self.forward),
            lax.ppermute(sends[1], self.axis, self.backward),
        )

    def land(self, carry):
        if self.step >= self.steps:
            return carry
        (got_a, got_b), carry = lax.optimization_barrier((self.pending, carry))
        n, me, s = self.n, self.me, self.step
        if s < n - 1:
            self.run_a = got_a.astype(jnp.float32) + self.take(self.ahead, me - 1 - s)
            self.run_b = got_b.astype(jnp.float32) + self.take(self.behind, me + 1 + s)
            if s == n - 2:
                self.own_a = self.run_a.astype(jnp.bfloat16)
                self.own_b = self.run_b.astype(jnp.bfloat16)
                zeros = jnp.zeros(self.ahead.shape, jnp.bfloat16)
                self.out_a = lax.dynamic_update_index_in_dim(zeros, self.own_a, (me + 1) % n, 0)
                self.out_b = lax.dynamic_update_index_in_dim(zeros, self.own_b, (me - 1) % n, 0)
        else:
            t = s - (n - 1)
            self.own_a, self.own_b = got_a, got_b
            self.out_a = lax.dynamic_update_index_in_dim(self.out_a, got_a, (me - t) % n, 0)
            self.out_b = lax.dynamic_update_index_in_dim(self.out_b, got_b, (me + t) % n, 0)
        self.step += 1
        return carry

    def result(self):
        while self.step < self.steps:
            self.issue()
            self.land(())
        return jnp.stack([self.out_a, self.out_b]).reshape(self.shape).astype(jnp.float32)


def per_device(
    tokens,
    lengths,
    placement,
    attention_gain,
    query_weight,
    key_weight,
    value_weight,
    query_gain,
    key_gain,
    output_weight,
    feed_gain,
    gate_weight,
    up_weight,
    down_weight,
    cotangent,
):
    row_count = tokens.shape[0]
    head_width = query_gain.shape[0]
    value_heads = key_weight.shape[1] // head_width
    query_heads = query_weight.shape[1] // head_width
    group_size = query_heads // value_heads
    slot_index = lax.axis_index("fsdp") * lax.axis_size("rep") + lax.axis_index("rep")
    slot_length = lengths[placement[slot_index]]
    valid_rows = (jnp.arange(row_count) < slot_length).astype(jnp.float32)[:, None]
    cosine, sine = angle_tables(row_count, head_width)
    cosine = cosine[:, None, :]
    sine = sine[:, None, :]
    scale = head_width ** (-0.5)
    gain_query = query_gain.astype(jnp.float32)
    gain_key = key_gain.astype(jnp.float32)
    gains = lax.all_gather(jnp.stack([attention_gain, feed_gain]), "fsdp", axis=1, tiled=True)
    attention_set = (
        gains[0],
        lax.all_gather(query_weight, "fsdp", axis=0, tiled=True),
        lax.all_gather(key_weight, "fsdp", axis=0, tiled=True),
        lax.all_gather(value_weight, "fsdp", axis=0, tiled=True),
        lax.all_gather(output_weight, "fsdp", axis=0, tiled=True),
    )
    gate_block = lax.all_to_all(gate_weight, "fsdp", 1, 0, tiled=True)
    up_block = lax.all_to_all(up_weight, "fsdp", 1, 0, tiled=True)
    tokens, gate_block, up_block = lax.optimization_barrier((tokens, gate_block, up_block))
    inputs_wide = tokens.astype(jnp.float32)
    gain_one = attention_set[0].astype(jnp.float32)
    normed_one, normal_one, inverse_one = rms_forward(inputs_wide, gain_one)
    normed_one_low = normed_one.astype(jnp.bfloat16)
    query_raw = jnp.dot(
        normed_one_low, attention_set[1], preferred_element_type=jnp.float32
    ).reshape(row_count, query_heads, head_width)
    key_raw = jnp.dot(normed_one_low, attention_set[2], preferred_element_type=jnp.float32).reshape(
        row_count, value_heads, head_width
    )
    value_low = (
        jnp.dot(normed_one_low, attention_set[3], preferred_element_type=jnp.float32)
        .astype(jnp.bfloat16)
        .reshape(row_count, value_heads, head_width)
    )
    query_normed, query_normal, query_inverse = rms_forward(query_raw, gain_query)
    key_normed, key_normal, key_inverse = rms_forward(key_raw, gain_key)
    query_low = (
        (rotate(query_normed, cosine, sine) * scale)
        .astype(jnp.bfloat16)
        .reshape(row_count, value_heads, group_size, head_width)
    )
    key_low = rotate(key_normed, cosine, sine).astype(jnp.bfloat16)
    scores = masked_scores(query_low, key_low)
    row_top = jnp.max(scores, axis=-1, keepdims=True)
    exp_scores = jnp.exp(scores - row_top)
    row_total = jnp.sum(exp_scores, axis=-1, keepdims=True)
    probs_low = (exp_scores / row_total).astype(jnp.bfloat16)
    log_total = row_top + jnp.log(row_total)
    mixed = jnp.einsum("kgqs,skd->qkgd", probs_low, value_low, preferred_element_type=jnp.float32)
    mixed_low = mixed.reshape(row_count, query_heads * head_width).astype(jnp.bfloat16)
    branch = jnp.dot(mixed_low, attention_set[4], preferred_element_type=jnp.float32)
    middle = inputs_wide + branch
    gain_two = gains[1].astype(jnp.float32)
    normed_two, normal_two, inverse_two = rms_forward(middle, gain_two)
    normed_two_low = normed_two.astype(jnp.bfloat16)
    normed_two_group = lax.all_gather(normed_two_low, "fsdp", axis=0, tiled=True)
    gate_value = jnp.dot(normed_two_group, gate_block, preferred_element_type=jnp.float32)
    up_value = jnp.dot(normed_two_group, up_block, preferred_element_type=jnp.float32)
    hidden_low = (jax.nn.silu(gate_value) * up_value).astype(jnp.bfloat16)
    down_part = jnp.dot(hidden_low, down_weight, preferred_element_type=jnp.float32)
    grad_top = cotangent.astype(jnp.float32) * valid_rows
    grad_down_low = grad_top.astype(jnp.bfloat16)
    grad_down_group = lax.all_gather(grad_down_low, "fsdp", axis=0, tiled=True)
    down_grad = inner_rows(hidden_low, grad_down_group)
    grad_hidden = times_transposed(grad_down_group, down_weight)
    sigmoid_gate = jax.nn.sigmoid(gate_value)
    grad_gate_low = (
        grad_hidden * up_value * sigmoid_gate * (1.0 + gate_value * (1.0 - sigmoid_gate))
    ).astype(jnp.bfloat16)
    grad_up_low = (grad_hidden * (gate_value * sigmoid_gate)).astype(jnp.bfloat16)
    grad_normed_part = times_transposed(grad_gate_low, gate_block) + times_transposed(
        grad_up_low, up_block
    )
    grad_normed_two = lax.psum_scatter(
        grad_normed_part.astype(jnp.bfloat16), "fsdp", scatter_dimension=0, tiled=True
    ).astype(jnp.float32)
    gate_grad_block = inner_rows(normed_two_group, grad_gate_low)
    up_grad_block = inner_rows(normed_two_group, grad_up_low)
    grad_normed_two, down_part = lax.optimization_barrier((grad_normed_two, down_part))
    down_value = lax.psum_scatter(
        down_part.astype(jnp.bfloat16), "fsdp", scatter_dimension=0, tiled=True
    ).astype(jnp.float32)
    grad_from_two, gain_two_terms = rms_backward(grad_normed_two, normal_two, inverse_two, gain_two)
    feed_gain_grad = jnp.sum(gain_two_terms, axis=0)
    grad_middle = grad_top + grad_from_two
    feed_parts = (
        None,
        lax.all_to_all(gate_grad_block.astype(jnp.bfloat16), "fsdp", 0, 1, tiled=True),
        lax.all_to_all(up_grad_block.astype(jnp.bfloat16), "fsdp", 0, 1, tiled=True),
        down_grad.astype(jnp.bfloat16),
    )
    feed_width = feed_parts[1].shape[1]
    feed_rows = [feed_parts[1].shape[0], feed_parts[2].shape[0]]
    feed_stack = jnp.concatenate(
        [feed_parts[1], feed_parts[2], feed_parts[3].reshape(-1, feed_width)], axis=0
    )
    ring = RepRing(feed_stack, "rep")
    ring.issue()
    grad_branch_low = grad_middle.astype(jnp.bfloat16)
    output_grad = inner_rows(mixed_low, grad_branch_low)
    grad_mixed_low = (
        times_transposed(grad_branch_low, attention_set[4])
        .astype(jnp.bfloat16)
        .reshape(row_count, value_heads, group_size, head_width)
    )
    grad_mixed_low, output_grad = ring.land((grad_mixed_low, output_grad))
    ring.issue()
    scores_again = masked_scores(query_low, key_low)
    probs_again = jnp.exp(scores_again - log_total)
    probs_again_low = probs_again.astype(jnp.bfloat16)
    grad_probs = jnp.einsum(
        "qkgd,skd->kgqs", grad_mixed_low, value_low, preferred_element_type=jnp.float32
    )
    row_term = jnp.sum(probs_again * grad_probs, axis=-1, keepdims=True)
    grad_scores_low = (probs_again * (grad_probs - row_term)).astype(jnp.bfloat16)
    grad_scores_low, probs_again_low = ring.land((grad_scores_low, probs_again_low))
    ring.issue()
    grad_query_rot = (
        jnp.einsum(
            "kgqs,skd->qkgd", grad_scores_low, key_low, preferred_element_type=jnp.float32
        ).reshape(row_count, query_heads, head_width)
        * scale
    )
    grad_key_rot = jnp.einsum(
        "kgqs,qkgd->skd", grad_scores_low, query_low, preferred_element_type=jnp.float32
    )
    grad_value_low = (
        jnp.einsum(
            "kgqs,qkgd->skd", probs_again_low, grad_mixed_low, preferred_element_type=jnp.float32
        )
        .astype(jnp.bfloat16)
        .reshape(row_count, value_heads * head_width)
    )
    grad_query_rot, grad_key_rot, grad_value_low = ring.land(
        (grad_query_rot, grad_key_rot, grad_value_low)
    )
    ring.issue()
    grad_query_raw, query_gain_terms = rms_backward(
        unrotate(grad_query_rot, cosine, sine), query_normal, query_inverse, gain_query
    )
    grad_key_raw, key_gain_terms = rms_backward(
        unrotate(grad_key_rot, cosine, sine), key_normal, key_inverse, gain_key
    )
    query_gain_grad = jnp.sum(query_gain_terms, axis=(0, 1))
    key_gain_grad = jnp.sum(key_gain_terms, axis=(0, 1))
    grad_query_low = grad_query_raw.astype(jnp.bfloat16).reshape(
        row_count, query_heads * head_width
    )
    grad_key_low = grad_key_raw.astype(jnp.bfloat16).reshape(row_count, value_heads * head_width)
    value_grad = inner_rows(normed_one_low, grad_value_low)
    grad_query_low, grad_key_low = ring.land((grad_query_low, grad_key_low))
    ring.issue()
    query_grad = inner_rows(normed_one_low, grad_query_low)
    key_grad = inner_rows(normed_one_low, grad_key_low)
    grad_normed_one = times_transposed(grad_query_low, attention_set[1])
    grad_normed_one, down_value = ring.land((grad_normed_one, down_value))
    ring.issue()
    layer_out = ((middle + down_value) * valid_rows).astype(jnp.bfloat16)
    grad_normed_one = (
        grad_normed_one
        + times_transposed(grad_key_low, attention_set[2])
        + times_transposed(grad_value_low, attention_set[3])
    )
    grad_from_one, gain_one_terms = rms_backward(grad_normed_one, normal_one, inverse_one, gain_one)
    attention_gain_grad = jnp.sum(gain_one_terms, axis=0)
    input_grad = grad_middle + grad_from_one
    input_grad = ring.land(input_grad)
    feed_sum = ring.result()
    feed_rep = (
        feed_sum[: feed_rows[0]],
        feed_sum[feed_rows[0] : feed_rows[0] + feed_rows[1]],
        feed_sum[feed_rows[0] + feed_rows[1] :].reshape(feed_parts[3].shape),
    )
    model_width = attention_gain_grad.shape[0]
    gain_share = model_width // lax.axis_size("fsdp")
    gain_sums = lax.psum(
        jnp.concatenate([attention_gain_grad, feed_gain_grad, query_gain_grad, key_gain_grad]),
        ("fsdp", "rep"),
    )
    gain_start = lax.axis_index("fsdp") * gain_share
    attention_gain_out = lax.dynamic_slice_in_dim(gain_sums, gain_start, gain_share)
    feed_gain_out = lax.dynamic_slice_in_dim(gain_sums, model_width + gain_start, gain_share)
    query_gain_out = gain_sums[2 * model_width : 2 * model_width + head_width]
    key_gain_out = gain_sums[2 * model_width + head_width :]

    def low_sum(v):
        return lax.psum_scatter(v.astype(jnp.bfloat16), "fsdp", scatter_dimension=0, tiled=True)

    attention_parts = (
        None, low_sum(query_grad), low_sum(key_grad), low_sum(value_grad), low_sum(output_grad)
    )
    finals = (
        feed_gain_out,
        feed_rep[0],
        feed_rep[1],
        feed_rep[2],
        attention_gain_out,
        lax.psum(attention_parts[1].astype(jnp.bfloat16), "rep").astype(jnp.float32),
        lax.psum(attention_parts[2].astype(jnp.bfloat16), "rep").astype(jnp.float32),
        lax.psum(attention_parts[3].astype(jnp.bfloat16), "rep").astype(jnp.float32),
        lax.psum(attention_parts[4].astype(jnp.bfloat16), "rep").astype(jnp.float32),
    )
    return (
        layer_out,
        input_grad,
        finals[4],
        finals[5],
        finals[6],
        finals[7],
        query_gain_out,
        key_gain_out,
        finals[8],
        finals[0],
        finals[1],
        finals[2],
        finals[3],
    )


def solution(mesh):
    return jax.shard_map(
        per_device,
        mesh=mesh,
        in_specs=(
            P(("fsdp", "rep"), None),
            P(),
            P(),
            P("fsdp"),
            P("fsdp", None),
            P("fsdp", None),
            P("fsdp", None),
            P(),
            P(),
            P("fsdp", None),
            P("fsdp"),
            P("fsdp", None),
            P("fsdp", None),
            P("fsdp", None),
            P(("fsdp", "rep"), None),
        ),
        out_specs=(
            P(("fsdp", "rep"), None),
            P(("fsdp", "rep"), None),
            P("fsdp"),
            P("fsdp", None),
            P("fsdp", None),
            P("fsdp", None),
            P(),
            P(),
            P("fsdp", None),
            P("fsdp"),
            P("fsdp", None),
            P("fsdp", None),
            P("fsdp", None),
        ),
        check_vma=False,
    )
```

```python
import jax
import jax.numpy as jnp
from jax import lax
from jax.sharding import PartitionSpec as P


EPSILON = 1e-06
ROPE_BASE = 1000000.0


def angle_tables(length, width):
    exponent = jnp.arange(width // 2).astype(jnp.float32) * (2.0 / width)
    frequency = ROPE_BASE ** (-exponent)
    position = jnp.arange(length).astype(jnp.float32)
    phase = position[:, None] * frequency[None, :]
    phase = jnp.concatenate([phase, phase], axis=-1)
    return (jnp.cos(phase), jnp.sin(phase))


def turn_half(values):
    half_width = values.shape[-1] // 2
    return jnp.concatenate([-values[..., half_width:], values[..., :half_width]], axis=-1)


def rotate(values, cosine, sine):
    return values * cosine + turn_half(values) * sine


def unrotate(grads_out, cosine, sine):
    return grads_out * cosine - turn_half(grads_out * sine)


def rms_forward(values, norm_gain):
    inverse = lax.rsqrt(jnp.mean(values * values, axis=-1, keepdims=True) + EPSILON)
    normal = values * inverse
    return (normal * norm_gain, normal, inverse)


def rms_backward(grads_out, normal, inverse, norm_gain):
    scaled = grads_out * norm_gain
    grads_in = inverse * (scaled - normal * jnp.mean(scaled * normal, axis=-1, keepdims=True))
    return (grads_in, grads_out * normal)


def inner_rows(left, right):
    return lax.dot_general(
        left, right, (((0,), (0,)), ((), ())), preferred_element_type=jnp.float32
    )


def times_transposed(left, right):
    return lax.dot_general(
        left, right, (((1,), (1,)), ((), ())), preferred_element_type=jnp.float32
    )


def masked_scores(query_low, key_low):
    scores = jnp.einsum("qkgd,skd->kgqs", query_low, key_low, preferred_element_type=jnp.float32)
    length = query_low.shape[0]
    causal = jnp.arange(length)[:, None] >= jnp.arange(length)[None, :]
    return jnp.where(causal, scores, -1000000000.0)


class RepRing:
    def __init__(self, part, axis):
        n = lax.axis_size(axis)
        self.n, self.axis, self.shape = n, axis, part.shape
        self.me = lax.axis_index(axis)
        self.forward = [(i, (i + 1) % n) for i in range(n)]
        self.backward = [(i, (i - 1) % n) for i in range(n)]
        pieces = part.reshape((2, n, part.shape[0] // (2 * n)) + part.shape[1:])
        self.ahead, self.behind = pieces[0], pieces[1]
        self.run_a = self.take(self.ahead, self.me)
        self.run_b = self.take(self.behind, self.me)
        self.step = 0
        self.steps = 2 * (n - 1)

    def take(self, q, i):
        return lax.dynamic_index_in_dim(q, i % self.n, axis=0, keepdims=False).astype(
            jnp.float32
        )

    def issue(self):
        if self.step >= self.steps:
            return
        if self.step < self.n - 1:
            sends = (self.run_a.astype(jnp.bfloat16), self.run_b.astype(jnp.bfloat16))
        else:
            sends = (self.own_a, self.own_b)
        self.pending = (
            lax.ppermute(sends[0], self.axis, self.forward),
            lax.ppermute(sends[1], self.axis, self.backward),
        )

    def land(self, carry):
        if self.step >= self.steps:
            return carry
        (got_a, got_b), carry = lax.optimization_barrier((self.pending, carry))
        n, me, s = self.n, self.me, self.step
        if s < n - 1:
            self.run_a = got_a.astype(jnp.float32) + self.take(self.ahead, me - 1 - s)
            self.run_b = got_b.astype(jnp.float32) + self.take(self.behind, me + 1 + s)
            if s == n - 2:
                self.own_a = self.run_a.astype(jnp.bfloat16)
                self.own_b = self.run_b.astype(jnp.bfloat16)
                zeros = jnp.zeros(self.ahead.shape, jnp.bfloat16)
                self.out_a = lax.dynamic_update_index_in_dim(zeros, self.own_a, (me + 1) % n, 0)
                self.out_b = lax.dynamic_update_index_in_dim(zeros, self.own_b, (me - 1) % n, 0)
        else:
            t = s - (n - 1)
            self.own_a, self.own_b = got_a, got_b
            self.out_a = lax.dynamic_update_index_in_dim(self.out_a, got_a, (me - t) % n, 0)
            self.out_b = lax.dynamic_update_index_in_dim(self.out_b, got_b, (me + t) % n, 0)
        self.step += 1
        return carry

    def result(self):
        while self.step < self.steps:
            self.issue()
            self.land(())
        return jnp.stack([self.out_a, self.out_b]).reshape(self.shape).astype(jnp.float32)


def per_device(
    tokens,
    lengths,
    placement,
    attention_gain,
    query_weight,
    key_weight,
    value_weight,
    query_gain,
    key_gain,
    output_weight,
    feed_gain,
    gate_weight,
    up_weight,
    down_weight,
    cotangent,
):
    row_count = tokens.shape[0]
    head_width = query_gain.shape[0]
    value_heads = key_weight.shape[1] // head_width
    query_heads = query_weight.shape[1] // head_width
    group_size = query_heads // value_heads
    slot_index = lax.axis_index("fsdp") * lax.axis_size("rep") + lax.axis_index("rep")
    slot_length = lengths[placement[slot_index]]
    valid_rows = (jnp.arange(row_count) < slot_length).astype(jnp.float32)[:, None]
    cosine, sine = angle_tables(row_count, head_width)
    cosine = cosine[:, None, :]
    sine = sine[:, None, :]
    scale = head_width ** (-0.5)
    gain_query = query_gain.astype(jnp.float32)
    gain_key = key_gain.astype(jnp.float32)
    gains = lax.all_gather(jnp.stack([attention_gain, feed_gain]), "fsdp", axis=1, tiled=True)
    attention_set = (
        gains[0],
        lax.all_gather(query_weight, "fsdp", axis=0, tiled=True),
        lax.all_gather(key_weight, "fsdp", axis=0, tiled=True),
        lax.all_gather(value_weight, "fsdp", axis=0, tiled=True),
        lax.all_gather(output_weight, "fsdp", axis=0, tiled=True),
    )
    gate_block = lax.all_to_all(gate_weight, "fsdp", 1, 0, tiled=True)
    up_block = lax.all_to_all(up_weight, "fsdp", 1, 0, tiled=True)
    tokens, gate_block, up_block = lax.optimization_barrier((tokens, gate_block, up_block))
    inputs_wide = tokens.astype(jnp.float32)
    gain_one = attention_set[0].astype(jnp.float32)
    normed_one, normal_one, inverse_one = rms_forward(inputs_wide, gain_one)
    normed_one_low = normed_one.astype(jnp.bfloat16)
    query_raw = jnp.dot(
        normed_one_low, attention_set[1], preferred_element_type=jnp.float32
    ).reshape(row_count, query_heads, head_width)
    key_raw = jnp.dot(normed_one_low, attention_set[2], preferred_element_type=jnp.float32).reshape(
        row_count, value_heads, head_width
    )
    value_low = (
        jnp.dot(normed_one_low, attention_set[3], preferred_element_type=jnp.float32)
        .astype(jnp.bfloat16)
        .reshape(row_count, value_heads, head_width)
    )
    query_normed, query_normal, query_inverse = rms_forward(query_raw, gain_query)
    key_normed, key_normal, key_inverse = rms_forward(key_raw, gain_key)
    query_low = (
        (rotate(query_normed, cosine, sine) * scale)
        .astype(jnp.bfloat16)
        .reshape(row_count, value_heads, group_size, head_width)
    )
    key_low = rotate(key_normed, cosine, sine).astype(jnp.bfloat16)
    scores = masked_scores(query_low, key_low)
    row_top = jnp.max(scores, axis=-1, keepdims=True)
    exp_scores = jnp.exp(scores - row_top)
    row_total = jnp.sum(exp_scores, axis=-1, keepdims=True)
    probs_low = (exp_scores / row_total).astype(jnp.bfloat16)
    log_total = row_top + jnp.log(row_total)
    mixed = jnp.einsum("kgqs,skd->qkgd", probs_low, value_low, preferred_element_type=jnp.float32)
    mixed_low = mixed.reshape(row_count, query_heads * head_width).astype(jnp.bfloat16)
    branch = jnp.dot(mixed_low, attention_set[4], preferred_element_type=jnp.float32)
    middle = inputs_wide + branch
    gain_two = gains[1].astype(jnp.float32)
    normed_two, normal_two, inverse_two = rms_forward(middle, gain_two)
    normed_two_low = normed_two.astype(jnp.bfloat16)
    normed_two_group = lax.all_gather(normed_two_low, "fsdp", axis=0, tiled=True)
    gate_value = jnp.dot(normed_two_group, gate_block, preferred_element_type=jnp.float32)
    up_value = jnp.dot(normed_two_group, up_block, preferred_element_type=jnp.float32)
    hidden_low = (jax.nn.silu(gate_value) * up_value).astype(jnp.bfloat16)
    down_part = jnp.dot(hidden_low, down_weight, preferred_element_type=jnp.float32)
    gate_value, up_value, hidden_low, down_part = lax.optimization_barrier(
        (gate_value, up_value, hidden_low, down_part)
    )
    down_value = lax.psum_scatter(
        down_part.astype(jnp.bfloat16), "fsdp", scatter_dimension=0, tiled=True
    ).astype(jnp.float32)
    grad_top = cotangent.astype(jnp.float32) * valid_rows
    grad_down_low = grad_top.astype(jnp.bfloat16)
    grad_down_group = lax.all_gather(grad_down_low, "fsdp", axis=0, tiled=True)
    down_grad = inner_rows(hidden_low, grad_down_group)
    grad_hidden = times_transposed(grad_down_group, down_weight)
    sigmoid_gate = jax.nn.sigmoid(gate_value)
    grad_gate_low = (
        grad_hidden * up_value * sigmoid_gate * (1.0 + gate_value * (1.0 - sigmoid_gate))
    ).astype(jnp.bfloat16)
    grad_up_low = (grad_hidden * (gate_value * sigmoid_gate)).astype(jnp.bfloat16)
    grad_normed_part = times_transposed(grad_gate_low, gate_block) + times_transposed(
        grad_up_low, up_block
    )
    grad_normed_two = lax.psum_scatter(
        grad_normed_part.astype(jnp.bfloat16), "fsdp", scatter_dimension=0, tiled=True
    ).astype(jnp.float32)
    gate_grad_block = inner_rows(normed_two_group, grad_gate_low)
    up_grad_block = inner_rows(normed_two_group, grad_up_low)
    grad_from_two, gain_two_terms = rms_backward(grad_normed_two, normal_two, inverse_two, gain_two)
    feed_gain_grad = jnp.sum(gain_two_terms, axis=0)
    grad_middle = grad_top + grad_from_two
    feed_parts = (
        None,
        lax.all_to_all(gate_grad_block.astype(jnp.bfloat16), "fsdp", 0, 1, tiled=True),
        lax.all_to_all(up_grad_block.astype(jnp.bfloat16), "fsdp", 0, 1, tiled=True),
        down_grad.astype(jnp.bfloat16),
    )
    feed_width = feed_parts[1].shape[1]
    feed_rows = [feed_parts[1].shape[0], feed_parts[2].shape[0]]
    feed_stack = jnp.concatenate(
        [feed_parts[1], feed_parts[2], feed_parts[3].reshape(-1, feed_width)], axis=0
    )
    ring = RepRing(feed_stack, "rep")
    ring.issue()
    grad_branch_low = grad_middle.astype(jnp.bfloat16)
    output_grad = inner_rows(mixed_low, grad_branch_low)
    grad_mixed_low = (
        times_transposed(grad_branch_low, attention_set[4])
        .astype(jnp.bfloat16)
        .reshape(row_count, value_heads, group_size, head_width)
    )
    grad_mixed_low, output_grad = ring.land((grad_mixed_low, output_grad))
    ring.issue()
    scores_again = masked_scores(query_low, key_low)
    probs_again = jnp.exp(scores_again - log_total)
    probs_again_low = probs_again.astype(jnp.bfloat16)
    grad_probs = jnp.einsum(
        "qkgd,skd->kgqs", grad_mixed_low, value_low, preferred_element_type=jnp.float32
    )
    row_term = jnp.sum(probs_again * grad_probs, axis=-1, keepdims=True)
    grad_scores_low = (probs_again * (grad_probs - row_term)).astype(jnp.bfloat16)
    grad_scores_low, probs_again_low = ring.land((grad_scores_low, probs_again_low))
    ring.issue()
    grad_query_rot = (
        jnp.einsum(
            "kgqs,skd->qkgd", grad_scores_low, key_low, preferred_element_type=jnp.float32
        ).reshape(row_count, query_heads, head_width)
        * scale
    )
    grad_key_rot = jnp.einsum(
        "kgqs,qkgd->skd", grad_scores_low, query_low, preferred_element_type=jnp.float32
    )
    grad_value_low = (
        jnp.einsum(
            "kgqs,qkgd->skd", probs_again_low, grad_mixed_low, preferred_element_type=jnp.float32
        )
        .astype(jnp.bfloat16)
        .reshape(row_count, value_heads * head_width)
    )
    grad_query_rot, grad_key_rot, grad_value_low = ring.land(
        (grad_query_rot, grad_key_rot, grad_value_low)
    )
    grad_query_raw, query_gain_terms = rms_backward(
        unrotate(grad_query_rot, cosine, sine), query_normal, query_inverse, gain_query
    )
    grad_key_raw, key_gain_terms = rms_backward(
        unrotate(grad_key_rot, cosine, sine), key_normal, key_inverse, gain_key
    )
    query_gain_grad = jnp.sum(query_gain_terms, axis=(0, 1))
    key_gain_grad = jnp.sum(key_gain_terms, axis=(0, 1))
    grad_query_low = grad_query_raw.astype(jnp.bfloat16).reshape(
        row_count, query_heads * head_width
    )
    grad_key_low = grad_key_raw.astype(jnp.bfloat16).reshape(row_count, value_heads * head_width)
    value_grad = inner_rows(normed_one_low, grad_value_low)
    query_grad = inner_rows(normed_one_low, grad_query_low)
    key_grad = inner_rows(normed_one_low, grad_key_low)
    grad_normed_one = times_transposed(grad_query_low, attention_set[1])
    grad_normed_one, down_value = lax.optimization_barrier((grad_normed_one, down_value))
    layer_out = ((middle + down_value) * valid_rows).astype(jnp.bfloat16)
    grad_normed_one = (
        grad_normed_one
        + times_transposed(grad_key_low, attention_set[2])
        + times_transposed(grad_value_low, attention_set[3])
    )
    grad_from_one, gain_one_terms = rms_backward(grad_normed_one, normal_one, inverse_one, gain_one)
    attention_gain_grad = jnp.sum(gain_one_terms, axis=0)
    input_grad = grad_middle + grad_from_one
    feed_sum = ring.result()
    feed_rep = (
        feed_sum[: feed_rows[0]],
        feed_sum[feed_rows[0] : feed_rows[0] + feed_rows[1]],
        feed_sum[feed_rows[0] + feed_rows[1] :].reshape(feed_parts[3].shape),
    )
    model_width = attention_gain_grad.shape[0]
    gain_share = model_width // lax.axis_size("fsdp")
    gain_sums = lax.psum(
        jnp.concatenate([attention_gain_grad, feed_gain_grad, query_gain_grad, key_gain_grad]),
        ("fsdp", "rep"),
    )
    gain_start = lax.axis_index("fsdp") * gain_share
    attention_gain_out = lax.dynamic_slice_in_dim(gain_sums, gain_start, gain_share)
    feed_gain_out = lax.dynamic_slice_in_dim(gain_sums, model_width + gain_start, gain_share)
    query_gain_out = gain_sums[2 * model_width : 2 * model_width + head_width]
    key_gain_out = gain_sums[2 * model_width + head_width :]

    def low_sum(v):
        return lax.psum_scatter(v.astype(jnp.bfloat16), "fsdp", scatter_dimension=0, tiled=True)

    attention_parts = (
        None, low_sum(query_grad), low_sum(key_grad), low_sum(value_grad), low_sum(output_grad)
    )
    finals = (
        feed_gain_out,
        feed_rep[0],
        feed_rep[1],
        feed_rep[2],
        attention_gain_out,
        lax.psum(attention_parts[1].astype(jnp.bfloat16), "rep").astype(jnp.float32),
        lax.psum(attention_parts[2].astype(jnp.bfloat16), "rep").astype(jnp.float32),
        lax.psum(attention_parts[3].astype(jnp.bfloat16), "rep").astype(jnp.float32),
        lax.psum(attention_parts[4].astype(jnp.bfloat16), "rep").astype(jnp.float32),
    )
    return (
        layer_out,
        input_grad,
        finals[4],
        finals[5],
        finals[6],
        finals[7],
        query_gain_out,
        key_gain_out,
        finals[8],
        finals[0],
        finals[1],
        finals[2],
        finals[3],
    )


def solution(mesh):
    return jax.shard_map(
        per_device,
        mesh=mesh,
        in_specs=(
            P(("fsdp", "rep"), None),
            P(),
            P(),
            P("fsdp"),
            P("fsdp", None),
            P("fsdp", None),
            P("fsdp", None),
            P(),
            P(),
            P("fsdp", None),
            P("fsdp"),
            P("fsdp", None),
            P("fsdp", None),
            P("fsdp", None),
            P(("fsdp", "rep"), None),
        ),
        out_specs=(
            P(("fsdp", "rep"), None),
            P(("fsdp", "rep"), None),
            P("fsdp"),
            P("fsdp", None),
            P("fsdp", None),
            P("fsdp", None),
            P(),
            P(),
            P("fsdp", None),
            P("fsdp"),
            P("fsdp", None),
            P("fsdp", None),
            P("fsdp", None),
        ),
        check_vma=False,
    )
```

```python
import jax
import jax.numpy as jnp
from jax import lax
from jax.sharding import PartitionSpec as P


EPSILON = 1e-06
ROPE_BASE = 1000000.0


def angle_tables(length, width):
    exponent = jnp.arange(width // 2).astype(jnp.float32) * (2.0 / width)
    frequency = ROPE_BASE ** (-exponent)
    position = jnp.arange(length).astype(jnp.float32)
    phase = position[:, None] * frequency[None, :]
    phase = jnp.concatenate([phase, phase], axis=-1)
    return (jnp.cos(phase), jnp.sin(phase))


def turn_half(values):
    half_width = values.shape[-1] // 2
    return jnp.concatenate([-values[..., half_width:], values[..., :half_width]], axis=-1)


def rotate(values, cosine, sine):
    return values * cosine + turn_half(values) * sine


def unrotate(grads_out, cosine, sine):
    return grads_out * cosine - turn_half(grads_out * sine)


def rms_forward(values, norm_gain):
    inverse = lax.rsqrt(jnp.mean(values * values, axis=-1, keepdims=True) + EPSILON)
    normal = values * inverse
    return (normal * norm_gain, normal, inverse)


def rms_backward(grads_out, normal, inverse, norm_gain):
    scaled = grads_out * norm_gain
    grads_in = inverse * (scaled - normal * jnp.mean(scaled * normal, axis=-1, keepdims=True))
    return (grads_in, grads_out * normal)


def inner_rows(left, right):
    return lax.dot_general(
        left, right, (((0,), (0,)), ((), ())), preferred_element_type=jnp.float32
    )


def times_transposed(left, right):
    return lax.dot_general(
        left, right, (((1,), (1,)), ((), ())), preferred_element_type=jnp.float32
    )


def masked_scores(query_low, key_low):
    scores = jnp.einsum("qkgd,skd->kgqs", query_low, key_low, preferred_element_type=jnp.float32)
    length = query_low.shape[0]
    causal = jnp.arange(length)[:, None] >= jnp.arange(length)[None, :]
    return jnp.where(causal, scores, -1000000000.0)


class RepRing:
    def __init__(self, part, axis):
        n = lax.axis_size(axis)
        self.n, self.axis, self.shape = n, axis, part.shape
        self.me = lax.axis_index(axis)
        self.forward = [(i, (i + 1) % n) for i in range(n)]
        self.backward = [(i, (i - 1) % n) for i in range(n)]
        pieces = part.reshape((2, n, part.shape[0] // (2 * n)) + part.shape[1:])
        self.ahead, self.behind = pieces[0], pieces[1]
        self.run_a = self.take(self.ahead, self.me)
        self.run_b = self.take(self.behind, self.me)
        self.step = 0
        self.steps = 2 * (n - 1)

    def take(self, q, i):
        return lax.dynamic_index_in_dim(q, i % self.n, axis=0, keepdims=False).astype(
            jnp.float32
        )

    def issue(self):
        if self.step >= self.steps:
            return
        if self.step < self.n - 1:
            sends = (self.run_a.astype(jnp.bfloat16), self.run_b.astype(jnp.bfloat16))
        else:
            sends = (self.own_a, self.own_b)
        self.pending = (
            lax.ppermute(sends[0], self.axis, self.forward),
            lax.ppermute(sends[1], self.axis, self.backward),
        )

    def land(self, carry):
        if self.step >= self.steps:
            return carry
        (got_a, got_b), carry = lax.optimization_barrier((self.pending, carry))
        n, me, s = self.n, self.me, self.step
        if s < n - 1:
            self.run_a = got_a.astype(jnp.float32) + self.take(self.ahead, me - 1 - s)
            self.run_b = got_b.astype(jnp.float32) + self.take(self.behind, me + 1 + s)
            if s == n - 2:
                self.own_a = self.run_a.astype(jnp.bfloat16)
                self.own_b = self.run_b.astype(jnp.bfloat16)
                zeros = jnp.zeros(self.ahead.shape, jnp.bfloat16)
                self.out_a = lax.dynamic_update_index_in_dim(zeros, self.own_a, (me + 1) % n, 0)
                self.out_b = lax.dynamic_update_index_in_dim(zeros, self.own_b, (me - 1) % n, 0)
        else:
            t = s - (n - 1)
            self.own_a, self.own_b = got_a, got_b
            self.out_a = lax.dynamic_update_index_in_dim(self.out_a, got_a, (me - t) % n, 0)
            self.out_b = lax.dynamic_update_index_in_dim(self.out_b, got_b, (me + t) % n, 0)
        self.step += 1
        return carry

    def result(self):
        while self.step < self.steps:
            self.issue()
            self.land(())
        return jnp.stack([self.out_a, self.out_b]).reshape(self.shape).astype(jnp.float32)


def per_device(
    tokens,
    lengths,
    placement,
    attention_gain,
    query_weight,
    key_weight,
    value_weight,
    query_gain,
    key_gain,
    output_weight,
    feed_gain,
    gate_weight,
    up_weight,
    down_weight,
    cotangent,
):
    row_count = tokens.shape[0]
    head_width = query_gain.shape[0]
    value_heads = key_weight.shape[1] // head_width
    query_heads = query_weight.shape[1] // head_width
    group_size = query_heads // value_heads
    slot_index = lax.axis_index("fsdp") * lax.axis_size("rep") + lax.axis_index("rep")
    slot_length = lengths[placement[slot_index]]
    valid_rows = (jnp.arange(row_count) < slot_length).astype(jnp.float32)[:, None]
    cosine, sine = angle_tables(row_count, head_width)
    cosine = cosine[:, None, :]
    sine = sine[:, None, :]
    scale = head_width ** (-0.5)
    gain_query = query_gain.astype(jnp.float32)
    gain_key = key_gain.astype(jnp.float32)
    gains = lax.all_gather(jnp.stack([attention_gain, feed_gain]), "fsdp", axis=1, tiled=True)
    attention_set = (
        gains[0],
        lax.all_gather(query_weight, "fsdp", axis=0, tiled=True),
        lax.all_gather(key_weight, "fsdp", axis=0, tiled=True),
        lax.all_gather(value_weight, "fsdp", axis=0, tiled=True),
        lax.all_gather(output_weight, "fsdp", axis=0, tiled=True),
    )
    gate_block = lax.all_to_all(gate_weight, "fsdp", 1, 0, tiled=True)
    up_block = lax.all_to_all(up_weight, "fsdp", 1, 0, tiled=True)
    tokens, gate_block, up_block = lax.optimization_barrier((tokens, gate_block, up_block))
    inputs_wide = tokens.astype(jnp.float32)
    gain_one = attention_set[0].astype(jnp.float32)
    normed_one, normal_one, inverse_one = rms_forward(inputs_wide, gain_one)
    normed_one_low = normed_one.astype(jnp.bfloat16)
    query_raw = jnp.dot(
        normed_one_low, attention_set[1], preferred_element_type=jnp.float32
    ).reshape(row_count, query_heads, head_width)
    key_raw = jnp.dot(normed_one_low, attention_set[2], preferred_element_type=jnp.float32).reshape(
        row_count, value_heads, head_width
    )
    value_low = (
        jnp.dot(normed_one_low, attention_set[3], preferred_element_type=jnp.float32)
        .astype(jnp.bfloat16)
        .reshape(row_count, value_heads, head_width)
    )
    query_normed, query_normal, query_inverse = rms_forward(query_raw, gain_query)
    key_normed, key_normal, key_inverse = rms_forward(key_raw, gain_key)
    query_low = (
        (rotate(query_normed, cosine, sine) * scale)
        .astype(jnp.bfloat16)
        .reshape(row_count, value_heads, group_size, head_width)
    )
    key_low = rotate(key_normed, cosine, sine).astype(jnp.bfloat16)
    scores = masked_scores(query_low, key_low)
    row_top = jnp.max(scores, axis=-1, keepdims=True)
    exp_scores = jnp.exp(scores - row_top)
    row_total = jnp.sum(exp_scores, axis=-1, keepdims=True)
    probs_low = (exp_scores / row_total).astype(jnp.bfloat16)
    log_total = row_top + jnp.log(row_total)
    mixed = jnp.einsum("kgqs,skd->qkgd", probs_low, value_low, preferred_element_type=jnp.float32)
    mixed_low = mixed.reshape(row_count, query_heads * head_width).astype(jnp.bfloat16)
    branch = jnp.dot(mixed_low, attention_set[4], preferred_element_type=jnp.float32)
    middle = inputs_wide + branch
    gain_two = gains[1].astype(jnp.float32)
    normed_two, normal_two, inverse_two = rms_forward(middle, gain_two)
    normed_two_low = normed_two.astype(jnp.bfloat16)
    normed_two_group = lax.all_gather(normed_two_low, "fsdp", axis=0, tiled=True)
    gate_value = jnp.dot(normed_two_group, gate_block, preferred_element_type=jnp.float32)
    up_value = jnp.dot(normed_two_group, up_block, preferred_element_type=jnp.float32)
    hidden_low = (jax.nn.silu(gate_value) * up_value).astype(jnp.bfloat16)
    down_part = jnp.dot(hidden_low, down_weight, preferred_element_type=jnp.float32)
    gate_value, up_value, hidden_low, down_part = lax.optimization_barrier(
        (gate_value, up_value, hidden_low, down_part)
    )
    down_value = lax.psum_scatter(
        down_part.astype(jnp.bfloat16), "fsdp", scatter_dimension=0, tiled=True
    ).astype(jnp.float32)
    grad_top = cotangent.astype(jnp.float32) * valid_rows
    grad_down_low = grad_top.astype(jnp.bfloat16)
    grad_down_group = lax.all_gather(grad_down_low, "fsdp", axis=0, tiled=True)
    down_grad = inner_rows(hidden_low, grad_down_group)
    grad_hidden = times_transposed(grad_down_group, down_weight)
    sigmoid_gate = jax.nn.sigmoid(gate_value)
    grad_gate_low = (
        grad_hidden * up_value * sigmoid_gate * (1.0 + gate_value * (1.0 - sigmoid_gate))
    ).astype(jnp.bfloat16)
    grad_up_low = (grad_hidden * (gate_value * sigmoid_gate)).astype(jnp.bfloat16)
    grad_normed_part = times_transposed(grad_gate_low, gate_block) + times_transposed(
        grad_up_low, up_block
    )
    grad_normed_two = lax.psum_scatter(
        grad_normed_part.astype(jnp.bfloat16), "fsdp", scatter_dimension=0, tiled=True
    ).astype(jnp.float32)
    gate_grad_block = inner_rows(normed_two_group, grad_gate_low)
    up_grad_block = inner_rows(normed_two_group, grad_up_low)
    grad_from_two, gain_two_terms = rms_backward(grad_normed_two, normal_two, inverse_two, gain_two)
    feed_gain_grad = jnp.sum(gain_two_terms, axis=0)
    grad_middle = grad_top + grad_from_two
    feed_parts = (
        None,
        lax.all_to_all(gate_grad_block.astype(jnp.bfloat16), "fsdp", 0, 1, tiled=True),
        lax.all_to_all(up_grad_block.astype(jnp.bfloat16), "fsdp", 0, 1, tiled=True),
        down_grad.astype(jnp.bfloat16),
    )
    feed_width = feed_parts[1].shape[1]
    feed_rows = [feed_parts[1].shape[0], feed_parts[2].shape[0]]
    feed_stack = jnp.concatenate(
        [feed_parts[1], feed_parts[2], feed_parts[3].reshape(-1, feed_width)], axis=0
    )
    ring = RepRing(feed_stack, "rep")
    ring.issue()
    grad_branch_low = grad_middle.astype(jnp.bfloat16)
    output_grad = inner_rows(mixed_low, grad_branch_low)
    grad_mixed_low = (
        times_transposed(grad_branch_low, attention_set[4])
        .astype(jnp.bfloat16)
        .reshape(row_count, value_heads, group_size, head_width)
    )
    grad_mixed_low, output_grad = ring.land((grad_mixed_low, output_grad))
    ring.issue()
    scores_again = masked_scores(query_low, key_low)
    probs_again = jnp.exp(scores_again - log_total)
    probs_again_low = probs_again.astype(jnp.bfloat16)
    grad_probs = jnp.einsum(
        "qkgd,skd->kgqs", grad_mixed_low, value_low, preferred_element_type=jnp.float32
    )
    row_term = jnp.sum(probs_again * grad_probs, axis=-1, keepdims=True)
    grad_scores_low = (probs_again * (grad_probs - row_term)).astype(jnp.bfloat16)
    grad_scores_low, probs_again_low = ring.land((grad_scores_low, probs_again_low))
    ring.issue()
    grad_query_rot = (
        jnp.einsum(
            "kgqs,skd->qkgd", grad_scores_low, key_low, preferred_element_type=jnp.float32
        ).reshape(row_count, query_heads, head_width)
        * scale
    )
    grad_key_rot = jnp.einsum(
        "kgqs,qkgd->skd", grad_scores_low, query_low, preferred_element_type=jnp.float32
    )
    grad_value_low = (
        jnp.einsum(
            "kgqs,qkgd->skd", probs_again_low, grad_mixed_low, preferred_element_type=jnp.float32
        )
        .astype(jnp.bfloat16)
        .reshape(row_count, value_heads * head_width)
    )
    grad_query_rot, grad_key_rot, grad_value_low = ring.land(
        (grad_query_rot, grad_key_rot, grad_value_low)
    )
    ring.issue()
    grad_query_raw, query_gain_terms = rms_backward(
        unrotate(grad_query_rot, cosine, sine), query_normal, query_inverse, gain_query
    )
    grad_key_raw, key_gain_terms = rms_backward(
        unrotate(grad_key_rot, cosine, sine), key_normal, key_inverse, gain_key
    )
    query_gain_grad = jnp.sum(query_gain_terms, axis=(0, 1))
    key_gain_grad = jnp.sum(key_gain_terms, axis=(0, 1))
    grad_query_low = grad_query_raw.astype(jnp.bfloat16).reshape(
        row_count, query_heads * head_width
    )
    grad_key_low = grad_key_raw.astype(jnp.bfloat16).reshape(row_count, value_heads * head_width)
    value_grad = inner_rows(normed_one_low, grad_value_low)
    grad_query_low, grad_key_low = ring.land((grad_query_low, grad_key_low))
    ring.issue()
    query_grad = inner_rows(normed_one_low, grad_query_low)
    key_grad = inner_rows(normed_one_low, grad_key_low)
    grad_normed_one = times_transposed(grad_query_low, attention_set[1])
    grad_normed_one, down_value = ring.land((grad_normed_one, down_value))
    ring.issue()
    layer_out = ((middle + down_value) * valid_rows).astype(jnp.bfloat16)
    grad_normed_one = (
        grad_normed_one
        + times_transposed(grad_key_low, attention_set[2])
        + times_transposed(grad_value_low, attention_set[3])
    )
    grad_from_one, gain_one_terms = rms_backward(grad_normed_one, normal_one, inverse_one, gain_one)
    attention_gain_grad = jnp.sum(gain_one_terms, axis=0)
    input_grad = grad_middle + grad_from_one
    input_grad = ring.land(input_grad)
    feed_sum = ring.result()
    feed_rep = (
        feed_sum[: feed_rows[0]],
        feed_sum[feed_rows[0] : feed_rows[0] + feed_rows[1]],
        feed_sum[feed_rows[0] + feed_rows[1] :].reshape(feed_parts[3].shape),
    )
    model_width = attention_gain_grad.shape[0]
    gain_share = model_width // lax.axis_size("fsdp")
    gain_sums = lax.psum(
        jnp.concatenate([attention_gain_grad, feed_gain_grad, query_gain_grad, key_gain_grad]),
        ("fsdp", "rep"),
    )
    gain_start = lax.axis_index("fsdp") * gain_share
    attention_gain_out = lax.dynamic_slice_in_dim(gain_sums, gain_start, gain_share)
    feed_gain_out = lax.dynamic_slice_in_dim(gain_sums, model_width + gain_start, gain_share)
    query_gain_out = gain_sums[2 * model_width : 2 * model_width + head_width]
    key_gain_out = gain_sums[2 * model_width + head_width :]

    def low_sum(v):
        return lax.psum_scatter(v.astype(jnp.bfloat16), "fsdp", scatter_dimension=0, tiled=True)

    attention_parts = (
        None, low_sum(query_grad), low_sum(key_grad), low_sum(value_grad), low_sum(output_grad)
    )
    output_rep = lax.psum(attention_parts[4].astype(jnp.bfloat16), "rep")
    output_rep, *late_parts = lax.optimization_barrier(
        (output_rep,) + tuple(attention_parts[i].astype(jnp.bfloat16) for i in (1, 2, 3))
    )
    finals = (
        feed_gain_out,
        feed_rep[0],
        feed_rep[1],
        feed_rep[2],
        attention_gain_out,
        lax.psum(late_parts[0], "rep").astype(jnp.float32),
        lax.psum(late_parts[1], "rep").astype(jnp.float32),
        lax.psum(late_parts[2], "rep").astype(jnp.float32),
        output_rep.astype(jnp.float32),
    )
    return (
        layer_out,
        input_grad,
        finals[4],
        finals[5],
        finals[6],
        finals[7],
        query_gain_out,
        key_gain_out,
        finals[8],
        finals[0],
        finals[1],
        finals[2],
        finals[3],
    )


def solution(mesh):
    return jax.shard_map(
        per_device,
        mesh=mesh,
        in_specs=(
            P(("fsdp", "rep"), None),
            P(),
            P(),
            P("fsdp"),
            P("fsdp", None),
            P("fsdp", None),
            P("fsdp", None),
            P(),
            P(),
            P("fsdp", None),
            P("fsdp"),
            P("fsdp", None),
            P("fsdp", None),
            P("fsdp", None),
            P(("fsdp", "rep"), None),
        ),
        out_specs=(
            P(("fsdp", "rep"), None),
            P(("fsdp", "rep"), None),
            P("fsdp"),
            P("fsdp", None),
            P("fsdp", None),
            P("fsdp", None),
            P(),
            P(),
            P("fsdp", None),
            P("fsdp"),
            P("fsdp", None),
            P("fsdp", None),
            P("fsdp", None),
        ),
        check_vma=False,
    )
```

```python
import jax
import jax.numpy as jnp
from jax import lax
from jax.sharding import PartitionSpec as P


EPSILON = 1e-06
ROPE_BASE = 1000000.0


def angle_tables(length, width):
    exponent = jnp.arange(width // 2).astype(jnp.float32) * (2.0 / width)
    frequency = ROPE_BASE ** (-exponent)
    position = jnp.arange(length).astype(jnp.float32)
    phase = position[:, None] * frequency[None, :]
    phase = jnp.concatenate([phase, phase], axis=-1)
    return (jnp.cos(phase), jnp.sin(phase))


def turn_half(values):
    half_width = values.shape[-1] // 2
    return jnp.concatenate([-values[..., half_width:], values[..., :half_width]], axis=-1)


def rotate(values, cosine, sine):
    return values * cosine + turn_half(values) * sine


def unrotate(grads_out, cosine, sine):
    return grads_out * cosine - turn_half(grads_out * sine)


def rms_forward(values, norm_gain):
    inverse = lax.rsqrt(jnp.mean(values * values, axis=-1, keepdims=True) + EPSILON)
    normal = values * inverse
    return (normal * norm_gain, normal, inverse)


def rms_backward(grads_out, normal, inverse, norm_gain):
    scaled = grads_out * norm_gain
    grads_in = inverse * (scaled - normal * jnp.mean(scaled * normal, axis=-1, keepdims=True))
    return (grads_in, grads_out * normal)


def inner_rows(left, right):
    return lax.dot_general(
        left, right, (((0,), (0,)), ((), ())), preferred_element_type=jnp.float32
    )


def times_transposed(left, right):
    return lax.dot_general(
        left, right, (((1,), (1,)), ((), ())), preferred_element_type=jnp.float32
    )


def masked_scores(query_low, key_low):
    scores = jnp.einsum("qkgd,skd->kgqs", query_low, key_low, preferred_element_type=jnp.float32)
    length = query_low.shape[0]
    causal = jnp.arange(length)[:, None] >= jnp.arange(length)[None, :]
    return jnp.where(causal, scores, -1000000000.0)


class RepRing:
    def __init__(self, part, axis):
        n = lax.axis_size(axis)
        self.n, self.axis, self.shape = n, axis, part.shape
        self.me = lax.axis_index(axis)
        self.forward = [(i, (i + 1) % n) for i in range(n)]
        self.backward = [(i, (i - 1) % n) for i in range(n)]
        pieces = part.reshape((2, n, part.shape[0] // (2 * n)) + part.shape[1:])
        self.ahead, self.behind = pieces[0], pieces[1]
        self.run_a = self.take(self.ahead, self.me)
        self.run_b = self.take(self.behind, self.me)
        self.step = 0
        self.steps = 2 * (n - 1)

    def take(self, q, i):
        return lax.dynamic_index_in_dim(q, i % self.n, axis=0, keepdims=False).astype(
            jnp.float32
        )

    def issue(self):
        if self.step >= self.steps:
            return
        if self.step < self.n - 1:
            sends = (self.run_a.astype(jnp.bfloat16), self.run_b.astype(jnp.bfloat16))
        else:
            sends = (self.own_a, self.own_b)
        self.pending = (
            lax.ppermute(sends[0], self.axis, self.forward),
            lax.ppermute(sends[1], self.axis, self.backward),
        )

    def land(self, carry):
        if self.step >= self.steps:
            return carry
        (got_a, got_b), carry = lax.optimization_barrier((self.pending, carry))
        n, me, s = self.n, self.me, self.step
        if s < n - 1:
            self.run_a = got_a.astype(jnp.float32) + self.take(self.ahead, me - 1 - s)
            self.run_b = got_b.astype(jnp.float32) + self.take(self.behind, me + 1 + s)
            if s == n - 2:
                self.own_a = self.run_a.astype(jnp.bfloat16)
                self.own_b = self.run_b.astype(jnp.bfloat16)
                zeros = jnp.zeros(self.ahead.shape, jnp.bfloat16)
                self.out_a = lax.dynamic_update_index_in_dim(zeros, self.own_a, (me + 1) % n, 0)
                self.out_b = lax.dynamic_update_index_in_dim(zeros, self.own_b, (me - 1) % n, 0)
        else:
            t = s - (n - 1)
            self.own_a, self.own_b = got_a, got_b
            self.out_a = lax.dynamic_update_index_in_dim(self.out_a, got_a, (me - t) % n, 0)
            self.out_b = lax.dynamic_update_index_in_dim(self.out_b, got_b, (me + t) % n, 0)
        self.step += 1
        return carry

    def result(self):
        while self.step < self.steps:
            self.issue()
            self.land(())
        return jnp.stack([self.out_a, self.out_b]).reshape(self.shape).astype(jnp.float32)


def per_device(
    tokens,
    lengths,
    placement,
    attention_gain,
    query_weight,
    key_weight,
    value_weight,
    query_gain,
    key_gain,
    output_weight,
    feed_gain,
    gate_weight,
    up_weight,
    down_weight,
    cotangent,
):
    row_count = tokens.shape[0]
    head_width = query_gain.shape[0]
    value_heads = key_weight.shape[1] // head_width
    query_heads = query_weight.shape[1] // head_width
    group_size = query_heads // value_heads
    slot_index = lax.axis_index("fsdp") * lax.axis_size("rep") + lax.axis_index("rep")
    slot_length = lengths[placement[slot_index]]
    valid_rows = (jnp.arange(row_count) < slot_length).astype(jnp.float32)[:, None]
    cosine, sine = angle_tables(row_count, head_width)
    cosine = cosine[:, None, :]
    sine = sine[:, None, :]
    scale = head_width ** (-0.5)
    gain_query = query_gain.astype(jnp.float32)
    gain_key = key_gain.astype(jnp.float32)
    gains = lax.all_gather(jnp.stack([attention_gain, feed_gain]), "fsdp", axis=1, tiled=True)
    attention_set = (
        gains[0],
        lax.all_gather(query_weight, "fsdp", axis=0, tiled=True),
        lax.all_gather(key_weight, "fsdp", axis=0, tiled=True),
        lax.all_gather(value_weight, "fsdp", axis=0, tiled=True),
        lax.all_gather(output_weight, "fsdp", axis=0, tiled=True),
    )
    gate_block = lax.all_to_all(gate_weight, "fsdp", 1, 0, tiled=True)
    up_block = lax.all_to_all(up_weight, "fsdp", 1, 0, tiled=True)
    tokens, gate_block, up_block = lax.optimization_barrier((tokens, gate_block, up_block))
    inputs_wide = tokens.astype(jnp.float32)
    gain_one = attention_set[0].astype(jnp.float32)
    normed_one, normal_one, inverse_one = rms_forward(inputs_wide, gain_one)
    normed_one_low = normed_one.astype(jnp.bfloat16)
    query_raw = jnp.dot(
        normed_one_low, attention_set[1], preferred_element_type=jnp.float32
    ).reshape(row_count, query_heads, head_width)
    key_raw = jnp.dot(normed_one_low, attention_set[2], preferred_element_type=jnp.float32).reshape(
        row_count, value_heads, head_width
    )
    value_low = (
        jnp.dot(normed_one_low, attention_set[3], preferred_element_type=jnp.float32)
        .astype(jnp.bfloat16)
        .reshape(row_count, value_heads, head_width)
    )
    query_normed, query_normal, query_inverse = rms_forward(query_raw, gain_query)
    key_normed, key_normal, key_inverse = rms_forward(key_raw, gain_key)
    query_low = (
        (rotate(query_normed, cosine, sine) * scale)
        .astype(jnp.bfloat16)
        .reshape(row_count, value_heads, group_size, head_width)
    )
    key_low = rotate(key_normed, cosine, sine).astype(jnp.bfloat16)
    scores = masked_scores(query_low, key_low)
    row_top = jnp.max(scores, axis=-1, keepdims=True)
    exp_scores = jnp.exp(scores - row_top)
    row_total = jnp.sum(exp_scores, axis=-1, keepdims=True)
    probs_low = (exp_scores / row_total).astype(jnp.bfloat16)
    log_total = row_top + jnp.log(row_total)
    mixed = jnp.einsum("kgqs,skd->qkgd", probs_low, value_low, preferred_element_type=jnp.float32)
    mixed_low = mixed.reshape(row_count, query_heads * head_width).astype(jnp.bfloat16)
    branch = jnp.dot(mixed_low, attention_set[4], preferred_element_type=jnp.float32)
    middle = inputs_wide + branch
    gain_two = gains[1].astype(jnp.float32)
    normed_two, normal_two, inverse_two = rms_forward(middle, gain_two)
    normed_two_low = normed_two.astype(jnp.bfloat16)
    normed_two_group = lax.all_gather(normed_two_low, "fsdp", axis=0, tiled=True)
    gate_value = jnp.dot(normed_two_group, gate_block, preferred_element_type=jnp.float32)
    up_value = jnp.dot(normed_two_group, up_block, preferred_element_type=jnp.float32)
    hidden_low = (jax.nn.silu(gate_value) * up_value).astype(jnp.bfloat16)
    down_part = jnp.dot(hidden_low, down_weight, preferred_element_type=jnp.float32)
    gate_value, up_value, hidden_low, down_part = lax.optimization_barrier(
        (gate_value, up_value, hidden_low, down_part)
    )
    down_value = lax.psum_scatter(
        down_part.astype(jnp.bfloat16), "fsdp", scatter_dimension=0, tiled=True
    ).astype(jnp.float32)
    grad_top = cotangent.astype(jnp.float32) * valid_rows
    grad_down_low = grad_top.astype(jnp.bfloat16)
    grad_down_group = lax.all_gather(grad_down_low, "fsdp", axis=0, tiled=True)
    down_grad = inner_rows(hidden_low, grad_down_group)
    grad_hidden = times_transposed(grad_down_group, down_weight)
    sigmoid_gate = jax.nn.sigmoid(gate_value)
    grad_gate_low = (
        grad_hidden * up_value * sigmoid_gate * (1.0 + gate_value * (1.0 - sigmoid_gate))
    ).astype(jnp.bfloat16)
    grad_up_low = (grad_hidden * (gate_value * sigmoid_gate)).astype(jnp.bfloat16)
    grad_normed_part = times_transposed(grad_gate_low, gate_block) + times_transposed(
        grad_up_low, up_block
    )
    grad_normed_two = lax.psum_scatter(
        grad_normed_part.astype(jnp.bfloat16), "fsdp", scatter_dimension=0, tiled=True
    ).astype(jnp.float32)
    gate_grad_block = inner_rows(normed_two_group, grad_gate_low)
    up_grad_block = inner_rows(normed_two_group, grad_up_low)
    grad_from_two, gain_two_terms = rms_backward(grad_normed_two, normal_two, inverse_two, gain_two)
    feed_gain_grad = jnp.sum(gain_two_terms, axis=0)
    grad_middle = grad_top + grad_from_two
    feed_parts = (
        None,
        lax.all_to_all(gate_grad_block.astype(jnp.bfloat16), "fsdp", 0, 1, tiled=True),
        lax.all_to_all(up_grad_block.astype(jnp.bfloat16), "fsdp", 0, 1, tiled=True),
        down_grad.astype(jnp.bfloat16),
    )
    feed_width = feed_parts[1].shape[1]
    feed_rows = [feed_parts[1].shape[0], feed_parts[2].shape[0]]
    feed_stack = jnp.concatenate(
        [feed_parts[1], feed_parts[2], feed_parts[3].reshape(-1, feed_width)], axis=0
    )
    ring = RepRing(feed_stack, "rep")
    ring.issue()
    grad_branch_low = grad_middle.astype(jnp.bfloat16)
    output_grad = inner_rows(mixed_low, grad_branch_low)
    grad_mixed_low = (
        times_transposed(grad_branch_low, attention_set[4])
        .astype(jnp.bfloat16)
        .reshape(row_count, value_heads, group_size, head_width)
    )
    grad_mixed_low = ring.land(grad_mixed_low)
    ring.issue()
    scores_again = masked_scores(query_low, key_low)
    probs_again = jnp.exp(scores_again - log_total)
    probs_again_low = probs_again.astype(jnp.bfloat16)
    grad_probs = jnp.einsum(
        "qkgd,skd->kgqs", grad_mixed_low, value_low, preferred_element_type=jnp.float32
    )
    row_term = jnp.sum(probs_again * grad_probs, axis=-1, keepdims=True)
    grad_scores_low = (probs_again * (grad_probs - row_term)).astype(jnp.bfloat16)
    grad_scores_low, probs_again_low = ring.land((grad_scores_low, probs_again_low))
    ring.issue()
    grad_query_rot = (
        jnp.einsum(
            "kgqs,skd->qkgd", grad_scores_low, key_low, preferred_element_type=jnp.float32
        ).reshape(row_count, query_heads, head_width)
        * scale
    )
    grad_key_rot = jnp.einsum(
        "kgqs,qkgd->skd", grad_scores_low, query_low, preferred_element_type=jnp.float32
    )
    grad_value_low = (
        jnp.einsum(
            "kgqs,qkgd->skd", probs_again_low, grad_mixed_low, preferred_element_type=jnp.float32
        )
        .astype(jnp.bfloat16)
        .reshape(row_count, value_heads * head_width)
    )
    value_grad = inner_rows(normed_one_low, grad_value_low)
    grad_query_rot, grad_key_rot, grad_value_low = ring.land(
        (grad_query_rot, grad_key_rot, grad_value_low)
    )
    ring.issue()
    grad_query_raw, query_gain_terms = rms_backward(
        unrotate(grad_query_rot, cosine, sine), query_normal, query_inverse, gain_query
    )
    grad_key_raw, key_gain_terms = rms_backward(
        unrotate(grad_key_rot, cosine, sine), key_normal, key_inverse, gain_key
    )
    query_gain_grad = jnp.sum(query_gain_terms, axis=(0, 1))
    key_gain_grad = jnp.sum(key_gain_terms, axis=(0, 1))
    grad_query_low = grad_query_raw.astype(jnp.bfloat16).reshape(
        row_count, query_heads * head_width
    )
    grad_key_low = grad_key_raw.astype(jnp.bfloat16).reshape(row_count, value_heads * head_width)
    query_grad = inner_rows(normed_one_low, grad_query_low)
    key_grad = inner_rows(normed_one_low, grad_key_low)
    grad_query_low, grad_key_low = ring.land((grad_query_low, grad_key_low))
    ring.issue()
    grad_normed_one = times_transposed(grad_query_low, attention_set[1])
    grad_normed_one, down_value = ring.land((grad_normed_one, down_value))
    ring.issue()
    layer_out = ((middle + down_value) * valid_rows).astype(jnp.bfloat16)
    grad_normed_one = (
        grad_normed_one
        + times_transposed(grad_key_low, attention_set[2])
        + times_transposed(grad_value_low, attention_set[3])
    )
    grad_from_one, gain_one_terms = rms_backward(grad_normed_one, normal_one, inverse_one, gain_one)
    attention_gain_grad = jnp.sum(gain_one_terms, axis=0)
    input_grad = grad_middle + grad_from_one
    input_grad = ring.land(input_grad)
    feed_sum = ring.result()
    feed_rep = (
        feed_sum[: feed_rows[0]],
        feed_sum[feed_rows[0] : feed_rows[0] + feed_rows[1]],
        feed_sum[feed_rows[0] + feed_rows[1] :].reshape(feed_parts[3].shape),
    )
    model_width = attention_gain_grad.shape[0]
    gain_share = model_width // lax.axis_size("fsdp")
    gain_sums = lax.psum(
        jnp.concatenate([attention_gain_grad, feed_gain_grad, query_gain_grad, key_gain_grad]),
        ("fsdp", "rep"),
    )
    gain_start = lax.axis_index("fsdp") * gain_share
    attention_gain_out = lax.dynamic_slice_in_dim(gain_sums, gain_start, gain_share)
    feed_gain_out = lax.dynamic_slice_in_dim(gain_sums, model_width + gain_start, gain_share)
    query_gain_out = gain_sums[2 * model_width : 2 * model_width + head_width]
    key_gain_out = gain_sums[2 * model_width + head_width :]

    def low_sum(v):
        return lax.psum_scatter(v.astype(jnp.bfloat16), "fsdp", scatter_dimension=0, tiled=True)

    attention_parts = (
        None, low_sum(query_grad), low_sum(key_grad), low_sum(value_grad), low_sum(output_grad)
    )
    finals = (
        feed_gain_out,
        feed_rep[0],
        feed_rep[1],
        feed_rep[2],
        attention_gain_out,
        lax.psum(attention_parts[1].astype(jnp.bfloat16), "rep").astype(jnp.float32),
        lax.psum(attention_parts[2].astype(jnp.bfloat16), "rep").astype(jnp.float32),
        lax.psum(attention_parts[3].astype(jnp.bfloat16), "rep").astype(jnp.float32),
        lax.psum(attention_parts[4].astype(jnp.bfloat16), "rep").astype(jnp.float32),
    )
    return (
        layer_out,
        input_grad,
        finals[4],
        finals[5],
        finals[6],
        finals[7],
        query_gain_out,
        key_gain_out,
        finals[8],
        finals[0],
        finals[1],
        finals[2],
        finals[3],
    )


def solution(mesh):
    return jax.shard_map(
        per_device,
        mesh=mesh,
        in_specs=(
            P(("fsdp", "rep"), None),
            P(),
            P(),
            P("fsdp"),
            P("fsdp", None),
            P("fsdp", None),
            P("fsdp", None),
            P(),
            P(),
            P("fsdp", None),
            P("fsdp"),
            P("fsdp", None),
            P("fsdp", None),
            P("fsdp", None),
            P(("fsdp", "rep"), None),
        ),
        out_specs=(
            P(("fsdp", "rep"), None),
            P(("fsdp", "rep"), None),
            P("fsdp"),
            P("fsdp", None),
            P("fsdp", None),
            P("fsdp", None),
            P(),
            P(),
            P("fsdp", None),
            P("fsdp"),
            P("fsdp", None),
            P("fsdp", None),
            P("fsdp", None),
        ),
        check_vma=False,
    )
```

```python
import jax
import jax.numpy as jnp
from jax import lax
from jax.sharding import PartitionSpec as P


EPSILON = 1e-06
ROPE_BASE = 1000000.0


def angle_tables(length, width):
    exponent = jnp.arange(width // 2).astype(jnp.float32) * (2.0 / width)
    frequency = ROPE_BASE ** (-exponent)
    position = jnp.arange(length).astype(jnp.float32)
    phase = position[:, None] * frequency[None, :]
    phase = jnp.concatenate([phase, phase], axis=-1)
    return (jnp.cos(phase), jnp.sin(phase))


def turn_half(values):
    half_width = values.shape[-1] // 2
    return jnp.concatenate([-values[..., half_width:], values[..., :half_width]], axis=-1)


def rotate(values, cosine, sine):
    return values * cosine + turn_half(values) * sine


def unrotate(grads_out, cosine, sine):
    return grads_out * cosine - turn_half(grads_out * sine)


def rms_forward(values, norm_gain):
    inverse = lax.rsqrt(jnp.mean(values * values, axis=-1, keepdims=True) + EPSILON)
    normal = values * inverse
    return (normal * norm_gain, normal, inverse)


def rms_backward(grads_out, normal, inverse, norm_gain):
    scaled = grads_out * norm_gain
    grads_in = inverse * (scaled - normal * jnp.mean(scaled * normal, axis=-1, keepdims=True))
    return (grads_in, grads_out * normal)


def inner_rows(left, right):
    return lax.dot_general(
        left, right, (((0,), (0,)), ((), ())), preferred_element_type=jnp.float32
    )


def times_transposed(left, right):
    return lax.dot_general(
        left, right, (((1,), (1,)), ((), ())), preferred_element_type=jnp.float32
    )


def masked_scores(query_low, key_low):
    scores = jnp.einsum("qkgd,skd->kgqs", query_low, key_low, preferred_element_type=jnp.float32)
    length = query_low.shape[0]
    causal = jnp.arange(length)[:, None] >= jnp.arange(length)[None, :]
    return jnp.where(causal, scores, -1000000000.0)


class RepRing:
    def __init__(self, part, axis):
        n = lax.axis_size(axis)
        self.n, self.axis, self.shape = n, axis, part.shape
        self.me = lax.axis_index(axis)
        self.forward = [(i, (i + 1) % n) for i in range(n)]
        self.backward = [(i, (i - 1) % n) for i in range(n)]
        pieces = part.reshape((2, n, part.shape[0] // (2 * n)) + part.shape[1:])
        self.ahead, self.behind = pieces[0], pieces[1]
        self.run_a = self.take(self.ahead, self.me)
        self.run_b = self.take(self.behind, self.me)
        self.step = 0
        self.steps = 2 * (n - 1)

    def take(self, q, i):
        return lax.dynamic_index_in_dim(q, i % self.n, axis=0, keepdims=False).astype(
            jnp.float32
        )

    def issue(self):
        if self.step >= self.steps:
            return
        if self.step < self.n - 1:
            sends = (self.run_a.astype(jnp.bfloat16), self.run_b.astype(jnp.bfloat16))
        else:
            sends = (self.own_a, self.own_b)
        self.pending = (
            lax.ppermute(sends[0], self.axis, self.forward),
            lax.ppermute(sends[1], self.axis, self.backward),
        )

    def land(self, carry):
        if self.step >= self.steps:
            return carry
        (got_a, got_b), carry = lax.optimization_barrier((self.pending, carry))
        n, me, s = self.n, self.me, self.step
        if s < n - 1:
            self.run_a = got_a.astype(jnp.float32) + self.take(self.ahead, me - 1 - s)
            self.run_b = got_b.astype(jnp.float32) + self.take(self.behind, me + 1 + s)
            if s == n - 2:
                self.own_a = self.run_a.astype(jnp.bfloat16)
                self.own_b = self.run_b.astype(jnp.bfloat16)
                zeros = jnp.zeros(self.ahead.shape, jnp.bfloat16)
                self.out_a = lax.dynamic_update_index_in_dim(zeros, self.own_a, (me + 1) % n, 0)
                self.out_b = lax.dynamic_update_index_in_dim(zeros, self.own_b, (me - 1) % n, 0)
        else:
            t = s - (n - 1)
            self.own_a, self.own_b = got_a, got_b
            self.out_a = lax.dynamic_update_index_in_dim(self.out_a, got_a, (me - t) % n, 0)
            self.out_b = lax.dynamic_update_index_in_dim(self.out_b, got_b, (me + t) % n, 0)
        self.step += 1
        return carry

    def result(self):
        while self.step < self.steps:
            self.issue()
            self.land(())
        return jnp.stack([self.out_a, self.out_b]).reshape(self.shape).astype(jnp.float32)


def per_device(
    tokens,
    lengths,
    placement,
    attention_gain,
    query_weight,
    key_weight,
    value_weight,
    query_gain,
    key_gain,
    output_weight,
    feed_gain,
    gate_weight,
    up_weight,
    down_weight,
    cotangent,
):
    row_count = tokens.shape[0]
    head_width = query_gain.shape[0]
    value_heads = key_weight.shape[1] // head_width
    query_heads = query_weight.shape[1] // head_width
    group_size = query_heads // value_heads
    slot_index = lax.axis_index("fsdp") * lax.axis_size("rep") + lax.axis_index("rep")
    slot_length = lengths[placement[slot_index]]
    valid_rows = (jnp.arange(row_count) < slot_length).astype(jnp.float32)[:, None]
    cosine, sine = angle_tables(row_count, head_width)
    cosine = cosine[:, None, :]
    sine = sine[:, None, :]
    scale = head_width ** (-0.5)
    gain_query = query_gain.astype(jnp.float32)
    gain_key = key_gain.astype(jnp.float32)
    gains = lax.all_gather(jnp.stack([attention_gain, feed_gain]), "fsdp", axis=1, tiled=True)
    attention_set = (
        gains[0],
        lax.all_gather(query_weight, "fsdp", axis=0, tiled=True),
        lax.all_gather(key_weight, "fsdp", axis=0, tiled=True),
        lax.all_gather(value_weight, "fsdp", axis=0, tiled=True),
        lax.all_gather(output_weight, "fsdp", axis=0, tiled=True),
    )
    gate_block = lax.all_to_all(gate_weight, "fsdp", 1, 0, tiled=True)
    up_block = lax.all_to_all(up_weight, "fsdp", 1, 0, tiled=True)
    tokens, gate_block, up_block = lax.optimization_barrier((tokens, gate_block, up_block))
    inputs_wide = tokens.astype(jnp.float32)
    gain_one = attention_set[0].astype(jnp.float32)
    normed_one, normal_one, inverse_one = rms_forward(inputs_wide, gain_one)
    normed_one_low = normed_one.astype(jnp.bfloat16)
    query_raw = jnp.dot(
        normed_one_low, attention_set[1], preferred_element_type=jnp.float32
    ).reshape(row_count, query_heads, head_width)
    key_raw = jnp.dot(normed_one_low, attention_set[2], preferred_element_type=jnp.float32).reshape(
        row_count, value_heads, head_width
    )
    value_low = (
        jnp.dot(normed_one_low, attention_set[3], preferred_element_type=jnp.float32)
        .astype(jnp.bfloat16)
        .reshape(row_count, value_heads, head_width)
    )
    query_normed, query_normal, query_inverse = rms_forward(query_raw, gain_query)
    key_normed, key_normal, key_inverse = rms_forward(key_raw, gain_key)
    query_low = (
        (rotate(query_normed, cosine, sine) * scale)
        .astype(jnp.bfloat16)
        .reshape(row_count, value_heads, group_size, head_width)
    )
    key_low = rotate(key_normed, cosine, sine).astype(jnp.bfloat16)
    scores = masked_scores(query_low, key_low)
    row_top = jnp.max(scores, axis=-1, keepdims=True)
    exp_scores = jnp.exp(scores - row_top)
    row_total = jnp.sum(exp_scores, axis=-1, keepdims=True)
    probs_low = (exp_scores / row_total).astype(jnp.bfloat16)
    log_total = row_top + jnp.log(row_total)
    mixed = jnp.einsum("kgqs,skd->qkgd", probs_low, value_low, preferred_element_type=jnp.float32)
    mixed_low = mixed.reshape(row_count, query_heads * head_width).astype(jnp.bfloat16)
    branch = jnp.dot(mixed_low, attention_set[4], preferred_element_type=jnp.float32)
    middle = inputs_wide + branch
    gain_two = gains[1].astype(jnp.float32)
    normed_two, normal_two, inverse_two = rms_forward(middle, gain_two)
    normed_two_low = normed_two.astype(jnp.bfloat16)
    normed_two_group = lax.all_gather(normed_two_low, "fsdp", axis=0, tiled=True)
    gate_value = jnp.dot(normed_two_group, gate_block, preferred_element_type=jnp.float32)
    up_value = jnp.dot(normed_two_group, up_block, preferred_element_type=jnp.float32)
    hidden_low = (jax.nn.silu(gate_value) * up_value).astype(jnp.bfloat16)
    down_part = jnp.dot(hidden_low, down_weight, preferred_element_type=jnp.float32)
    gate_value, up_value, hidden_low, down_part = lax.optimization_barrier(
        (gate_value, up_value, hidden_low, down_part)
    )
    down_value = lax.psum_scatter(
        down_part.astype(jnp.bfloat16), "fsdp", scatter_dimension=0, tiled=True
    ).astype(jnp.float32)
    grad_top = cotangent.astype(jnp.float32) * valid_rows
    grad_down_low = grad_top.astype(jnp.bfloat16)
    grad_down_group = lax.all_gather(grad_down_low, "fsdp", axis=0, tiled=True)
    down_grad = inner_rows(hidden_low, grad_down_group)
    grad_hidden = times_transposed(grad_down_group, down_weight)
    sigmoid_gate = jax.nn.sigmoid(gate_value)
    grad_gate_low = (
        grad_hidden * up_value * sigmoid_gate * (1.0 + gate_value * (1.0 - sigmoid_gate))
    ).astype(jnp.bfloat16)
    grad_up_low = (grad_hidden * (gate_value * sigmoid_gate)).astype(jnp.bfloat16)
    grad_normed_part = times_transposed(grad_gate_low, gate_block) + times_transposed(
        grad_up_low, up_block
    )
    grad_normed_two = lax.psum_scatter(
        grad_normed_part.astype(jnp.bfloat16), "fsdp", scatter_dimension=0, tiled=True
    ).astype(jnp.float32)
    gate_grad_block = inner_rows(normed_two_group, grad_gate_low)
    up_grad_block = inner_rows(normed_two_group, grad_up_low)
    grad_from_two, gain_two_terms = rms_backward(grad_normed_two, normal_two, inverse_two, gain_two)
    feed_gain_grad = jnp.sum(gain_two_terms, axis=0)
    grad_middle = grad_top + grad_from_two
    feed_parts = (
        None,
        lax.all_to_all(gate_grad_block.astype(jnp.bfloat16), "fsdp", 0, 1, tiled=True),
        lax.all_to_all(up_grad_block.astype(jnp.bfloat16), "fsdp", 0, 1, tiled=True),
        down_grad.astype(jnp.bfloat16),
    )
    feed_width = feed_parts[1].shape[1]
    feed_rows = [feed_parts[1].shape[0], feed_parts[2].shape[0]]
    feed_stack = jnp.concatenate(
        [feed_parts[1], feed_parts[2], feed_parts[3].reshape(-1, feed_width)], axis=0
    )
    ring = RepRing(feed_stack, "rep")
    ring.issue()
    grad_branch_low = grad_middle.astype(jnp.bfloat16)
    output_grad = inner_rows(mixed_low, grad_branch_low)
    grad_mixed_low = (
        times_transposed(grad_branch_low, attention_set[4])
        .astype(jnp.bfloat16)
        .reshape(row_count, value_heads, group_size, head_width)
    )
    grad_mixed_low = ring.land(grad_mixed_low)
    ring.issue()
    scores_again = masked_scores(query_low, key_low)
    probs_again = jnp.exp(scores_again - log_total)
    probs_again_low = probs_again.astype(jnp.bfloat16)
    grad_probs = jnp.einsum(
        "qkgd,skd->kgqs", grad_mixed_low, value_low, preferred_element_type=jnp.float32
    )
    row_term = jnp.sum(probs_again * grad_probs, axis=-1, keepdims=True)
    grad_scores_low = (probs_again * (grad_probs - row_term)).astype(jnp.bfloat16)
    grad_scores_low, probs_again_low = ring.land((grad_scores_low, probs_again_low))
    ring.issue()
    grad_query_rot = (
        jnp.einsum(
            "kgqs,skd->qkgd", grad_scores_low, key_low, preferred_element_type=jnp.float32
        ).reshape(row_count, query_heads, head_width)
        * scale
    )
    grad_key_rot = jnp.einsum(
        "kgqs,qkgd->skd", grad_scores_low, query_low, preferred_element_type=jnp.float32
    )
    grad_value_low = (
        jnp.einsum(
            "kgqs,qkgd->skd", probs_again_low, grad_mixed_low, preferred_element_type=jnp.float32
        )
        .astype(jnp.bfloat16)
        .reshape(row_count, value_heads * head_width)
    )
    value_grad = inner_rows(normed_one_low, grad_value_low)
    grad_query_rot, grad_key_rot, grad_value_low = ring.land(
        (grad_query_rot, grad_key_rot, grad_value_low)
    )
    ring.issue()
    grad_query_raw, query_gain_terms = rms_backward(
        unrotate(grad_query_rot, cosine, sine), query_normal, query_inverse, gain_query
    )
    grad_key_raw, key_gain_terms = rms_backward(
        unrotate(grad_key_rot, cosine, sine), key_normal, key_inverse, gain_key
    )
    query_gain_grad = jnp.sum(query_gain_terms, axis=(0, 1))
    key_gain_grad = jnp.sum(key_gain_terms, axis=(0, 1))
    grad_query_low = grad_query_raw.astype(jnp.bfloat16).reshape(
        row_count, query_heads * head_width
    )
    grad_key_low = grad_key_raw.astype(jnp.bfloat16).reshape(row_count, value_heads * head_width)
    query_grad = inner_rows(normed_one_low, grad_query_low)
    key_grad = inner_rows(normed_one_low, grad_key_low)
    grad_query_low, grad_key_low = ring.land((grad_query_low, grad_key_low))
    ring.issue()
    grad_normed_one = times_transposed(grad_query_low, attention_set[1])
    grad_normed_one, down_value = ring.land((grad_normed_one, down_value))
    ring.issue()
    layer_out = ((middle + down_value) * valid_rows).astype(jnp.bfloat16)
    grad_normed_one = (
        grad_normed_one
        + times_transposed(grad_key_low, attention_set[2])
        + times_transposed(grad_value_low, attention_set[3])
    )
    grad_from_one, gain_one_terms = rms_backward(grad_normed_one, normal_one, inverse_one, gain_one)
    attention_gain_grad = jnp.sum(gain_one_terms, axis=0)
    input_grad = grad_middle + grad_from_one
    input_grad = ring.land(input_grad)
    feed_sum = ring.result()
    feed_rep = (
        feed_sum[: feed_rows[0]],
        feed_sum[feed_rows[0] : feed_rows[0] + feed_rows[1]],
        feed_sum[feed_rows[0] + feed_rows[1] :].reshape(feed_parts[3].shape),
    )
    model_width = attention_gain_grad.shape[0]
    fsdp_count = lax.axis_size("fsdp")
    gain_share = model_width // fsdp_count
    head_terms = jnp.concatenate([query_gain_grad, key_gain_grad])
    head_cols = -(-head_terms.shape[0] // gain_share)
    head_block = jnp.pad(head_terms, (0, head_cols * gain_share - head_terms.shape[0]))
    head_block = head_block.reshape(head_cols, gain_share).T
    gain_cols = jnp.concatenate(
        [
            attention_gain_grad[:, None],
            feed_gain_grad[:, None],
            jnp.tile(head_block, (fsdp_count, 1)),
        ],
        axis=1,
    )
    key_width = key_grad.shape[1]
    key_grad = jnp.concatenate([key_grad, gain_cols], axis=1)

    def low_sum(v):
        return lax.psum_scatter(v.astype(jnp.bfloat16), "fsdp", scatter_dimension=0, tiled=True)

    attention_parts = (
        None, low_sum(query_grad), low_sum(key_grad), low_sum(value_grad), low_sum(output_grad)
    )
    finals = (
        None,
        feed_rep[0],
        feed_rep[1],
        feed_rep[2],
        None,
        lax.psum(attention_parts[1].astype(jnp.bfloat16), "rep").astype(jnp.float32),
        lax.psum(attention_parts[2].astype(jnp.bfloat16), "rep").astype(jnp.float32),
        lax.psum(attention_parts[3].astype(jnp.bfloat16), "rep").astype(jnp.float32),
        lax.psum(attention_parts[4].astype(jnp.bfloat16), "rep").astype(jnp.float32),
    )
    key_rep = finals[6]
    gain_rep = key_rep[:, key_width:]
    attention_gain_out = gain_rep[:, 0]
    feed_gain_out = gain_rep[:, 1]
    head_sum = gain_rep[:, 2:].T.reshape(-1)
    query_gain_out = head_sum[:head_width]
    key_gain_out = head_sum[head_width : 2 * head_width]
    return (
        layer_out,
        input_grad,
        attention_gain_out,
        finals[5],
        key_rep[:, :key_width],
        finals[7],
        query_gain_out,
        key_gain_out,
        finals[8],
        feed_gain_out,
        finals[1],
        finals[2],
        finals[3],
    )


def solution(mesh):
    return jax.shard_map(
        per_device,
        mesh=mesh,
        in_specs=(
            P(("fsdp", "rep"), None),
            P(),
            P(),
            P("fsdp"),
            P("fsdp", None),
            P("fsdp", None),
            P("fsdp", None),
            P(),
            P(),
            P("fsdp", None),
            P("fsdp"),
            P("fsdp", None),
            P("fsdp", None),
            P("fsdp", None),
            P(("fsdp", "rep"), None),
        ),
        out_specs=(
            P(("fsdp", "rep"), None),
            P(("fsdp", "rep"), None),
            P("fsdp"),
            P("fsdp", None),
            P("fsdp", None),
            P("fsdp", None),
            P(),
            P(),
            P("fsdp", None),
            P("fsdp"),
            P("fsdp", None),
            P("fsdp", None),
            P("fsdp", None),
        ),
        check_vma=False,
    )
```

```python
import jax
import jax.numpy as jnp
from jax import lax
from jax.sharding import PartitionSpec as P


EPSILON = 1e-06
ROPE_BASE = 1000000.0


def angle_tables(length, width):
    exponent = jnp.arange(width // 2).astype(jnp.float32) * (2.0 / width)
    frequency = ROPE_BASE ** (-exponent)
    position = jnp.arange(length).astype(jnp.float32)
    phase = position[:, None] * frequency[None, :]
    phase = jnp.concatenate([phase, phase], axis=-1)
    return (jnp.cos(phase), jnp.sin(phase))


def turn_half(values):
    half_width = values.shape[-1] // 2
    return jnp.concatenate([-values[..., half_width:], values[..., :half_width]], axis=-1)


def rotate(values, cosine, sine):
    return values * cosine + turn_half(values) * sine


def unrotate(grads_out, cosine, sine):
    return grads_out * cosine - turn_half(grads_out * sine)


def rms_forward(values, norm_gain):
    inverse = lax.rsqrt(jnp.mean(values * values, axis=-1, keepdims=True) + EPSILON)
    normal = values * inverse
    return (normal * norm_gain, normal, inverse)


def rms_backward(grads_out, normal, inverse, norm_gain):
    scaled = grads_out * norm_gain
    grads_in = inverse * (scaled - normal * jnp.mean(scaled * normal, axis=-1, keepdims=True))
    return (grads_in, grads_out * normal)


def inner_rows(left, right):
    return lax.dot_general(
        left, right, (((0,), (0,)), ((), ())), preferred_element_type=jnp.float32
    )


def times_transposed(left, right):
    return lax.dot_general(
        left, right, (((1,), (1,)), ((), ())), preferred_element_type=jnp.float32
    )


def masked_scores(query_low, key_low):
    scores = jnp.einsum("qkgd,skd->kgqs", query_low, key_low, preferred_element_type=jnp.float32)
    length = query_low.shape[0]
    causal = jnp.arange(length)[:, None] >= jnp.arange(length)[None, :]
    return jnp.where(causal, scores, -1000000000.0)


class RepRing:
    def __init__(self, part, axis):
        n = lax.axis_size(axis)
        self.n, self.axis, self.shape = n, axis, part.shape
        self.me = lax.axis_index(axis)
        self.forward = [(i, (i + 1) % n) for i in range(n)]
        self.backward = [(i, (i - 1) % n) for i in range(n)]
        pieces = part.reshape((2, n, part.shape[0] // (2 * n)) + part.shape[1:])
        self.ahead, self.behind = pieces[0], pieces[1]
        self.run_a = self.take(self.ahead, self.me)
        self.run_b = self.take(self.behind, self.me)
        self.step = 0
        self.steps = 2 * (n - 1)

    def take(self, q, i):
        return lax.dynamic_index_in_dim(q, i % self.n, axis=0, keepdims=False).astype(
            jnp.float32
        )

    def issue(self):
        if self.step >= self.steps:
            return
        if self.step < self.n - 1:
            sends = (self.run_a.astype(jnp.bfloat16), self.run_b.astype(jnp.bfloat16))
        else:
            sends = (self.own_a, self.own_b)
        self.pending = (
            lax.ppermute(sends[0], self.axis, self.forward),
            lax.ppermute(sends[1], self.axis, self.backward),
        )

    def land(self, carry):
        if self.step >= self.steps:
            return carry
        (got_a, got_b), carry = lax.optimization_barrier((self.pending, carry))
        n, me, s = self.n, self.me, self.step
        if s < n - 1:
            self.run_a = got_a.astype(jnp.float32) + self.take(self.ahead, me - 1 - s)
            self.run_b = got_b.astype(jnp.float32) + self.take(self.behind, me + 1 + s)
            if s == n - 2:
                self.own_a = self.run_a.astype(jnp.bfloat16)
                self.own_b = self.run_b.astype(jnp.bfloat16)
                zeros = jnp.zeros(self.ahead.shape, jnp.bfloat16)
                self.out_a = lax.dynamic_update_index_in_dim(zeros, self.own_a, (me + 1) % n, 0)
                self.out_b = lax.dynamic_update_index_in_dim(zeros, self.own_b, (me - 1) % n, 0)
        else:
            t = s - (n - 1)
            self.own_a, self.own_b = got_a, got_b
            self.out_a = lax.dynamic_update_index_in_dim(self.out_a, got_a, (me - t) % n, 0)
            self.out_b = lax.dynamic_update_index_in_dim(self.out_b, got_b, (me + t) % n, 0)
        self.step += 1
        return carry

    def result(self):
        while self.step < self.steps:
            self.issue()
            self.land(())
        return jnp.stack([self.out_a, self.out_b]).reshape(self.shape).astype(jnp.float32)


def per_device(
    tokens,
    lengths,
    placement,
    attention_gain,
    query_weight,
    key_weight,
    value_weight,
    query_gain,
    key_gain,
    output_weight,
    feed_gain,
    gate_weight,
    up_weight,
    down_weight,
    cotangent,
):
    row_count = tokens.shape[0]
    head_width = query_gain.shape[0]
    value_heads = key_weight.shape[1] // head_width
    query_heads = query_weight.shape[1] // head_width
    group_size = query_heads // value_heads
    slot_index = lax.axis_index("fsdp") * lax.axis_size("rep") + lax.axis_index("rep")
    slot_length = lengths[placement[slot_index]]
    valid_rows = (jnp.arange(row_count) < slot_length).astype(jnp.float32)[:, None]
    cosine, sine = angle_tables(row_count, head_width)
    cosine = cosine[:, None, :]
    sine = sine[:, None, :]
    scale = head_width ** (-0.5)
    gain_query = query_gain.astype(jnp.float32)
    gain_key = key_gain.astype(jnp.float32)
    gains = lax.all_gather(jnp.stack([attention_gain, feed_gain]), "fsdp", axis=1, tiled=True)
    attention_set = (
        gains[0],
        lax.all_gather(query_weight, "fsdp", axis=0, tiled=True),
        lax.all_gather(key_weight, "fsdp", axis=0, tiled=True),
        lax.all_gather(value_weight, "fsdp", axis=0, tiled=True),
        lax.all_gather(output_weight, "fsdp", axis=0, tiled=True),
    )
    gate_block = lax.all_to_all(gate_weight, "fsdp", 1, 0, tiled=True)
    up_block = lax.all_to_all(up_weight, "fsdp", 1, 0, tiled=True)
    tokens, gate_block, up_block = lax.optimization_barrier((tokens, gate_block, up_block))
    inputs_wide = tokens.astype(jnp.float32)
    gain_one = attention_set[0].astype(jnp.float32)
    normed_one, normal_one, inverse_one = rms_forward(inputs_wide, gain_one)
    normed_one_low = normed_one.astype(jnp.bfloat16)
    query_raw = jnp.dot(
        normed_one_low, attention_set[1], preferred_element_type=jnp.float32
    ).reshape(row_count, query_heads, head_width)
    key_raw = jnp.dot(normed_one_low, attention_set[2], preferred_element_type=jnp.float32).reshape(
        row_count, value_heads, head_width
    )
    value_low = (
        jnp.dot(normed_one_low, attention_set[3], preferred_element_type=jnp.float32)
        .astype(jnp.bfloat16)
        .reshape(row_count, value_heads, head_width)
    )
    query_normed, query_normal, query_inverse = rms_forward(query_raw, gain_query)
    key_normed, key_normal, key_inverse = rms_forward(key_raw, gain_key)
    query_low = (
        (rotate(query_normed, cosine, sine) * scale)
        .astype(jnp.bfloat16)
        .reshape(row_count, value_heads, group_size, head_width)
    )
    key_low = rotate(key_normed, cosine, sine).astype(jnp.bfloat16)
    scores = masked_scores(query_low, key_low)
    row_top = jnp.max(scores, axis=-1, keepdims=True)
    exp_scores = jnp.exp(scores - row_top)
    row_total = jnp.sum(exp_scores, axis=-1, keepdims=True)
    probs_low = (exp_scores / row_total).astype(jnp.bfloat16)
    log_total = row_top + jnp.log(row_total)
    mixed = jnp.einsum("kgqs,skd->qkgd", probs_low, value_low, preferred_element_type=jnp.float32)
    mixed_low = mixed.reshape(row_count, query_heads * head_width).astype(jnp.bfloat16)
    branch = jnp.dot(mixed_low, attention_set[4], preferred_element_type=jnp.float32)
    middle = inputs_wide + branch
    gain_two = gains[1].astype(jnp.float32)
    normed_two, normal_two, inverse_two = rms_forward(middle, gain_two)
    normed_two_low = normed_two.astype(jnp.bfloat16)
    normed_two_group = lax.all_gather(normed_two_low, "fsdp", axis=0, tiled=True)
    gate_value = jnp.dot(normed_two_group, gate_block, preferred_element_type=jnp.float32)
    up_value = jnp.dot(normed_two_group, up_block, preferred_element_type=jnp.float32)
    hidden_low = (jax.nn.silu(gate_value) * up_value).astype(jnp.bfloat16)
    down_part = jnp.dot(hidden_low, down_weight, preferred_element_type=jnp.float32)
    gate_value, up_value, hidden_low, down_part = lax.optimization_barrier(
        (gate_value, up_value, hidden_low, down_part)
    )
    down_value = lax.psum_scatter(
        down_part.astype(jnp.bfloat16), "fsdp", scatter_dimension=0, tiled=True
    ).astype(jnp.float32)
    grad_top = cotangent.astype(jnp.float32) * valid_rows
    grad_down_low = grad_top.astype(jnp.bfloat16)
    grad_down_group = lax.all_gather(grad_down_low, "fsdp", axis=0, tiled=True)
    down_grad = inner_rows(hidden_low, grad_down_group)
    grad_hidden = times_transposed(grad_down_group, down_weight)
    sigmoid_gate = jax.nn.sigmoid(gate_value)
    grad_gate_low = (
        grad_hidden * up_value * sigmoid_gate * (1.0 + gate_value * (1.0 - sigmoid_gate))
    ).astype(jnp.bfloat16)
    grad_up_low = (grad_hidden * (gate_value * sigmoid_gate)).astype(jnp.bfloat16)
    grad_normed_part = times_transposed(grad_gate_low, gate_block) + times_transposed(
        grad_up_low, up_block
    )
    grad_normed_two = lax.psum_scatter(
        grad_normed_part.astype(jnp.bfloat16), "fsdp", scatter_dimension=0, tiled=True
    ).astype(jnp.float32)
    gate_grad_block = inner_rows(normed_two_group, grad_gate_low)
    up_grad_block = inner_rows(normed_two_group, grad_up_low)
    grad_from_two, gain_two_terms = rms_backward(grad_normed_two, normal_two, inverse_two, gain_two)
    feed_gain_grad = jnp.sum(gain_two_terms, axis=0)
    grad_middle = grad_top + grad_from_two
    feed_parts = (
        None,
        lax.all_to_all(gate_grad_block.astype(jnp.bfloat16), "fsdp", 0, 1, tiled=True),
        lax.all_to_all(up_grad_block.astype(jnp.bfloat16), "fsdp", 0, 1, tiled=True),
        down_grad.astype(jnp.bfloat16),
    )
    feed_width = feed_parts[1].shape[1]
    feed_rows = [feed_parts[1].shape[0], feed_parts[2].shape[0]]
    feed_stack = jnp.concatenate(
        [feed_parts[1], feed_parts[2], feed_parts[3].reshape(-1, feed_width)], axis=0
    )
    ring = RepRing(feed_stack, "rep")
    ring.issue()
    grad_branch_low = grad_middle.astype(jnp.bfloat16)
    output_grad = inner_rows(mixed_low, grad_branch_low)
    grad_mixed_low = (
        times_transposed(grad_branch_low, attention_set[4])
        .astype(jnp.bfloat16)
        .reshape(row_count, value_heads, group_size, head_width)
    )
    grad_mixed_low = ring.land(grad_mixed_low)
    ring.issue()
    scores_again = masked_scores(query_low, key_low)
    probs_again = jnp.exp(scores_again - log_total)
    probs_again_low = probs_again.astype(jnp.bfloat16)
    grad_probs = jnp.einsum(
        "qkgd,skd->kgqs", grad_mixed_low, value_low, preferred_element_type=jnp.float32
    )
    row_term = jnp.sum(probs_again * grad_probs, axis=-1, keepdims=True)
    grad_scores_low = (probs_again * (grad_probs - row_term)).astype(jnp.bfloat16)
    grad_scores_low, probs_again_low = ring.land((grad_scores_low, probs_again_low))
    ring.issue()
    grad_query_rot = (
        jnp.einsum(
            "kgqs,skd->qkgd", grad_scores_low, key_low, preferred_element_type=jnp.float32
        ).reshape(row_count, query_heads, head_width)
        * scale
    )
    grad_key_rot = jnp.einsum(
        "kgqs,qkgd->skd", grad_scores_low, query_low, preferred_element_type=jnp.float32
    )
    grad_value_low = (
        jnp.einsum(
            "kgqs,qkgd->skd", probs_again_low, grad_mixed_low, preferred_element_type=jnp.float32
        )
        .astype(jnp.bfloat16)
        .reshape(row_count, value_heads * head_width)
    )
    value_grad = inner_rows(normed_one_low, grad_value_low)
    grad_query_rot, grad_key_rot, grad_value_low = ring.land(
        (grad_query_rot, grad_key_rot, grad_value_low)
    )
    ring.issue()
    grad_query_raw, query_gain_terms = rms_backward(
        unrotate(grad_query_rot, cosine, sine), query_normal, query_inverse, gain_query
    )
    grad_key_raw, key_gain_terms = rms_backward(
        unrotate(grad_key_rot, cosine, sine), key_normal, key_inverse, gain_key
    )
    query_gain_grad = jnp.sum(query_gain_terms, axis=(0, 1))
    key_gain_grad = jnp.sum(key_gain_terms, axis=(0, 1))
    grad_query_low = grad_query_raw.astype(jnp.bfloat16).reshape(
        row_count, query_heads * head_width
    )
    grad_key_low = grad_key_raw.astype(jnp.bfloat16).reshape(row_count, value_heads * head_width)
    query_grad = inner_rows(normed_one_low, grad_query_low)
    key_grad = inner_rows(normed_one_low, grad_key_low)
    grad_query_low, grad_key_low = ring.land((grad_query_low, grad_key_low))
    ring.issue()
    grad_normed_one = times_transposed(grad_query_low, attention_set[1])
    grad_normed_one, down_value = ring.land((grad_normed_one, down_value))
    ring.issue()
    layer_out = ((middle + down_value) * valid_rows).astype(jnp.bfloat16)
    grad_normed_one = (
        grad_normed_one
        + times_transposed(grad_key_low, attention_set[2])
        + times_transposed(grad_value_low, attention_set[3])
    )
    grad_from_one, gain_one_terms = rms_backward(grad_normed_one, normal_one, inverse_one, gain_one)
    attention_gain_grad = jnp.sum(gain_one_terms, axis=0)
    input_grad = grad_middle + grad_from_one
    input_grad = ring.land(input_grad)
    feed_sum = ring.result()
    feed_rep = (
        feed_sum[: feed_rows[0]],
        feed_sum[feed_rows[0] : feed_rows[0] + feed_rows[1]],
        feed_sum[feed_rows[0] + feed_rows[1] :].reshape(feed_parts[3].shape),
    )
    model_width = attention_gain_grad.shape[0]
    fsdp_count = lax.axis_size("fsdp")
    gain_share = model_width // fsdp_count
    head_terms = jnp.concatenate([query_gain_grad, key_gain_grad])
    head_cols = -(-head_terms.shape[0] // gain_share)
    head_block = jnp.pad(head_terms, (0, head_cols * gain_share - head_terms.shape[0]))
    head_block = head_block.reshape(head_cols, gain_share).T
    gain_cols = jnp.concatenate(
        [
            attention_gain_grad[:, None],
            feed_gain_grad[:, None],
            jnp.tile(head_block, (fsdp_count, 1)),
        ],
        axis=1,
    )
    gain_parts = lax.all_to_all(gain_cols, "fsdp", 0, 1, tiled=True)
    gain_part = gain_parts.reshape(gain_share, fsdp_count, gain_cols.shape[1]).sum(axis=1)
    gain_rep = lax.psum(gain_part.astype(jnp.bfloat16), "rep").astype(jnp.float32)
    attention_gain_out = gain_rep[:, 0]
    feed_gain_out = gain_rep[:, 1]
    head_sum = gain_rep[:, 2:].T.reshape(-1)
    query_gain_out = head_sum[:head_width]
    key_gain_out = head_sum[head_width : 2 * head_width]

    def low_sum(v):
        return lax.psum_scatter(v.astype(jnp.bfloat16), "fsdp", scatter_dimension=0, tiled=True)

    attention_parts = (
        None, low_sum(query_grad), low_sum(key_grad), low_sum(value_grad), low_sum(output_grad)
    )
    finals = (
        feed_gain_out,
        feed_rep[0],
        feed_rep[1],
        feed_rep[2],
        attention_gain_out,
        lax.psum(attention_parts[1].astype(jnp.bfloat16), "rep").astype(jnp.float32),
        lax.psum(attention_parts[2].astype(jnp.bfloat16), "rep").astype(jnp.float32),
        lax.psum(attention_parts[3].astype(jnp.bfloat16), "rep").astype(jnp.float32),
        lax.psum(attention_parts[4].astype(jnp.bfloat16), "rep").astype(jnp.float32),
    )
    return (
        layer_out,
        input_grad,
        finals[4],
        finals[5],
        finals[6],
        finals[7],
        query_gain_out,
        key_gain_out,
        finals[8],
        finals[0],
        finals[1],
        finals[2],
        finals[3],
    )


def solution(mesh):
    return jax.shard_map(
        per_device,
        mesh=mesh,
        in_specs=(
            P(("fsdp", "rep"), None),
            P(),
            P(),
            P("fsdp"),
            P("fsdp", None),
            P("fsdp", None),
            P("fsdp", None),
            P(),
            P(),
            P("fsdp", None),
            P("fsdp"),
            P("fsdp", None),
            P("fsdp", None),
            P("fsdp", None),
            P(("fsdp", "rep"), None),
        ),
        out_specs=(
            P(("fsdp", "rep"), None),
            P(("fsdp", "rep"), None),
            P("fsdp"),
            P("fsdp", None),
            P("fsdp", None),
            P("fsdp", None),
            P(),
            P(),
            P("fsdp", None),
            P("fsdp"),
            P("fsdp", None),
            P("fsdp", None),
            P("fsdp", None),
        ),
        check_vma=False,
    )
```

```python
import jax
import jax.numpy as jnp
from jax import lax
from jax.sharding import PartitionSpec as P


EPSILON = 1e-06
ROPE_BASE = 1000000.0


def angle_tables(length, width):
    exponent = jnp.arange(width // 2).astype(jnp.float32) * (2.0 / width)
    frequency = ROPE_BASE ** (-exponent)
    position = jnp.arange(length).astype(jnp.float32)
    phase = position[:, None] * frequency[None, :]
    phase = jnp.concatenate([phase, phase], axis=-1)
    return (jnp.cos(phase), jnp.sin(phase))


def turn_half(values):
    half_width = values.shape[-1] // 2
    return jnp.concatenate([-values[..., half_width:], values[..., :half_width]], axis=-1)


def rotate(values, cosine, sine):
    return values * cosine + turn_half(values) * sine


def unrotate(grads_out, cosine, sine):
    return grads_out * cosine - turn_half(grads_out * sine)


def rms_forward(values, norm_gain):
    inverse = lax.rsqrt(jnp.mean(values * values, axis=-1, keepdims=True) + EPSILON)
    normal = values * inverse
    return (normal * norm_gain, normal, inverse)


def rms_backward(grads_out, normal, inverse, norm_gain):
    scaled = grads_out * norm_gain
    grads_in = inverse * (scaled - normal * jnp.mean(scaled * normal, axis=-1, keepdims=True))
    return (grads_in, grads_out * normal)


def inner_rows(left, right):
    return lax.dot_general(
        left, right, (((0,), (0,)), ((), ())), preferred_element_type=jnp.float32
    )


def times_transposed(left, right):
    return lax.dot_general(
        left, right, (((1,), (1,)), ((), ())), preferred_element_type=jnp.float32
    )


def masked_scores(query_low, key_low):
    scores = jnp.einsum("qkgd,skd->kgqs", query_low, key_low, preferred_element_type=jnp.float32)
    length = query_low.shape[0]
    causal = jnp.arange(length)[:, None] >= jnp.arange(length)[None, :]
    return jnp.where(causal, scores, -1000000000.0)


class RepRing:
    def __init__(self, part, axis):
        n = lax.axis_size(axis)
        self.n, self.axis, self.shape = n, axis, part.shape
        self.me = lax.axis_index(axis)
        self.forward = [(i, (i + 1) % n) for i in range(n)]
        self.backward = [(i, (i - 1) % n) for i in range(n)]
        pieces = part.reshape((2, n, part.shape[0] // (2 * n)) + part.shape[1:])
        self.ahead, self.behind = pieces[0], pieces[1]
        self.run_a = self.take(self.ahead, self.me)
        self.run_b = self.take(self.behind, self.me)
        self.step = 0
        self.steps = 2 * (n - 1)

    def take(self, q, i):
        return lax.dynamic_index_in_dim(q, i % self.n, axis=0, keepdims=False).astype(
            jnp.float32
        )

    def issue(self):
        if self.step >= self.steps:
            return
        if self.step < self.n - 1:
            sends = (self.run_a.astype(jnp.bfloat16), self.run_b.astype(jnp.bfloat16))
        else:
            sends = (self.own_a, self.own_b)
        self.pending = (
            lax.ppermute(sends[0], self.axis, self.forward),
            lax.ppermute(sends[1], self.axis, self.backward),
        )

    def land(self, carry):
        if self.step >= self.steps:
            return carry
        (got_a, got_b), carry = lax.optimization_barrier((self.pending, carry))
        n, me, s = self.n, self.me, self.step
        if s < n - 1:
            self.run_a = got_a.astype(jnp.float32) + self.take(self.ahead, me - 1 - s)
            self.run_b = got_b.astype(jnp.float32) + self.take(self.behind, me + 1 + s)
            if s == n - 2:
                self.own_a = self.run_a.astype(jnp.bfloat16)
                self.own_b = self.run_b.astype(jnp.bfloat16)
                zeros = jnp.zeros(self.ahead.shape, jnp.bfloat16)
                self.out_a = lax.dynamic_update_index_in_dim(zeros, self.own_a, (me + 1) % n, 0)
                self.out_b = lax.dynamic_update_index_in_dim(zeros, self.own_b, (me - 1) % n, 0)
        else:
            t = s - (n - 1)
            self.own_a, self.own_b = got_a, got_b
            self.out_a = lax.dynamic_update_index_in_dim(self.out_a, got_a, (me - t) % n, 0)
            self.out_b = lax.dynamic_update_index_in_dim(self.out_b, got_b, (me + t) % n, 0)
        self.step += 1
        return carry

    def result(self):
        while self.step < self.steps:
            self.issue()
            self.land(())
        return jnp.stack([self.out_a, self.out_b]).reshape(self.shape).astype(jnp.float32)


def per_device(
    tokens,
    lengths,
    placement,
    attention_gain,
    query_weight,
    key_weight,
    value_weight,
    query_gain,
    key_gain,
    output_weight,
    feed_gain,
    gate_weight,
    up_weight,
    down_weight,
    cotangent,
):
    row_count = tokens.shape[0]
    head_width = query_gain.shape[0]
    value_heads = key_weight.shape[1] // head_width
    query_heads = query_weight.shape[1] // head_width
    group_size = query_heads // value_heads
    slot_index = lax.axis_index("fsdp") * lax.axis_size("rep") + lax.axis_index("rep")
    slot_length = lengths[placement[slot_index]]
    valid_rows = (jnp.arange(row_count) < slot_length).astype(jnp.float32)[:, None]
    cosine, sine = angle_tables(row_count, head_width)
    cosine = cosine[:, None, :]
    sine = sine[:, None, :]
    scale = head_width ** (-0.5)
    gain_query = query_gain.astype(jnp.float32)
    gain_key = key_gain.astype(jnp.float32)
    gains = lax.all_gather(jnp.stack([attention_gain, feed_gain]), "fsdp", axis=1, tiled=True)
    attention_set = (
        gains[0],
        lax.all_gather(query_weight, "fsdp", axis=0, tiled=True),
        lax.all_gather(key_weight, "fsdp", axis=0, tiled=True),
        lax.all_gather(value_weight, "fsdp", axis=0, tiled=True),
        lax.all_gather(output_weight, "fsdp", axis=0, tiled=True),
    )
    gate_block = lax.all_to_all(gate_weight, "fsdp", 1, 0, tiled=True)
    up_block = lax.all_to_all(up_weight, "fsdp", 1, 0, tiled=True)
    tokens, gate_block, up_block = lax.optimization_barrier((tokens, gate_block, up_block))
    inputs_wide = tokens.astype(jnp.float32)
    gain_one = attention_set[0].astype(jnp.float32)
    normed_one, normal_one, inverse_one = rms_forward(inputs_wide, gain_one)
    normed_one_low = normed_one.astype(jnp.bfloat16)
    query_raw = jnp.dot(
        normed_one_low, attention_set[1], preferred_element_type=jnp.float32
    ).reshape(row_count, query_heads, head_width)
    key_raw = jnp.dot(normed_one_low, attention_set[2], preferred_element_type=jnp.float32).reshape(
        row_count, value_heads, head_width
    )
    value_low = (
        jnp.dot(normed_one_low, attention_set[3], preferred_element_type=jnp.float32)
        .astype(jnp.bfloat16)
        .reshape(row_count, value_heads, head_width)
    )
    query_normed, query_normal, query_inverse = rms_forward(query_raw, gain_query)
    key_normed, key_normal, key_inverse = rms_forward(key_raw, gain_key)
    query_low = (
        (rotate(query_normed, cosine, sine) * scale)
        .astype(jnp.bfloat16)
        .reshape(row_count, value_heads, group_size, head_width)
    )
    key_low = rotate(key_normed, cosine, sine).astype(jnp.bfloat16)
    scores = masked_scores(query_low, key_low)
    row_top = jnp.max(scores, axis=-1, keepdims=True)
    exp_scores = jnp.exp(scores - row_top)
    row_total = jnp.sum(exp_scores, axis=-1, keepdims=True)
    probs_low = (exp_scores / row_total).astype(jnp.bfloat16)
    log_total = row_top + jnp.log(row_total)
    mixed = jnp.einsum("kgqs,skd->qkgd", probs_low, value_low, preferred_element_type=jnp.float32)
    mixed_low = mixed.reshape(row_count, query_heads * head_width).astype(jnp.bfloat16)
    branch = jnp.dot(mixed_low, attention_set[4], preferred_element_type=jnp.float32)
    middle = inputs_wide + branch
    gain_two = gains[1].astype(jnp.float32)
    normed_two, normal_two, inverse_two = rms_forward(middle, gain_two)
    normed_two_low = normed_two.astype(jnp.bfloat16)
    normed_two_group = lax.all_gather(normed_two_low, "fsdp", axis=0, tiled=True)
    gate_value = jnp.dot(normed_two_group, gate_block, preferred_element_type=jnp.float32)
    up_value = jnp.dot(normed_two_group, up_block, preferred_element_type=jnp.float32)
    hidden_low = (jax.nn.silu(gate_value) * up_value).astype(jnp.bfloat16)
    down_part = jnp.dot(hidden_low, down_weight, preferred_element_type=jnp.float32)
    gate_value, up_value, hidden_low, down_part = lax.optimization_barrier(
        (gate_value, up_value, hidden_low, down_part)
    )
    down_value = lax.psum_scatter(
        down_part.astype(jnp.bfloat16), "fsdp", scatter_dimension=0, tiled=True
    ).astype(jnp.float32)
    grad_top = cotangent.astype(jnp.float32) * valid_rows
    grad_down_low = grad_top.astype(jnp.bfloat16)
    grad_down_group = lax.all_gather(grad_down_low, "fsdp", axis=0, tiled=True)
    down_grad = inner_rows(hidden_low, grad_down_group)
    grad_hidden = times_transposed(grad_down_group, down_weight)
    sigmoid_gate = jax.nn.sigmoid(gate_value)
    grad_gate_low = (
        grad_hidden * up_value * sigmoid_gate * (1.0 + gate_value * (1.0 - sigmoid_gate))
    ).astype(jnp.bfloat16)
    grad_up_low = (grad_hidden * (gate_value * sigmoid_gate)).astype(jnp.bfloat16)
    grad_normed_part = times_transposed(grad_gate_low, gate_block) + times_transposed(
        grad_up_low, up_block
    )
    grad_normed_two = lax.psum_scatter(
        grad_normed_part.astype(jnp.bfloat16), "fsdp", scatter_dimension=0, tiled=True
    ).astype(jnp.float32)
    gate_grad_block = inner_rows(normed_two_group, grad_gate_low)
    up_grad_block = inner_rows(normed_two_group, grad_up_low)
    grad_from_two, gain_two_terms = rms_backward(grad_normed_two, normal_two, inverse_two, gain_two)
    feed_gain_grad = jnp.sum(gain_two_terms, axis=0)
    grad_middle = grad_top + grad_from_two
    feed_parts = (
        None,
        lax.all_to_all(gate_grad_block.astype(jnp.bfloat16), "fsdp", 0, 1, tiled=True),
        lax.all_to_all(up_grad_block.astype(jnp.bfloat16), "fsdp", 0, 1, tiled=True),
        down_grad.astype(jnp.bfloat16),
    )
    feed_width = feed_parts[1].shape[1]
    feed_rows = [feed_parts[1].shape[0], feed_parts[2].shape[0]]
    feed_stack = jnp.concatenate(
        [feed_parts[1], feed_parts[2], feed_parts[3].reshape(-1, feed_width)], axis=0
    )
    ring = RepRing(feed_stack, "rep")
    ring.issue()
    grad_branch_low = grad_middle.astype(jnp.bfloat16)
    output_grad = inner_rows(mixed_low, grad_branch_low)
    grad_mixed_low = (
        times_transposed(grad_branch_low, attention_set[4])
        .astype(jnp.bfloat16)
        .reshape(row_count, value_heads, group_size, head_width)
    )
    grad_mixed_low = ring.land(grad_mixed_low)
    ring.issue()
    scores_again = masked_scores(query_low, key_low)
    probs_again = jnp.exp(scores_again - log_total)
    probs_again_low = probs_again.astype(jnp.bfloat16)
    grad_probs = jnp.einsum(
        "qkgd,skd->kgqs", grad_mixed_low, value_low, preferred_element_type=jnp.float32
    )
    row_term = jnp.sum(probs_again * grad_probs, axis=-1, keepdims=True)
    grad_scores_low = (probs_again * (grad_probs - row_term)).astype(jnp.bfloat16)
    grad_scores_low, probs_again_low = ring.land((grad_scores_low, probs_again_low))
    ring.issue()
    grad_query_rot = (
        jnp.einsum(
            "kgqs,skd->qkgd", grad_scores_low, key_low, preferred_element_type=jnp.float32
        ).reshape(row_count, query_heads, head_width)
        * scale
    )
    grad_key_rot = jnp.einsum(
        "kgqs,qkgd->skd", grad_scores_low, query_low, preferred_element_type=jnp.float32
    )
    grad_value_low = (
        jnp.einsum(
            "kgqs,qkgd->skd", probs_again_low, grad_mixed_low, preferred_element_type=jnp.float32
        )
        .astype(jnp.bfloat16)
        .reshape(row_count, value_heads * head_width)
    )
    value_grad = inner_rows(normed_one_low, grad_value_low)
    grad_query_rot, grad_key_rot, grad_value_low = ring.land(
        (grad_query_rot, grad_key_rot, grad_value_low)
    )
    ring.issue()
    grad_query_raw, query_gain_terms = rms_backward(
        unrotate(grad_query_rot, cosine, sine), query_normal, query_inverse, gain_query
    )
    grad_key_raw, key_gain_terms = rms_backward(
        unrotate(grad_key_rot, cosine, sine), key_normal, key_inverse, gain_key
    )
    query_gain_grad = jnp.sum(query_gain_terms, axis=(0, 1))
    key_gain_grad = jnp.sum(key_gain_terms, axis=(0, 1))
    grad_query_low = grad_query_raw.astype(jnp.bfloat16).reshape(
        row_count, query_heads * head_width
    )
    grad_key_low = grad_key_raw.astype(jnp.bfloat16).reshape(row_count, value_heads * head_width)
    query_grad = inner_rows(normed_one_low, grad_query_low)
    key_grad = inner_rows(normed_one_low, grad_key_low)
    grad_query_low, grad_key_low = ring.land((grad_query_low, grad_key_low))
    ring.issue()
    grad_normed_one = times_transposed(grad_query_low, attention_set[1])
    grad_normed_one, down_value = ring.land((grad_normed_one, down_value))
    ring.issue()
    layer_out = ((middle + down_value) * valid_rows).astype(jnp.bfloat16)
    grad_normed_one = (
        grad_normed_one
        + times_transposed(grad_key_low, attention_set[2])
        + times_transposed(grad_value_low, attention_set[3])
    )
    grad_from_one, gain_one_terms = rms_backward(grad_normed_one, normal_one, inverse_one, gain_one)
    attention_gain_grad = jnp.sum(gain_one_terms, axis=0)
    input_grad = grad_middle + grad_from_one
    input_grad = ring.land(input_grad)
    feed_sum = ring.result()
    feed_rep = (
        feed_sum[: feed_rows[0]],
        feed_sum[feed_rows[0] : feed_rows[0] + feed_rows[1]],
        feed_sum[feed_rows[0] + feed_rows[1] :].reshape(feed_parts[3].shape),
    )
    model_width = attention_gain_grad.shape[0]
    fsdp_count = lax.axis_size("fsdp")
    gain_share = model_width // fsdp_count
    head_terms = jnp.concatenate([query_gain_grad, key_gain_grad])
    head_cols = -(-head_terms.shape[0] // gain_share)
    head_block = jnp.pad(head_terms, (0, head_cols * gain_share - head_terms.shape[0]))
    head_block = head_block.reshape(head_cols, gain_share).T
    gain_cols = jnp.concatenate(
        [
            attention_gain_grad[:, None],
            feed_gain_grad[:, None],
            jnp.tile(head_block, (fsdp_count, 1)),
        ],
        axis=1,
    )
    gain_parts = lax.all_to_all(gain_cols, "fsdp", 0, 1, tiled=True)
    gain_part = gain_parts.reshape(gain_share, fsdp_count, gain_cols.shape[1]).sum(axis=1)

    def low_sum(v):
        return lax.psum_scatter(v.astype(jnp.bfloat16), "fsdp", scatter_dimension=0, tiled=True)

    attention_parts = (
        None, low_sum(query_grad), low_sum(key_grad), low_sum(value_grad), low_sum(output_grad)
    )
    finals = (None, feed_rep[0], feed_rep[1], feed_rep[2], None)
    attention_rep = lax.psum(
        tuple(attention_parts[i].astype(jnp.bfloat16) for i in (1, 2, 3, 4)), "rep"
    )
    gain_part, attention_rep = lax.optimization_barrier((gain_part, attention_rep))
    finals = finals + tuple(r.astype(jnp.float32) for r in attention_rep)
    gain_rep = lax.psum(gain_part.astype(jnp.bfloat16), "rep").astype(jnp.float32)
    attention_gain_out = gain_rep[:, 0]
    feed_gain_out = gain_rep[:, 1]
    head_sum = gain_rep[:, 2:].T.reshape(-1)
    query_gain_out = head_sum[:head_width]
    key_gain_out = head_sum[head_width : 2 * head_width]
    return (
        layer_out,
        input_grad,
        attention_gain_out,
        finals[5],
        finals[6],
        finals[7],
        query_gain_out,
        key_gain_out,
        finals[8],
        feed_gain_out,
        finals[1],
        finals[2],
        finals[3],
    )


def solution(mesh):
    return jax.shard_map(
        per_device,
        mesh=mesh,
        in_specs=(
            P(("fsdp", "rep"), None),
            P(),
            P(),
            P("fsdp"),
            P("fsdp", None),
            P("fsdp", None),
            P("fsdp", None),
            P(),
            P(),
            P("fsdp", None),
            P("fsdp"),
            P("fsdp", None),
            P("fsdp", None),
            P("fsdp", None),
            P(("fsdp", "rep"), None),
        ),
        out_specs=(
            P(("fsdp", "rep"), None),
            P(("fsdp", "rep"), None),
            P("fsdp"),
            P("fsdp", None),
            P("fsdp", None),
            P("fsdp", None),
            P(),
            P(),
            P("fsdp", None),
            P("fsdp"),
            P("fsdp", None),
            P("fsdp", None),
            P("fsdp", None),
        ),
        check_vma=False,
    )
```

```python
import jax
import jax.numpy as jnp
from jax import lax
from jax.sharding import PartitionSpec as P


EPSILON = 1e-06
ROPE_BASE = 1000000.0


def angle_tables(length, width):
    exponent = jnp.arange(width // 2).astype(jnp.float32) * (2.0 / width)
    frequency = ROPE_BASE ** (-exponent)
    position = jnp.arange(length).astype(jnp.float32)
    phase = position[:, None] * frequency[None, :]
    phase = jnp.concatenate([phase, phase], axis=-1)
    return (jnp.cos(phase), jnp.sin(phase))


def turn_half(values):
    half_width = values.shape[-1] // 2
    return jnp.concatenate([-values[..., half_width:], values[..., :half_width]], axis=-1)


def rotate(values, cosine, sine):
    return values * cosine + turn_half(values) * sine


def unrotate(grads_out, cosine, sine):
    return grads_out * cosine - turn_half(grads_out * sine)


def rms_forward(values, norm_gain):
    inverse = lax.rsqrt(jnp.mean(values * values, axis=-1, keepdims=True) + EPSILON)
    normal = values * inverse
    return (normal * norm_gain, normal, inverse)


def rms_backward(grads_out, normal, inverse, norm_gain):
    scaled = grads_out * norm_gain
    grads_in = inverse * (scaled - normal * jnp.mean(scaled * normal, axis=-1, keepdims=True))
    return (grads_in, grads_out * normal)


def inner_rows(left, right):
    return lax.dot_general(
        left, right, (((0,), (0,)), ((), ())), preferred_element_type=jnp.float32
    )


def times_transposed(left, right):
    return lax.dot_general(
        left, right, (((1,), (1,)), ((), ())), preferred_element_type=jnp.float32
    )


def masked_scores(query_low, key_low):
    scores = jnp.einsum("qkgd,skd->kgqs", query_low, key_low, preferred_element_type=jnp.float32)
    length = query_low.shape[0]
    causal = jnp.arange(length)[:, None] >= jnp.arange(length)[None, :]
    return jnp.where(causal, scores, -1000000000.0)


class RepRing:
    def __init__(self, part, axis):
        n = lax.axis_size(axis)
        self.n, self.axis, self.shape = n, axis, part.shape
        self.me = lax.axis_index(axis)
        self.forward = [(i, (i + 1) % n) for i in range(n)]
        self.backward = [(i, (i - 1) % n) for i in range(n)]
        pieces = part.reshape((2, n, part.shape[0] // (2 * n)) + part.shape[1:])
        self.ahead, self.behind = pieces[0], pieces[1]
        self.run_a = self.take(self.ahead, self.me)
        self.run_b = self.take(self.behind, self.me)
        self.step = 0
        self.steps = 2 * (n - 1)

    def take(self, q, i):
        return lax.dynamic_index_in_dim(q, i % self.n, axis=0, keepdims=False).astype(
            jnp.float32
        )

    def issue(self):
        if self.step >= self.steps:
            return
        if self.step < self.n - 1:
            sends = (self.run_a.astype(jnp.bfloat16), self.run_b.astype(jnp.bfloat16))
        else:
            sends = (self.own_a, self.own_b)
        self.pending = (
            lax.ppermute(sends[0], self.axis, self.forward),
            lax.ppermute(sends[1], self.axis, self.backward),
        )

    def land(self, carry):
        if self.step >= self.steps:
            return carry
        (got_a, got_b), carry = lax.optimization_barrier((self.pending, carry))
        n, me, s = self.n, self.me, self.step
        if s < n - 1:
            self.run_a = got_a.astype(jnp.float32) + self.take(self.ahead, me - 1 - s)
            self.run_b = got_b.astype(jnp.float32) + self.take(self.behind, me + 1 + s)
            if s == n - 2:
                self.own_a = self.run_a.astype(jnp.bfloat16)
                self.own_b = self.run_b.astype(jnp.bfloat16)
                zeros = jnp.zeros(self.ahead.shape, jnp.bfloat16)
                self.out_a = lax.dynamic_update_index_in_dim(zeros, self.own_a, (me + 1) % n, 0)
                self.out_b = lax.dynamic_update_index_in_dim(zeros, self.own_b, (me - 1) % n, 0)
        else:
            t = s - (n - 1)
            self.own_a, self.own_b = got_a, got_b
            self.out_a = lax.dynamic_update_index_in_dim(self.out_a, got_a, (me - t) % n, 0)
            self.out_b = lax.dynamic_update_index_in_dim(self.out_b, got_b, (me + t) % n, 0)
        self.step += 1
        return carry

    def result(self):
        while self.step < self.steps:
            self.issue()
            self.land(())
        return jnp.stack([self.out_a, self.out_b]).reshape(self.shape).astype(jnp.float32)


def per_device(
    tokens,
    lengths,
    placement,
    attention_gain,
    query_weight,
    key_weight,
    value_weight,
    query_gain,
    key_gain,
    output_weight,
    feed_gain,
    gate_weight,
    up_weight,
    down_weight,
    cotangent,
):
    row_count = tokens.shape[0]
    head_width = query_gain.shape[0]
    value_heads = key_weight.shape[1] // head_width
    query_heads = query_weight.shape[1] // head_width
    group_size = query_heads // value_heads
    slot_index = lax.axis_index("fsdp") * lax.axis_size("rep") + lax.axis_index("rep")
    slot_length = lengths[placement[slot_index]]
    valid_rows = (jnp.arange(row_count) < slot_length).astype(jnp.float32)[:, None]
    cosine, sine = angle_tables(row_count, head_width)
    cosine = cosine[:, None, :]
    sine = sine[:, None, :]
    scale = head_width ** (-0.5)
    gain_query = query_gain.astype(jnp.float32)
    gain_key = key_gain.astype(jnp.float32)
    gains = lax.all_gather(jnp.stack([attention_gain, feed_gain]), "fsdp", axis=1, tiled=True)
    attention_set = (
        gains[0],
        lax.all_gather(query_weight, "fsdp", axis=0, tiled=True),
        lax.all_gather(key_weight, "fsdp", axis=0, tiled=True),
        lax.all_gather(value_weight, "fsdp", axis=0, tiled=True),
        lax.all_gather(output_weight, "fsdp", axis=0, tiled=True),
    )
    gate_block = lax.all_to_all(gate_weight, "fsdp", 1, 0, tiled=True)
    up_block = lax.all_to_all(up_weight, "fsdp", 1, 0, tiled=True)
    tokens, gate_block, up_block = lax.optimization_barrier((tokens, gate_block, up_block))
    inputs_wide = tokens.astype(jnp.float32)
    gain_one = attention_set[0].astype(jnp.float32)
    normed_one, normal_one, inverse_one = rms_forward(inputs_wide, gain_one)
    normed_one_low = normed_one.astype(jnp.bfloat16)
    query_raw = jnp.dot(
        normed_one_low, attention_set[1], preferred_element_type=jnp.float32
    ).reshape(row_count, query_heads, head_width)
    key_raw = jnp.dot(normed_one_low, attention_set[2], preferred_element_type=jnp.float32).reshape(
        row_count, value_heads, head_width
    )
    value_low = (
        jnp.dot(normed_one_low, attention_set[3], preferred_element_type=jnp.float32)
        .astype(jnp.bfloat16)
        .reshape(row_count, value_heads, head_width)
    )
    query_normed, query_normal, query_inverse = rms_forward(query_raw, gain_query)
    key_normed, key_normal, key_inverse = rms_forward(key_raw, gain_key)
    query_low = (
        (rotate(query_normed, cosine, sine) * scale)
        .astype(jnp.bfloat16)
        .reshape(row_count, value_heads, group_size, head_width)
    )
    key_low = rotate(key_normed, cosine, sine).astype(jnp.bfloat16)
    scores = masked_scores(query_low, key_low)
    row_top = jnp.max(scores, axis=-1, keepdims=True)
    exp_scores = jnp.exp(scores - row_top)
    row_total = jnp.sum(exp_scores, axis=-1, keepdims=True)
    probs_low = (exp_scores / row_total).astype(jnp.bfloat16)
    log_total = row_top + jnp.log(row_total)
    mixed = jnp.einsum("kgqs,skd->qkgd", probs_low, value_low, preferred_element_type=jnp.float32)
    mixed_low = mixed.reshape(row_count, query_heads * head_width).astype(jnp.bfloat16)
    branch = jnp.dot(mixed_low, attention_set[4], preferred_element_type=jnp.float32)
    middle = inputs_wide + branch
    gain_two = gains[1].astype(jnp.float32)
    normed_two, normal_two, inverse_two = rms_forward(middle, gain_two)
    normed_two_low = normed_two.astype(jnp.bfloat16)
    normed_two_group = lax.all_gather(normed_two_low, "fsdp", axis=0, tiled=True)
    gate_value = jnp.dot(normed_two_group, gate_block, preferred_element_type=jnp.float32)
    up_value = jnp.dot(normed_two_group, up_block, preferred_element_type=jnp.float32)
    hidden_low = (jax.nn.silu(gate_value) * up_value).astype(jnp.bfloat16)
    down_part = jnp.dot(hidden_low, down_weight, preferred_element_type=jnp.float32)
    gate_value, up_value, hidden_low, down_part = lax.optimization_barrier(
        (gate_value, up_value, hidden_low, down_part)
    )
    down_value = lax.psum_scatter(
        down_part.astype(jnp.bfloat16), "fsdp", scatter_dimension=0, tiled=True
    ).astype(jnp.float32)
    grad_top = cotangent.astype(jnp.float32) * valid_rows
    grad_down_low = grad_top.astype(jnp.bfloat16)
    grad_down_group = lax.all_gather(grad_down_low, "fsdp", axis=0, tiled=True)
    down_grad = inner_rows(hidden_low, grad_down_group)
    grad_hidden = times_transposed(grad_down_group, down_weight)
    sigmoid_gate = jax.nn.sigmoid(gate_value)
    grad_gate_low = (
        grad_hidden * up_value * sigmoid_gate * (1.0 + gate_value * (1.0 - sigmoid_gate))
    ).astype(jnp.bfloat16)
    grad_up_low = (grad_hidden * (gate_value * sigmoid_gate)).astype(jnp.bfloat16)
    grad_normed_part = times_transposed(grad_gate_low, gate_block) + times_transposed(
        grad_up_low, up_block
    )
    grad_normed_two = lax.psum_scatter(
        grad_normed_part.astype(jnp.bfloat16), "fsdp", scatter_dimension=0, tiled=True
    ).astype(jnp.float32)
    gate_grad_block = inner_rows(normed_two_group, grad_gate_low)
    up_grad_block = inner_rows(normed_two_group, grad_up_low)
    grad_from_two, gain_two_terms = rms_backward(grad_normed_two, normal_two, inverse_two, gain_two)
    feed_gain_grad = jnp.sum(gain_two_terms, axis=0)
    grad_middle = grad_top + grad_from_two
    feed_parts = (
        None,
        lax.all_to_all(gate_grad_block.astype(jnp.bfloat16), "fsdp", 0, 1, tiled=True),
        lax.all_to_all(up_grad_block.astype(jnp.bfloat16), "fsdp", 0, 1, tiled=True),
        down_grad.astype(jnp.bfloat16),
    )
    feed_width = feed_parts[1].shape[1]
    feed_rows = [feed_parts[1].shape[0], feed_parts[2].shape[0]]
    feed_stack = jnp.concatenate(
        [feed_parts[1], feed_parts[2], feed_parts[3].reshape(-1, feed_width)], axis=0
    )
    ring = RepRing(feed_stack, "rep")
    ring.issue()
    grad_branch_low = grad_middle.astype(jnp.bfloat16)
    output_grad = inner_rows(mixed_low, grad_branch_low)
    grad_mixed_low = (
        times_transposed(grad_branch_low, attention_set[4])
        .astype(jnp.bfloat16)
        .reshape(row_count, value_heads, group_size, head_width)
    )
    grad_mixed_low = ring.land(grad_mixed_low)
    ring.issue()
    scores_again = masked_scores(query_low, key_low)
    probs_again = jnp.exp(scores_again - log_total)
    probs_again_low = probs_again.astype(jnp.bfloat16)
    grad_probs = jnp.einsum(
        "qkgd,skd->kgqs", grad_mixed_low, value_low, preferred_element_type=jnp.float32
    )
    row_term = jnp.sum(probs_again * grad_probs, axis=-1, keepdims=True)
    grad_scores_low = (probs_again * (grad_probs - row_term)).astype(jnp.bfloat16)
    grad_scores_low, probs_again_low = ring.land((grad_scores_low, probs_again_low))
    ring.issue()
    grad_query_rot = (
        jnp.einsum(
            "kgqs,skd->qkgd", grad_scores_low, key_low, preferred_element_type=jnp.float32
        ).reshape(row_count, query_heads, head_width)
        * scale
    )
    grad_key_rot = jnp.einsum(
        "kgqs,qkgd->skd", grad_scores_low, query_low, preferred_element_type=jnp.float32
    )
    grad_value_low = (
        jnp.einsum(
            "kgqs,qkgd->skd", probs_again_low, grad_mixed_low, preferred_element_type=jnp.float32
        )
        .astype(jnp.bfloat16)
        .reshape(row_count, value_heads * head_width)
    )
    value_grad = inner_rows(normed_one_low, grad_value_low)
    grad_query_rot, grad_key_rot, grad_value_low = ring.land(
        (grad_query_rot, grad_key_rot, grad_value_low)
    )
    ring.issue()
    grad_query_raw, query_gain_terms = rms_backward(
        unrotate(grad_query_rot, cosine, sine), query_normal, query_inverse, gain_query
    )
    grad_key_raw, key_gain_terms = rms_backward(
        unrotate(grad_key_rot, cosine, sine), key_normal, key_inverse, gain_key
    )
    query_gain_grad = jnp.sum(query_gain_terms, axis=(0, 1))
    key_gain_grad = jnp.sum(key_gain_terms, axis=(0, 1))
    grad_query_low = grad_query_raw.astype(jnp.bfloat16).reshape(
        row_count, query_heads * head_width
    )
    grad_key_low = grad_key_raw.astype(jnp.bfloat16).reshape(row_count, value_heads * head_width)
    query_grad = inner_rows(normed_one_low, grad_query_low)
    key_grad = inner_rows(normed_one_low, grad_key_low)
    grad_query_low, grad_key_low = ring.land((grad_query_low, grad_key_low))
    ring.issue()
    grad_normed_one = times_transposed(grad_query_low, attention_set[1])
    grad_normed_one, down_value = ring.land((grad_normed_one, down_value))
    ring.issue()
    layer_out = ((middle + down_value) * valid_rows).astype(jnp.bfloat16)
    grad_normed_one = (
        grad_normed_one
        + times_transposed(grad_key_low, attention_set[2])
        + times_transposed(grad_value_low, attention_set[3])
    )
    grad_from_one, gain_one_terms = rms_backward(grad_normed_one, normal_one, inverse_one, gain_one)
    attention_gain_grad = jnp.sum(gain_one_terms, axis=0)
    input_grad = grad_middle + grad_from_one
    input_grad = ring.land(input_grad)
    feed_sum = ring.result()
    feed_rep = (
        feed_sum[: feed_rows[0]],
        feed_sum[feed_rows[0] : feed_rows[0] + feed_rows[1]],
        feed_sum[feed_rows[0] + feed_rows[1] :].reshape(feed_parts[3].shape),
    )
    model_width = attention_gain_grad.shape[0]
    fsdp_count = lax.axis_size("fsdp")
    gain_share = model_width // fsdp_count
    head_terms = jnp.concatenate([query_gain_grad, key_gain_grad])
    head_cols = -(-head_terms.shape[0] // gain_share)
    head_block = jnp.pad(head_terms, (0, head_cols * gain_share - head_terms.shape[0]))
    head_block = head_block.reshape(head_cols, gain_share).T
    gain_cols = jnp.concatenate(
        [
            attention_gain_grad[:, None],
            feed_gain_grad[:, None],
            jnp.tile(head_block, (fsdp_count, 1)),
        ],
        axis=1,
    )
    gain_parts = lax.all_to_all(gain_cols, "fsdp", 0, 1, tiled=True)
    gain_part = gain_parts.reshape(gain_share, fsdp_count, gain_cols.shape[1]).sum(axis=1)
    rep_count = lax.axis_size("rep")
    rep_share = gain_share // rep_count
    rep_parts = lax.all_to_all(gain_part, "rep", 0, 1, tiled=True)
    rep_block = rep_parts.reshape(rep_share, rep_count, gain_part.shape[1]).sum(axis=1)
    gain_rep = lax.all_to_all(jnp.tile(rep_block, (rep_count, 1)), "rep", 0, 0, tiled=True)
    attention_gain_out = gain_rep[:, 0]
    feed_gain_out = gain_rep[:, 1]
    head_sum = gain_rep[:, 2:].T.reshape(-1)
    query_gain_out = head_sum[:head_width]
    key_gain_out = head_sum[head_width : 2 * head_width]

    def low_sum(v):
        return lax.psum_scatter(v.astype(jnp.bfloat16), "fsdp", scatter_dimension=0, tiled=True)

    attention_parts = (
        None, low_sum(query_grad), low_sum(key_grad), low_sum(value_grad), low_sum(output_grad)
    )
    finals = (
        feed_gain_out,
        feed_rep[0],
        feed_rep[1],
        feed_rep[2],
        attention_gain_out,
        lax.psum(attention_parts[1].astype(jnp.bfloat16), "rep").astype(jnp.float32),
        lax.psum(attention_parts[2].astype(jnp.bfloat16), "rep").astype(jnp.float32),
        lax.psum(attention_parts[3].astype(jnp.bfloat16), "rep").astype(jnp.float32),
        lax.psum(attention_parts[4].astype(jnp.bfloat16), "rep").astype(jnp.float32),
    )
    return (
        layer_out,
        input_grad,
        finals[4],
        finals[5],
        finals[6],
        finals[7],
        query_gain_out,
        key_gain_out,
        finals[8],
        finals[0],
        finals[1],
        finals[2],
        finals[3],
    )


def solution(mesh):
    return jax.shard_map(
        per_device,
        mesh=mesh,
        in_specs=(
            P(("fsdp", "rep"), None),
            P(),
            P(),
            P("fsdp"),
            P("fsdp", None),
            P("fsdp", None),
            P("fsdp", None),
            P(),
            P(),
            P("fsdp", None),
            P("fsdp"),
            P("fsdp", None),
            P("fsdp", None),
            P("fsdp", None),
            P(("fsdp", "rep"), None),
        ),
        out_specs=(
            P(("fsdp", "rep"), None),
            P(("fsdp", "rep"), None),
            P("fsdp"),
            P("fsdp", None),
            P("fsdp", None),
            P("fsdp", None),
            P(),
            P(),
            P("fsdp", None),
            P("fsdp"),
            P("fsdp", None),
            P("fsdp", None),
            P("fsdp", None),
        ),
        check_vma=False,
    )
```
